32 devices in a mesh: groups: 2 (over y), lat: 4 (over z), slc: 2 (over x), rep: 2 (over core).
Axes of the slice: x: 2, y: 2, z: 4, core: 2. Of those that a mesh axis runs over, the one named last changes fastest.
Arguments:
- atom_xy: float32 [8, 2, 2, 256], P(('groups', 'lat'), 'slc'), parts along dimension 0, may hold values from 0 to 4096, as said below
- atom_species: int32 [8, 2, 256], P(('groups', 'lat'), 'slc'), parts along dimension 0, may hold values from 0 to 7
- atom_slab: int32 [8, 2, 256], P(('groups', 'lat'), 'slc'), parts along dimension 0, may hold values from 0 to 1
- species_amp: float32 [8], replicated, may hold values from 0.5 to 3
- species_spread: float32 [8], replicated, may hold values from 2 to 6
- margin: int32 [8, 2, 2, 2, 3, 128], P(('groups', 'lat'), 'slc', None, 'rep'), parts along dimension 0, may hold values from -1 to 255, as said below
- probe_pos: int32 [64, 2], P(('groups', 'lat', 'slc', 'rep')), parts along dimension 0, may hold values from 0 to 4092, as said below
Outputs:
- exit_wave: bfloat16 [64, 256, 2, 256], P(('groups', 'lat', 'slc', 'rep')), parts along dimension 0
The draws below stay inside these ranges and needn't reach their ends.
There are 2 independent parts, one for each index of `groups`. The reference program is written for one: setup_inputs(seed, part) draws one part's arguments, and reference() takes and returns one part's arrays. A program takes and returns all parts, laid end to end along the dimension named above; an argument that names none is the same for every part. Nothing has to cross between parts.
Inputs may be any that keep to these rules, and one draw needn't show every extreme that they name: `atom_xy`: atom a of tile v has x between (v * 256 + a) b and (v * 256 + a + 1) b with b = 4, and y in [0, 256). `probe_pos`: the 2 probes of one lateral index, slice owner and rep index share their x anchor; the centre of each window lies in tile t, x is a multiple of 4 taken modulo 4096, and y is below 256. `margin`: each block lists a run of consecutive local atom indices in rising order, then -1: the atoms of tile v whose x lies within 128 pixels of the probes' windows (x modulo 4096).
All inputs are finite; a program needn't handle non-finite values.
Results may differ from the reference program's by a relative error of at most 0.03.
Values may be sent and summed in bfloat16 or wider, within the bound.
No kernel may reach another device: no remote copies, remote signals or barrier semaphores. Data moves between devices by JAX's collectives and lax.ppermute only.
A program may use at most 128 MiB of HBM per device.

```python
import math
import jax
import jax.numpy as jnp
from jax import lax

W = 256
SL_DEV = 2
PB_DEV = 2
ATOM_DEV = 256
CAP = 128
NSPEC = 8
PROBES = 32
N_LAT = 4
N_SLC = 2
N_REP = 2


def batch_centres(key):
    base_key = jax.random.fold_in(key, 29)
    key_low, key_high, key_any, key_first, key_second = jax.random.split(base_key, 5)
    block_shape = (N_LAT, N_SLC, N_REP)
    low_band = jax.random.randint(key_low, block_shape, 0, CAP // 4)
    lateral_zero = jnp.arange(N_LAT, dtype=jnp.int32)[:, None, None] == 0
    rep_zero = jnp.arange(N_REP, dtype=jnp.int32)[None, None, :] == 0
    low_band = jnp.where(lateral_zero & rep_zero, CAP // 4 - 1, low_band)
    high_band = jax.random.randint(key_high, block_shape, ATOM_DEV - CAP // 4 + 1, ATOM_DEV)
    any_band = jax.random.randint(key_any, block_shape, 0, ATOM_DEV)
    first_slot = jax.random.randint(key_first, (N_LAT, 1, N_REP), 0, N_SLC)
    second_slot = (first_slot + jax.random.randint(key_second, (N_LAT, 1, N_REP), 1, N_SLC)) % N_SLC
    slot_index = jnp.arange(N_SLC, dtype=jnp.int32)[None, :, None]
    picked = jnp.where(slot_index == first_slot, low_band, jnp.where(slot_index == second_slot, high_band, any_band))
    return picked.astype(jnp.int32)


def draw_atom_xy(key, part):
    base_key = jax.random.fold_in(key, 5)
    key_jitter, key_along = jax.random.split(base_key, 2)
    cell_size = 2.0 * W / CAP
    tile_index = jnp.arange(N_LAT, dtype=jnp.float32)[:, None, None]
    atom_index = jnp.arange(ATOM_DEV, dtype=jnp.float32)[None, None, :]
    jitter = jax.random.uniform(key_jitter, (N_LAT, N_SLC, ATOM_DEV), jnp.float32, 0.1, 0.9)
    across_x = (tile_index * ATOM_DEV + atom_index + jitter) * cell_size
    along_y = jax.random.uniform(key_along, (N_LAT, N_SLC, ATOM_DEV), jnp.float32, 0.0, 1.0) * W
    return jnp.stack([across_x, along_y], 2).astype(jnp.float32)


def draw_probe_pos(key, part):
    centres = batch_centres(key)
    cell_size = 2 * W // CAP
    tile_width = ATOM_DEV * cell_size
    field_width = N_LAT * tile_width
    tile_index = jnp.arange(N_LAT, dtype=jnp.int32)[:, None, None]
    anchor_x = (tile_index * tile_width + centres * cell_size - W // 2) % field_width
    anchor_x = jnp.broadcast_to(anchor_x[..., None], (N_LAT, N_SLC, N_REP, PB_DEV)).reshape(-1)
    anchor_y = jax.random.randint(jax.random.fold_in(key, 31), (PROBES,), 0, W)
    return jnp.stack([anchor_x, anchor_y], 1).astype(jnp.int32)


def draw_margin(key, part):
    centres = batch_centres(key)
    tile_index = jnp.arange(N_LAT, dtype=jnp.int32)[:, None]
    offsets = jnp.arange(3, dtype=jnp.int32)[None, :]
    target = (tile_index + offsets - 1) % N_LAT
    seen = jnp.transpose(centres[target], (0, 2, 3, 1))
    relative = seen - CAP // 2 + (jnp.arange(3, dtype=jnp.int32)[None, None, None, :] - 1) * ATOM_DEV
    run_start = jnp.maximum(relative, 0)
    run_end = jnp.minimum(relative + CAP, ATOM_DEV)
    run_length = jnp.maximum(run_end - run_start, 0)
    entries = jnp.arange(CAP, dtype=jnp.int32)
    listed = jnp.where(entries < run_length[..., None], run_start[..., None] + entries, -1)
    listed = jnp.broadcast_to(listed[:, None], (N_LAT, N_SLC, N_SLC, N_REP, 3, CAP))
    return listed.astype(jnp.int32)


def with_ends(drawn, rng, low, high):
    longest = drawn.shape.index(max(drawn.shape))
    spots = []
    for shift in (0, 1):
        where = [jax.random.randint(jax.random.fold_in(rng, axis), (), 0, length) for axis, length in enumerate(drawn.shape)]
        where[longest] = (where[longest] + shift) % drawn.shape[longest]
        spots.append(tuple(where))
    return drawn.at[spots[0]].set(low).at[spots[1]].set(high)


def setup_inputs(seed: int = 0, part: int = 0) -> dict:
    streams_of = jax.random.split(jax.random.key(seed), 8)
    part_keys = jax.random.split(jax.random.fold_in(streams_of[7], part), 8)
    return {
        "atom_xy": draw_atom_xy(jax.random.fold_in(jax.random.fold_in(streams_of[7], part), 71), part),
        "atom_species": with_ends(jax.random.randint(part_keys[1], (N_LAT, N_SLC, ATOM_DEV), 0, NSPEC), jax.random.fold_in(part_keys[1], 1), 0, NSPEC - 1).astype(jnp.int32),
        "atom_slab": with_ends(jax.random.randint(part_keys[2], (N_LAT, N_SLC, ATOM_DEV), 0, SL_DEV), jax.random.fold_in(part_keys[2], 1), 0, SL_DEV - 1).astype(jnp.int32),
        "species_amp": jnp.clip(jnp.exp(jax.random.uniform(streams_of[3], (NSPEC,), jnp.float32, math.log(0.5), math.log(3.0))), 0.5, 3.0),
        "species_spread": jnp.clip(jnp.exp(jax.random.uniform(streams_of[4], (NSPEC,), jnp.float32, math.log(2.0), math.log(6.0))), 2.0, 6.0),
        "margin": draw_margin(jax.random.fold_in(jax.random.fold_in(streams_of[7], part), 71), part),
        "probe_pos": draw_probe_pos(jax.random.fold_in(jax.random.fold_in(streams_of[7], part), 71), part),
    }


PROPAGATION_COEF = 0.001
DEFOCUS_COEF = 4.19

def centered_frequency(window):
    indices = jnp.arange(window, dtype=jnp.int32)
    return jnp.where(indices < window // 2, indices, indices - window).astype(jnp.float32)

def transform_matrices(window, direction):
    indices = jnp.arange(window, dtype=jnp.int32)
    product = indices[:, None] * indices[None, :] % window
    angle_table = 2.0 * math.pi / window * product.astype(jnp.float32)
    real_part = (jnp.cos(angle_table) / math.sqrt(window)).astype(jnp.bfloat16)
    imag_part = (direction * jnp.sin(angle_table) / math.sqrt(window)).astype(jnp.bfloat16)
    right_matrix = jnp.stack([jnp.stack([real_part, imag_part], 0), jnp.stack([-imag_part, real_part], 0)], 0)
    right_matrix = jnp.transpose(right_matrix, (0, 2, 1, 3)).reshape(2 * window, 2 * window)
    left_matrix = jnp.stack([jnp.stack([real_part, -imag_part], -1), jnp.stack([imag_part, real_part], -1)], 1)
    left_matrix = left_matrix.reshape(2 * window, 2 * window)
    return (left_matrix, right_matrix)

def propagator(window):
    frequency = centered_frequency(window)
    radius = frequency[:, None] * frequency[:, None] + frequency[None, :] * frequency[None, :]
    inside = (9.0 * radius < window * window).astype(jnp.float32)
    phase_angle = -PROPAGATION_COEF * (65536.0 / (window * window)) * radius
    return (inside * jnp.cos(phase_angle), inside * jnp.sin(phase_angle))

def left_apply(left_matrix, probe_wave):
    window = probe_wave.shape[0]
    return jnp.dot(left_matrix, probe_wave.reshape(2 * window, window), preferred_element_type=jnp.float32).reshape(window, 2, window)

def right_apply(right_matrix, probe_wave):
    window = probe_wave.shape[0]
    return jnp.dot(probe_wave.reshape(window, 2 * window), right_matrix, preferred_element_type=jnp.float32).reshape(window, 2, window)

def incident(window, inverse_left, inverse_right):
    frequency = centered_frequency(window)
    radius = frequency[:, None] * frequency[:, None] + frequency[None, :] * frequency[None, :]
    inside = (16.0 * radius < window * window).astype(jnp.float32)
    norm_scale = window / jnp.sqrt(jnp.sum(inside))
    phase_angle = -(DEFOCUS_COEF / window) * radius
    spectrum = jnp.stack([inside * norm_scale * jnp.cos(phase_angle), inside * norm_scale * jnp.sin(phase_angle)], 1).astype(jnp.bfloat16)
    start_rows = left_apply(inverse_left, spectrum).astype(jnp.bfloat16)
    return right_apply(inverse_right, start_rows).astype(jnp.bfloat16)

def one_slice(probe_wave, potential, tables):
    forward_left, forward_right, inverse_left, inverse_right, prop_real, prop_imag = tables
    cos_phase = jnp.cos(potential)
    sin_phase = jnp.sin(potential)
    real_part = probe_wave[:, 0, :].astype(jnp.float32)
    imag_part = probe_wave[:, 1, :].astype(jnp.float32)
    transmitted = jnp.stack([real_part * cos_phase - imag_part * sin_phase, real_part * sin_phase + imag_part * cos_phase], 1).astype(jnp.bfloat16)
    rowwise = right_apply(forward_right, transmitted).astype(jnp.bfloat16)
    spectrum = left_apply(forward_left, rowwise)
    spec_real = spectrum[:, 0, :]
    spec_imag = spectrum[:, 1, :]
    spectrum = jnp.stack([spec_real * prop_real - spec_imag * prop_imag, spec_real * prop_imag + spec_imag * prop_real], 1).astype(jnp.bfloat16)
    back_rows = left_apply(inverse_left, spectrum).astype(jnp.bfloat16)
    return right_apply(inverse_right, back_rows).astype(jnp.bfloat16)

def atom_fields(positions, species, slab, species_amp, species_spread, layers):
    species_match = (species[None, :] == jnp.arange(species_amp.shape[0], dtype=jnp.int32)[:, None]).astype(species_amp.dtype)
    amplitude = lax.optimization_barrier(jnp.sum(species_match * species_amp[:, None], 0))
    spread = lax.optimization_barrier(jnp.sum(species_match * species_spread[:, None], 0))
    inverse = 0.5 / (spread * spread)
    slab_match = (slab[None, :] == jnp.arange(layers, dtype=jnp.int32)[:, None]).astype(amplitude.dtype)
    return jnp.concatenate([positions, inverse[None, :], slab_match * amplitude[None, :]], 0)

def pick_rows(fields, pick_list):
    valid_mask = (pick_list >= 0).astype(fields.dtype)
    safe_index = jnp.maximum(pick_list, 0)
    gathered = fields[:, safe_index]
    return jnp.concatenate([gathered[:3], gathered[3:] * valid_mask[None]], 0)

def slab_potential(row_block, anchor, window, layers, field_x):
    pixels = jnp.arange(window, dtype=jnp.float32)
    half_width = 0.5 * window
    half_field = 0.5 * field_x
    inverse = row_block[2][:, None]
    dist_x = jnp.mod(row_block[0][:, None] - anchor[0].astype(jnp.float32) - pixels[None, :] + half_field, field_x) - half_field
    across = jnp.exp(-dist_x * dist_x * inverse).astype(jnp.bfloat16)
    dist_y = jnp.mod(row_block[1][:, None] - anchor[1].astype(jnp.float32) - pixels[None, :] + half_width, window) - half_width
    along = jnp.exp(-dist_y * dist_y * inverse)
    weighted = (row_block[3:3 + layers][:, :, None] * along[None]).astype(jnp.bfloat16)
    weighted = jnp.transpose(weighted, (1, 0, 2)).reshape(row_block.shape[1], layers * window)
    return jnp.dot(across.T, weighted, preferred_element_type=jnp.float32).reshape(window, layers, window)

def reference(atom_xy, atom_species, atom_slab, species_amp, species_spread, margin, probe_pos):
    layers = SL_DEV
    field_x = N_LAT * ATOM_DEV * (2 * W // CAP)
    forward_left, forward_right = transform_matrices(W, -1.0)
    inverse_left, inverse_right = transform_matrices(W, 1.0)
    prop_real, prop_imag = propagator(W)
    tables = (forward_left, forward_right, inverse_left, inverse_right, prop_real, prop_imag)
    start_wave = incident(W, inverse_left, inverse_right)

    def device_fields(positions, species, slab):
        return atom_fields(positions, species, slab, species_amp, species_spread, layers)
    field_table = jax.vmap(jax.vmap(device_fields))(atom_xy, atom_species, atom_slab)

    def run_probe(probe_index):
        lateral = probe_index // (PB_DEV * N_REP * N_SLC)
        entry_slot = probe_index // (PB_DEV * N_REP) % N_SLC
        replica = probe_index // PB_DEV % N_REP
        anchor = probe_pos[probe_index]
        probe_wave = start_wave
        for hop_index in range(N_SLC):
            owner_slot = (entry_slot + hop_index) % N_SLC
            blocks = []
            for offset in (2, 1, 0):
                source = (lateral - offset + 1) % N_LAT
                owner_fields = field_table[source, owner_slot]
                pick_list = margin[source, owner_slot, entry_slot, replica, offset]
                blocks.append(pick_rows(owner_fields, pick_list))
            row_block = jnp.concatenate(blocks, 1)
            potential = slab_potential(row_block, anchor, W, layers, field_x)
            for layer_index in range(layers):
                probe_wave = one_slice(probe_wave, potential[:, layer_index, :], tables)
        return probe_wave
    return lax.map(run_probe, jnp.arange(PROBES, dtype=jnp.int32))
```

```python
import functools
import math

import jax
import jax.numpy as jnp
from jax import lax
from jax.experimental import pallas as pl
from jax.experimental.pallas import tpu as pltpu
from jax.sharding import PartitionSpec as P

W = 256
SL_DEV = 2


PROPAGATION_COEF = 0.001
DEFOCUS_COEF = 4.19


def centered_frequency(window):
    indices = jnp.arange(window, dtype=jnp.int32)
    return jnp.where(indices < window // 2, indices, indices - window).astype(jnp.float32)


def dft_parts(window, direction):
    indices = jnp.arange(window, dtype=jnp.int32)
    product = indices[:, None] * indices[None, :] % window
    angle_table = 2.0 * math.pi / window * product.astype(jnp.float32)
    real_part = (jnp.cos(angle_table) / math.sqrt(window)).astype(jnp.bfloat16)
    imag_part = (direction * jnp.sin(angle_table) / math.sqrt(window)).astype(jnp.bfloat16)
    return real_part, imag_part


def block_tables(window):
    f_re, f_im = dft_parts(window, -1.0)
    i_re, i_im = dft_parts(window, 1.0)

    def right(re, im):
        return jnp.concatenate(
            [jnp.concatenate([re, im], 1), jnp.concatenate([-im, re], 1)], 0
        )

    def left(re, im):
        return jnp.concatenate(
            [jnp.concatenate([re, -im], 1), jnp.concatenate([im, re], 1)], 0
        )

    return left(f_re, f_im), right(f_re, f_im), left(i_re, i_im), right(i_re, i_im)


def propagator(window):
    frequency = centered_frequency(window)
    radius = frequency[:, None] * frequency[:, None] + frequency[None, :] * frequency[None, :]
    inside = (9.0 * radius < window * window).astype(jnp.float32)
    phase_angle = -PROPAGATION_COEF * (65536.0 / (window * window)) * radius
    return jnp.stack([inside * jnp.cos(phase_angle), inside * jnp.sin(phase_angle)], 0)


def start_spectrum(window):
    frequency = centered_frequency(window)
    radius = frequency[:, None] * frequency[:, None] + frequency[None, :] * frequency[None, :]
    inside = (16.0 * radius < window * window).astype(jnp.float32)
    norm_scale = window / jnp.sqrt(jnp.sum(inside))
    phase_angle = -(DEFOCUS_COEF / window) * radius
    spectrum = jnp.concatenate(
        [inside * norm_scale * jnp.cos(phase_angle), inside * norm_scale * jnp.sin(phase_angle)], 0
    )
    return spectrum.astype(jnp.bfloat16)


def atom_fields(positions, species, slab, species_amp, species_spread, layers):
    species_match = (
        species[None, :] == jnp.arange(species_amp.shape[0], dtype=jnp.int32)[:, None]
    ).astype(species_amp.dtype)
    amplitude = jnp.sum(species_match * species_amp[:, None], 0)
    spread = jnp.sum(species_match * species_spread[:, None], 0)
    inverse = 0.5 / (spread * spread)
    slab_match = (slab[None, :] == jnp.arange(layers, dtype=jnp.int32)[:, None]).astype(
        amplitude.dtype
    )
    return jnp.concatenate([positions, inverse[None, :], slab_match * amplitude[None, :]], 0)


def pick_rows(fields, pick_list):
    valid_mask = (pick_list >= 0).astype(fields.dtype)
    safe_index = jnp.maximum(pick_list, 0)
    gathered = fields[:, safe_index]
    return jnp.concatenate([gathered[:3], gathered[3:] * valid_mask[None]], 0)


def slab_potentials(row_block, anchors, window, layers, field_x):
    pixels = jnp.arange(window, dtype=jnp.float32)
    half_width = 0.5 * window
    half_field = 0.5 * field_x
    inverse = row_block[None, :, 2, :, None]
    shift_x = anchors[:, 0].astype(jnp.float32)[:, None, None, None]
    shift_y = anchors[:, 1].astype(jnp.float32)[:, None, None, None]
    dist_x = (
        jnp.mod(row_block[None, :, 0, :, None] - shift_x - pixels + half_field, field_x)
        - half_field
    )
    across = jnp.exp(-dist_x * dist_x * inverse).astype(jnp.bfloat16)
    dist_y = (
        jnp.mod(row_block[None, :, 1, :, None] - shift_y - pixels + half_width, window)
        - half_width
    )
    along = jnp.exp(-dist_y * dist_y * inverse)
    amplitudes = row_block[:, 3 : 3 + layers]
    weighted = (amplitudes[None, :, :, :, None] * along[:, :, None, :, :]).astype(jnp.bfloat16)
    return jnp.einsum("phax,phlay->phlxy", across, weighted, preferred_element_type=jnp.float32)


def slices_kernel(pot_ref, fl_ref, fr_ref, il_ref, ir_ref, prop_ref, spec_ref, out_ref, wave_ref):
    w = pot_ref.shape[-1]
    step = pl.program_id(1)
    f32, bf16 = jnp.float32, jnp.bfloat16

    def dot(a, b):
        return jnp.dot(a, b, preferred_element_type=f32)

    @pl.when(step == 0)
    def _():
        rows = dot(il_ref[...], spec_ref[...]).astype(bf16)
        rows = jnp.concatenate([rows[:w], rows[w:]], 1)
        wave_ref[...] = dot(rows, ir_ref[...]).astype(bf16)

    psi = wave_ref[...]
    wr = psi[:, :w].astype(f32)
    wi = psi[:, w:].astype(f32)
    v = pot_ref[0, 0]
    cv = jnp.cos(v)
    sv = jnp.sin(v)
    tr = (wr * cv - wi * sv).astype(bf16)
    ti = (wr * sv + wi * cv).astype(bf16)
    rw = dot(jnp.concatenate([tr, ti], 1), fr_ref[...]).astype(bf16)
    sp = dot(fl_ref[...], jnp.concatenate([rw[:, :w], rw[:, w:]], 0))
    sr = sp[:w]
    si = sp[w:]
    pr = prop_ref[0]
    pi = prop_ref[1]
    spb = jnp.concatenate(
        [(sr * pr - si * pi).astype(bf16), (sr * pi + si * pr).astype(bf16)], 0
    )
    br = dot(il_ref[...], spb).astype(bf16)
    psi = dot(jnp.concatenate([br[:w], br[w:]], 1), ir_ref[...]).astype(bf16)
    wave_ref[...] = psi

    @pl.when(step == pl.num_programs(1) - 1)
    def _():
        out_ref[0] = psi


def run_slices(pot, tables, prop, spec):
    batch, steps, w, _ = pot.shape
    fl, fr, il, ir = tables
    full = lambda shape: pl.BlockSpec(shape, lambda p, s: (0,) * len(shape))
    flops = batch * steps * 4 * 2 * w * (2 * w) * (2 * w)
    return pl.pallas_call(
        slices_kernel,
        out_shape=jax.ShapeDtypeStruct((batch, w, 2 * w), jnp.bfloat16),
        grid=(batch, steps),
        in_specs=[
            pl.BlockSpec((1, 1, w, w), lambda p, s: (p, s, 0, 0)),
            full((2 * w, 2 * w)),
            full((2 * w, 2 * w)),
            full((2 * w, 2 * w)),
            full((2 * w, 2 * w)),
            full((2, w, w)),
            full((2 * w, w)),
        ],
        out_specs=pl.BlockSpec((1, w, 2 * w), lambda p, s: (p, 0, 0)),
        scratch_shapes=[pltpu.VMEM((w, 2 * w), jnp.bfloat16)],
        compiler_params=pltpu.CompilerParams(
            dimension_semantics=("arbitrary", "arbitrary"),
        ),
        cost_estimate=pl.CostEstimate(
            flops=flops,
            transcendentals=batch * steps * 2 * w * w,
            bytes_accessed=batch * steps * w * w * 4 + 4 * (2 * w) ** 2 * 2 + batch * w * w * 4,
        ),
    )(pot, fl, fr, il, ir, prop, spec)


def shards(atom_xy, atom_species, atom_slab, species_amp, species_spread, margin, probe_pos):
    layers = SL_DEV
    window = W
    atoms = atom_xy.shape[-1]
    cap = margin.shape[-1]
    n_lat = lax.axis_size("lat")
    owners = lax.axis_size("slc")
    field_x = n_lat * atoms * (2 * window // cap)
    fields = atom_fields(
        atom_xy[0, 0], atom_species[0, 0], atom_slab[0, 0], species_amp, species_spread, layers
    )
    field_count = fields.shape[0]
    pick_table = margin[0, 0, :, 0]
    picked = jax.vmap(jax.vmap(lambda lst: pick_rows(fields, lst)))(pick_table)
    to_left = lax.ppermute(
        picked[:, 0], "lat", [((i + 1) % n_lat, i) for i in range(n_lat)]
    )
    to_right = lax.ppermute(
        picked[:, 2], "lat", [(i, (i + 1) % n_lat) for i in range(n_lat)]
    )
    local = jnp.stack([to_right, picked[:, 1], to_left], 1)
    gathered = lax.all_gather(local, "slc", axis=0, tiled=False)
    me = lax.axis_index("slc")
    mine = lax.dynamic_index_in_dim(gathered, me, 1, keepdims=False)
    hop_owner = (me + jnp.arange(owners)) % owners
    rows = jnp.take(mine, hop_owner, axis=0)
    rows = jnp.transpose(rows, (0, 2, 1, 3)).reshape(owners, field_count, 3 * cap)
    pot = slab_potentials(rows, probe_pos, window, layers, field_x)
    batch = probe_pos.shape[0]
    pot = pot.reshape(batch, owners * layers, window, window)
    tables = block_tables(window)
    wave = run_slices(pot, tables, propagator(window), start_spectrum(window))
    return wave.reshape(batch, window, 2, window)


def solution(mesh):
    in_specs = (
        P(("groups", "lat"), "slc", None, None),
        P(("groups", "lat"), "slc", None),
        P(("groups", "lat"), "slc", None),
        P(),
        P(),
        P(("groups", "lat"), "slc", None, "rep", None, None),
        P(("groups", "lat", "slc", "rep"), None),
    )
    out_specs = P(("groups", "lat", "slc", "rep"), None, None, None)
    return jax.shard_map(shards, mesh=mesh, in_specs=in_specs, out_specs=out_specs, check_vma=False)
```

```python
import functools
import math

import jax
import numpy as np
import jax.numpy as jnp
from jax import lax
from jax.experimental import pallas as pl
from jax.experimental.pallas import tpu as pltpu
from jax.sharding import PartitionSpec as P

W = 256
SL_DEV = 2


PROPAGATION_COEF = 0.001
DEFOCUS_COEF = 4.19


def centered_frequency(window):
    indices = np.arange(window, dtype=np.int32)
    return np.where(indices < window // 2, indices, indices - window).astype(np.float32)


def squared_radius(window):
    frequency = centered_frequency(window)
    return frequency[:, None] * frequency[:, None] + frequency[None, :] * frequency[None, :]


def dft_blocks(window):
    indices = np.arange(window, dtype=np.int32)
    product = indices[:, None] * indices[None, :] % window
    angle = np.float32(2.0 * math.pi / window) * product.astype(np.float32)
    scale = np.float32(math.sqrt(window))
    re = (np.cos(angle) / scale).astype(jnp.bfloat16)
    im = (np.sin(angle) / scale).astype(jnp.bfloat16)
    a = np.block([[re, -im], [im, re]])
    b = np.block([[re, im], [-im, re]])
    return a, b


def propagator(window):
    radius = squared_radius(window)
    inside = (np.float32(9.0) * radius < window * window).astype(np.float32)
    phase_angle = np.float32(-PROPAGATION_COEF * (65536.0 / (window * window))) * radius
    return np.stack([inside * np.cos(phase_angle), inside * np.sin(phase_angle)], 0)


def start_spectrum(window):
    radius = squared_radius(window)
    inside = (np.float32(16.0) * radius < window * window).astype(np.float32)
    norm_scale = np.float32(window) / np.sqrt(np.sum(inside, dtype=np.float32))
    phase_angle = np.float32(-(DEFOCUS_COEF / window)) * radius
    spectrum = np.concatenate(
        [inside * norm_scale * np.cos(phase_angle), inside * norm_scale * np.sin(phase_angle)], 0
    )
    return spectrum.astype(jnp.bfloat16)


def atom_fields(positions, species, slab, species_amp, species_spread, layers):
    species_match = (
        species[None, :] == jnp.arange(species_amp.shape[0], dtype=jnp.int32)[:, None]
    ).astype(species_amp.dtype)
    amplitude = jnp.sum(species_match * species_amp[:, None], 0)
    spread = jnp.sum(species_match * species_spread[:, None], 0)
    inverse = 0.5 / (spread * spread)
    slab_match = (slab[None, :] == jnp.arange(layers, dtype=jnp.int32)[:, None]).astype(
        amplitude.dtype
    )
    return jnp.concatenate([positions, inverse[None, :], slab_match * amplitude[None, :]], 0)


def pick_rows(fields, pick_list):
    valid_mask = (pick_list >= 0).astype(fields.dtype)
    safe_index = jnp.maximum(pick_list, 0)
    gathered = fields[:, safe_index]
    return jnp.concatenate([gathered[:3], gathered[3:] * valid_mask[None]], 0)


def wrap(value, period):
    return value - period * jnp.floor(value * (1.0 / period))


def slices_kernel(
    pos_ref, rows_ref, cols_ref, a_ref, b_ref, prop_ref, spec_ref, out_ref, wave_ref, pot_ref,
    *, field_x
):
    w = prop_ref.shape[-1]
    layers = pot_ref.shape[-1] // w
    p = pl.program_id(0)
    hop = pl.program_id(1)
    layer = pl.program_id(2)
    f32, bf16 = jnp.float32, jnp.bfloat16

    def dot(a, b):
        return jnp.dot(a, b, preferred_element_type=f32)

    @pl.when((hop == 0) & (layer == 0))
    def _():
        rows = dot(a_ref[...], spec_ref[...]).astype(bf16)
        rows = jnp.concatenate([rows[:w], rows[w:]], 1)
        wave_ref[...] = dot(rows, b_ref[...]).astype(bf16)

    @pl.when(layer == 0)
    def _():
        shift_x = pos_ref[p, 0].astype(f32)
        shift_y = pos_ref[p, 1].astype(f32)
        atom_x = rows_ref[0, 0:1, :]
        inverse_row = rows_ref[0, 2:3, :]
        pixel_col = lax.broadcasted_iota(jnp.int32, (w, 1), 0).astype(f32)
        dist_x = wrap(atom_x - shift_x - pixel_col + 0.5 * field_x, field_x) - 0.5 * field_x
        across = jnp.exp(-dist_x * dist_x * inverse_row).astype(bf16)
        atom_y = cols_ref[0, :, 1:2]
        inverse_col = cols_ref[0, :, 2:3]
        pixel_row = lax.broadcasted_iota(jnp.int32, (1, w), 1).astype(f32)
        dist_y = wrap(atom_y - shift_y - pixel_row + 0.5 * w, w) - 0.5 * w
        along = jnp.exp(-dist_y * dist_y * inverse_col)
        weighted = jnp.concatenate(
            [(cols_ref[0, :, 3 + l : 4 + l] * along).astype(bf16) for l in range(layers)], 1
        )
        pot_ref[...] = dot(across, weighted)

    psi = wave_ref[...]
    wr = psi[:, :w].astype(f32)
    wi = psi[:, w:].astype(f32)
    v = pot_ref[:, pl.ds(pl.multiple_of(layer * w, w), w)]
    cv = jnp.cos(v)
    sv = jnp.sin(v)
    tr = (wr * cv - wi * sv).astype(bf16)
    ti = (wr * sv + wi * cv).astype(bf16)
    rw = dot(jnp.concatenate([tr, ti], 1), a_ref[...]).astype(bf16)
    sp = dot(b_ref[...], jnp.concatenate([rw[:, :w], rw[:, w:]], 0))
    sr = sp[:w]
    si = sp[w:]
    pr = prop_ref[0]
    pi = prop_ref[1]
    spb = jnp.concatenate(
        [(sr * pr - si * pi).astype(bf16), (sr * pi + si * pr).astype(bf16)], 0
    )
    br = dot(a_ref[...], spb).astype(bf16)
    psi = dot(jnp.concatenate([br[:w], br[w:]], 1), b_ref[...]).astype(bf16)
    wave_ref[...] = psi

    @pl.when((hop == pl.num_programs(1) - 1) & (layer == pl.num_programs(2) - 1))
    def _():
        out_ref[0] = psi


def run_slices(probe_pos, rows, cols, window, layers, field_x):
    batch = probe_pos.shape[0]
    hops, fields, atoms = rows.shape
    w = window
    a, b = dft_blocks(w)
    prop = propagator(w)
    spec = start_spectrum(w)
    full = lambda shape: pl.BlockSpec(shape, lambda p, h, l, pos: (0,) * len(shape))
    steps = batch * hops * layers
    flops = steps * 4 * 2 * w * (2 * w) * (2 * w) + batch * hops * 2 * w * atoms * layers * w
    return pl.pallas_call(
        functools.partial(slices_kernel, field_x=float(field_x)),
        out_shape=jax.ShapeDtypeStruct((batch, w, 2 * w), jnp.bfloat16),
        grid_spec=pltpu.PrefetchScalarGridSpec(
            num_scalar_prefetch=1,
            grid=(batch, hops, layers),
            in_specs=[
                pl.BlockSpec((1, fields, atoms), lambda p, h, l, pos: (h, 0, 0)),
                pl.BlockSpec((1, atoms, fields), lambda p, h, l, pos: (h, 0, 0)),
                full((2 * w, 2 * w)),
                full((2 * w, 2 * w)),
                full((2, w, w)),
                full((2 * w, w)),
            ],
            out_specs=pl.BlockSpec((1, w, 2 * w), lambda p, h, l, pos: (p, 0, 0)),
            scratch_shapes=[
                pltpu.VMEM((w, 2 * w), jnp.bfloat16),
                pltpu.VMEM((w, layers * w), jnp.float32),
            ],
        ),
        compiler_params=pltpu.CompilerParams(
            dimension_semantics=("arbitrary", "arbitrary", "arbitrary"),
        ),
        cost_estimate=pl.CostEstimate(
            flops=flops,
            transcendentals=steps * 2 * w * w + batch * hops * 2 * atoms * w,
            bytes_accessed=2 * (2 * w) ** 2 * 2 + 3 * w * w * 4 + batch * w * w * 4,
        ),
    )(probe_pos, rows, cols, jnp.asarray(a), jnp.asarray(b), jnp.asarray(prop), jnp.asarray(spec))


def shards(atom_xy, atom_species, atom_slab, species_amp, species_spread, margin, probe_pos):
    layers = SL_DEV
    window = W
    atoms = atom_xy.shape[-1]
    cap = margin.shape[-1]
    n_lat = lax.axis_size("lat")
    owners = lax.axis_size("slc")
    field_x = n_lat * atoms * (2 * window // cap)
    fields = atom_fields(
        atom_xy[0, 0], atom_species[0, 0], atom_slab[0, 0], species_amp, species_spread, layers
    )
    field_count = fields.shape[0]
    pick_table = margin[0, 0, :, 0]
    picked = jax.vmap(jax.vmap(lambda lst: pick_rows(fields, lst)))(pick_table)
    to_left = lax.ppermute(
        picked[:, 0], "lat", [((i + 1) % n_lat, i) for i in range(n_lat)]
    )
    to_right = lax.ppermute(
        picked[:, 2], "lat", [(i, (i + 1) % n_lat) for i in range(n_lat)]
    )
    local = jnp.stack([to_right, picked[:, 1], to_left], 1)
    gathered = lax.all_gather(local, "slc", axis=0, tiled=False)
    me = lax.axis_index("slc")
    mine = lax.dynamic_index_in_dim(gathered, me, 1, keepdims=False)
    hop_owner = (me + jnp.arange(owners)) % owners
    rows = jnp.take(mine, hop_owner, axis=0)
    rows = jnp.transpose(rows, (0, 2, 1, 3)).reshape(owners, field_count, 3 * cap)
    cols = jnp.transpose(rows, (0, 2, 1))
    batch = probe_pos.shape[0]
    wave = run_slices(probe_pos, rows, cols, window, layers, field_x)
    return wave.reshape(batch, window, 2, window)


def solution(mesh):
    in_specs = (
        P(("groups", "lat"), "slc", None, None),
        P(("groups", "lat"), "slc", None),
        P(("groups", "lat"), "slc", None),
        P(),
        P(),
        P(("groups", "lat"), "slc", None, "rep", None, None),
        P(("groups", "lat", "slc", "rep"), None),
    )
    out_specs = P(("groups", "lat", "slc", "rep"), None, None, None)
    return jax.shard_map(shards, mesh=mesh, in_specs=in_specs, out_specs=out_specs, check_vma=False)
```

```python
import functools
import math

import jax
import numpy as np
import jax.numpy as jnp
from jax import lax
from jax.experimental import pallas as pl
from jax.experimental.pallas import tpu as pltpu
from jax.sharding import PartitionSpec as P

W = 256
SL_DEV = 2


PROPAGATION_COEF = 0.001
DEFOCUS_COEF = 4.19


def centered_frequency(window):
    indices = np.arange(window, dtype=np.int32)
    return np.where(indices < window // 2, indices, indices - window).astype(np.float32)


def squared_radius(window):
    frequency = centered_frequency(window)
    return frequency[:, None] * frequency[:, None] + frequency[None, :] * frequency[None, :]


def dft_blocks(window):
    indices = np.arange(window, dtype=np.int32)
    product = indices[:, None] * indices[None, :] % window
    angle = np.float32(2.0 * math.pi / window) * product.astype(np.float32)
    scale = np.float32(math.sqrt(window))
    re = (np.cos(angle) / scale).astype(jnp.bfloat16)
    im = (np.sin(angle) / scale).astype(jnp.bfloat16)
    a = np.block([[re, -im], [im, re]])
    b = np.block([[re, im], [-im, re]])
    return a, b


def propagator(window):
    radius = squared_radius(window)
    inside = (np.float32(9.0) * radius < window * window).astype(np.float32)
    phase_angle = np.float32(-PROPAGATION_COEF * (65536.0 / (window * window))) * radius
    return np.stack([inside * np.cos(phase_angle), inside * np.sin(phase_angle)], 0)


def start_spectrum(window):
    radius = squared_radius(window)
    inside = (np.float32(16.0) * radius < window * window).astype(np.float32)
    norm_scale = np.float32(window) / np.sqrt(np.sum(inside, dtype=np.float32))
    phase_angle = np.float32(-(DEFOCUS_COEF / window)) * radius
    spectrum = np.concatenate(
        [inside * norm_scale * np.cos(phase_angle), inside * norm_scale * np.sin(phase_angle)], 0
    )
    return spectrum.astype(jnp.bfloat16)


def atom_fields(positions, species, slab, species_amp, species_spread, layers):
    species_match = (
        species[None, :] == jnp.arange(species_amp.shape[0], dtype=jnp.int32)[:, None]
    ).astype(species_amp.dtype)
    amplitude = jnp.sum(species_match * species_amp[:, None], 0)
    spread = jnp.sum(species_match * species_spread[:, None], 0)
    inverse = 0.5 / (spread * spread)
    slab_match = (slab[None, :] == jnp.arange(layers, dtype=jnp.int32)[:, None]).astype(
        amplitude.dtype
    )
    return jnp.concatenate([positions, inverse[None, :], slab_match * amplitude[None, :]], 0)


def pick_rows(fields, pick_list):
    valid_mask = (pick_list >= 0).astype(fields.dtype)
    safe_index = jnp.maximum(pick_list, 0)
    gathered = fields[:, safe_index]
    return jnp.concatenate([gathered[:3], gathered[3:] * valid_mask[None]], 0)


def wrap(value, period):
    return value - period * jnp.floor(value * (1.0 / period))


def slices_kernel(
    pos_ref, rows_ref, cols_ref, a_ref, b_ref, prop_ref, spec_ref, out_ref, wave_ref, pot_ref,
    *, field_x
):
    batch = wave_ref.shape[0]
    w = prop_ref.shape[-1]
    layers = pot_ref.shape[-1] // w
    hop = pl.program_id(0)
    layer = pl.program_id(1)
    f32, bf16 = jnp.float32, jnp.bfloat16

    def dot(a, b):
        return jnp.dot(a, b, preferred_element_type=f32)

    @pl.when((hop == 0) & (layer == 0))
    def _():
        rows = dot(a_ref[...], spec_ref[...]).astype(bf16)
        rows = jnp.concatenate([rows[:w], rows[w:]], 1)
        start = dot(rows, b_ref[...]).astype(bf16)
        for p in range(batch):
            wave_ref[p] = start

    @pl.when(layer == 0)
    def _():
        atom_x = rows_ref[0, 0:1, :]
        inverse_row = rows_ref[0, 2:3, :]
        atom_y = cols_ref[0, :, 1:2]
        inverse_col = cols_ref[0, :, 2:3]
        pixel_col = lax.broadcasted_iota(jnp.int32, (w, 1), 0).astype(f32)
        pixel_row = lax.broadcasted_iota(jnp.int32, (1, w), 1).astype(f32)
        for p in range(batch):
            shift_x = pos_ref[p, 0].astype(f32)
            shift_y = pos_ref[p, 1].astype(f32)
            dist_x = wrap(atom_x - shift_x - pixel_col + 0.5 * field_x, field_x) - 0.5 * field_x
            across = jnp.exp(-dist_x * dist_x * inverse_row).astype(bf16)
            dist_y = wrap(atom_y - shift_y - pixel_row + 0.5 * w, w) - 0.5 * w
            along = jnp.exp(-dist_y * dist_y * inverse_col)
            weighted = jnp.concatenate(
                [(cols_ref[0, :, 3 + l : 4 + l] * along).astype(bf16) for l in range(layers)], 1
            )
            pot_ref[p] = dot(across, weighted)

    pr = prop_ref[0]
    pi = prop_ref[1]
    column = pl.ds(pl.multiple_of(layer * w, w), w)
    for p in range(batch):
        psi = wave_ref[p]
        wr = psi[:, :w].astype(f32)
        wi = psi[:, w:].astype(f32)
        v = pot_ref[p, :, column]
        cv = jnp.cos(v)
        sv = jnp.sin(v)
        tr = (wr * cv - wi * sv).astype(bf16)
        ti = (wr * sv + wi * cv).astype(bf16)
        rw = dot(jnp.concatenate([tr, ti], 1), a_ref[...]).astype(bf16)
        sp = dot(b_ref[...], jnp.concatenate([rw[:, :w], rw[:, w:]], 0))
        sr = sp[:w]
        si = sp[w:]
        spb = jnp.concatenate(
            [(sr * pr - si * pi).astype(bf16), (sr * pi + si * pr).astype(bf16)], 0
        )
        br = dot(a_ref[...], spb).astype(bf16)
        psi = dot(jnp.concatenate([br[:w], br[w:]], 1), b_ref[...]).astype(bf16)
        wave_ref[p] = psi

    @pl.when((hop == pl.num_programs(0) - 1) & (layer == pl.num_programs(1) - 1))
    def _():
        out_ref[...] = wave_ref[...]


def run_slices(probe_pos, rows, cols, window, layers, field_x):
    batch = probe_pos.shape[0]
    hops, fields, atoms = rows.shape
    w = window
    a, b = dft_blocks(w)
    prop = propagator(w)
    spec = start_spectrum(w)
    full = lambda shape: pl.BlockSpec(shape, lambda h, l, pos: (0,) * len(shape))
    steps = batch * hops * layers
    flops = steps * 4 * 2 * w * (2 * w) * (2 * w) + batch * hops * 2 * w * atoms * layers * w
    return pl.pallas_call(
        functools.partial(slices_kernel, field_x=float(field_x)),
        out_shape=jax.ShapeDtypeStruct((batch, w, 2 * w), jnp.bfloat16),
        grid_spec=pltpu.PrefetchScalarGridSpec(
            num_scalar_prefetch=1,
            grid=(hops, layers),
            in_specs=[
                pl.BlockSpec((1, fields, atoms), lambda h, l, pos: (h, 0, 0)),
                pl.BlockSpec((1, atoms, fields), lambda h, l, pos: (h, 0, 0)),
                full((2 * w, 2 * w)),
                full((2 * w, 2 * w)),
                full((2, w, w)),
                full((2 * w, w)),
            ],
            out_specs=full((batch, w, 2 * w)),
            scratch_shapes=[
                pltpu.VMEM((batch, w, 2 * w), jnp.bfloat16),
                pltpu.VMEM((batch, w, layers * w), jnp.float32),
            ],
        ),
        compiler_params=pltpu.CompilerParams(
            dimension_semantics=("arbitrary", "arbitrary"),
        ),
        cost_estimate=pl.CostEstimate(
            flops=flops,
            transcendentals=steps * 2 * w * w + batch * hops * 2 * atoms * w,
            bytes_accessed=2 * (2 * w) ** 2 * 2 + 3 * w * w * 4 + batch * w * w * 4,
        ),
    )(probe_pos, rows, cols, jnp.asarray(a), jnp.asarray(b), jnp.asarray(prop), jnp.asarray(spec))


def shards(atom_xy, atom_species, atom_slab, species_amp, species_spread, margin, probe_pos):
    layers = SL_DEV
    window = W
    atoms = atom_xy.shape[-1]
    cap = margin.shape[-1]
    n_lat = lax.axis_size("lat")
    owners = lax.axis_size("slc")
    field_x = n_lat * atoms * (2 * window // cap)
    fields = atom_fields(
        atom_xy[0, 0], atom_species[0, 0], atom_slab[0, 0], species_amp, species_spread, layers
    )
    field_count = fields.shape[0]
    pick_table = margin[0, 0, :, 0]
    picked = jax.vmap(jax.vmap(lambda lst: pick_rows(fields, lst)))(pick_table)
    to_left = lax.ppermute(
        picked[:, 0], "lat", [((i + 1) % n_lat, i) for i in range(n_lat)]
    )
    to_right = lax.ppermute(
        picked[:, 2], "lat", [(i, (i + 1) % n_lat) for i in range(n_lat)]
    )
    local = jnp.stack([to_right, picked[:, 1], to_left], 1)
    gathered = lax.all_gather(local, "slc", axis=0, tiled=False)
    me = lax.axis_index("slc")
    mine = lax.dynamic_index_in_dim(gathered, me, 1, keepdims=False)
    hop_owner = (me + jnp.arange(owners)) % owners
    rows = jnp.take(mine, hop_owner, axis=0)
    rows = jnp.transpose(rows, (0, 2, 1, 3)).reshape(owners, field_count, 3 * cap)
    cols = jnp.transpose(rows, (0, 2, 1))
    batch = probe_pos.shape[0]
    wave = run_slices(probe_pos, rows, cols, window, layers, field_x)
    return wave.reshape(batch, window, 2, window)


def solution(mesh):
    in_specs = (
        P(("groups", "lat"), "slc", None, None),
        P(("groups", "lat"), "slc", None),
        P(("groups", "lat"), "slc", None),
        P(),
        P(),
        P(("groups", "lat"), "slc", None, "rep", None, None),
        P(("groups", "lat", "slc", "rep"), None),
    )
    out_specs = P(("groups", "lat", "slc", "rep"), None, None, None)
    return jax.shard_map(shards, mesh=mesh, in_specs=in_specs, out_specs=out_specs, check_vma=False)
```

```python
import functools
import math

import jax
import numpy as np
import jax.numpy as jnp
from jax import lax
from jax.experimental import pallas as pl
from jax.experimental.pallas import tpu as pltpu
from jax.sharding import PartitionSpec as P

W = 256
SL_DEV = 2


PROPAGATION_COEF = 0.001
DEFOCUS_COEF = 4.19


def centered_frequency(window):
    indices = np.arange(window, dtype=np.int32)
    return np.where(indices < window // 2, indices, indices - window).astype(np.float32)


def squared_radius(window):
    frequency = centered_frequency(window)
    return frequency[:, None] * frequency[:, None] + frequency[None, :] * frequency[None, :]


def dft_blocks(window):
    indices = np.arange(window, dtype=np.int32)
    product = indices[:, None] * indices[None, :] % window
    angle = np.float32(2.0 * math.pi / window) * product.astype(np.float32)
    scale = np.float32(math.sqrt(window))
    re = (np.cos(angle) / scale).astype(jnp.bfloat16)
    im = (np.sin(angle) / scale).astype(jnp.bfloat16)
    a = np.block([[re, -im], [im, re]])
    b = np.block([[re, im], [-im, re]])
    return a, b


def propagator(window):
    radius = squared_radius(window)
    inside = (np.float32(9.0) * radius < window * window).astype(np.float32)
    phase_angle = np.float32(-PROPAGATION_COEF * (65536.0 / (window * window))) * radius
    return np.stack([inside * np.cos(phase_angle), inside * np.sin(phase_angle)], 0)


def start_spectrum(window):
    radius = squared_radius(window)
    inside = (np.float32(16.0) * radius < window * window).astype(np.float32)
    norm_scale = np.float32(window) / np.sqrt(np.sum(inside, dtype=np.float32))
    phase_angle = np.float32(-(DEFOCUS_COEF / window)) * radius
    spectrum = np.concatenate(
        [inside * norm_scale * np.cos(phase_angle), inside * norm_scale * np.sin(phase_angle)], 0
    )
    return spectrum.astype(jnp.bfloat16)


def atom_fields(positions, species, slab, species_amp, species_spread, layers):
    species_match = (
        species[None, :] == jnp.arange(species_amp.shape[0], dtype=jnp.int32)[:, None]
    ).astype(species_amp.dtype)
    amplitude = jnp.sum(species_match * species_amp[:, None], 0)
    spread = jnp.sum(species_match * species_spread[:, None], 0)
    inverse = 0.5 / (spread * spread)
    slab_match = (slab[None, :] == jnp.arange(layers, dtype=jnp.int32)[:, None]).astype(
        amplitude.dtype
    )
    return jnp.concatenate([positions, inverse[None, :], slab_match * amplitude[None, :]], 0)


def pick_rows(fields, pick_list):
    valid_mask = (pick_list >= 0).astype(fields.dtype)
    safe_index = jnp.maximum(pick_list, 0)
    gathered = fields[:, safe_index]
    return jnp.concatenate([gathered[:3], gathered[3:] * valid_mask[None]], 0)


def wrap(value, period):
    return value - period * jnp.floor(value * (1.0 / period))


def sincos(v):
    q = jnp.floor(v * 0.6366197723675814 + 0.5)
    r = v - q * 1.5703125
    r = r - q * 4.837512969970703125e-4
    r = r - q * 7.549789954891882e-8
    z = r * r
    s = r + r * z * (-1.6666654611e-1 + z * (8.3321608736e-3 + z * -1.9515295891e-4))
    c = 1.0 - 0.5 * z + z * z * (4.166664568298827e-2 + z * (-1.388731625493765e-3 + z * 2.443315711809948e-5))
    n = q.astype(jnp.int32)
    swap = (n & 1) == 1
    sin_v = jnp.where(swap, c, s)
    cos_v = jnp.where(swap, s, c)
    sin_v = jnp.where((n & 2) == 2, -sin_v, sin_v)
    cos_v = jnp.where(((n + 1) & 2) == 2, -cos_v, cos_v)
    return sin_v, cos_v


def slices_kernel(
    pos_ref, rows_ref, cols_ref, a_ref, b_ref, prop_ref, spec_ref, out_ref, wave_ref, pot_ref,
    *, field_x
):
    batch = wave_ref.shape[0]
    w = prop_ref.shape[-1]
    layers = pot_ref.shape[-1] // w
    hop = pl.program_id(0)
    layer = pl.program_id(1)
    f32, bf16 = jnp.float32, jnp.bfloat16

    def dot(a, b):
        return jnp.dot(a, b, preferred_element_type=f32)

    @pl.when((hop == 0) & (layer == 0))
    def _():
        rows = dot(a_ref[...], spec_ref[...]).astype(bf16)
        rows = jnp.concatenate([rows[:w], rows[w:]], 1)
        start = dot(rows, b_ref[...]).astype(bf16)
        for p in range(batch):
            wave_ref[p] = start

    @pl.when(layer == 0)
    def _():
        atom_x = rows_ref[0, 0:1, :]
        inverse_row = rows_ref[0, 2:3, :]
        atom_y = cols_ref[0, :, 1:2]
        inverse_col = cols_ref[0, :, 2:3]
        pixel_col = lax.broadcasted_iota(jnp.int32, (w, 1), 0).astype(f32)
        pixel_row = lax.broadcasted_iota(jnp.int32, (1, w), 1).astype(f32)
        for p in range(batch):
            shift_x = pos_ref[p, 0].astype(f32)
            shift_y = pos_ref[p, 1].astype(f32)
            dist_x = wrap(atom_x - shift_x - pixel_col + 0.5 * field_x, field_x) - 0.5 * field_x
            across = jnp.exp(-dist_x * dist_x * inverse_row).astype(bf16)
            dist_y = wrap(atom_y - shift_y - pixel_row + 0.5 * w, w) - 0.5 * w
            along = jnp.exp(-dist_y * dist_y * inverse_col)
            weighted = jnp.concatenate(
                [(cols_ref[0, :, 3 + l : 4 + l] * along).astype(bf16) for l in range(layers)], 1
            )
            pot_ref[p] = dot(across, weighted)

    pr = prop_ref[0]
    pi = prop_ref[1]
    column = pl.ds(pl.multiple_of(layer * w, w), w)
    for p in range(batch):
        psi = wave_ref[p]
        wr = psi[:, :w].astype(f32)
        wi = psi[:, w:].astype(f32)
        v = pot_ref[p, :, column]
        sv, cv = sincos(v)
        tr = (wr * cv - wi * sv).astype(bf16)
        ti = (wr * sv + wi * cv).astype(bf16)
        rw = dot(jnp.concatenate([tr, ti], 1), a_ref[...]).astype(bf16)
        sp = dot(b_ref[...], jnp.concatenate([rw[:, :w], rw[:, w:]], 0))
        sr = sp[:w]
        si = sp[w:]
        spb = jnp.concatenate(
            [(sr * pr - si * pi).astype(bf16), (sr * pi + si * pr).astype(bf16)], 0
        )
        br = dot(a_ref[...], spb).astype(bf16)
        psi = dot(jnp.concatenate([br[:w], br[w:]], 1), b_ref[...]).astype(bf16)
        wave_ref[p] = psi

    @pl.when((hop == pl.num_programs(0) - 1) & (layer == pl.num_programs(1) - 1))
    def _():
        out_ref[...] = wave_ref[...]


def run_slices(probe_pos, rows, cols, window, layers, field_x):
    batch = probe_pos.shape[0]
    hops, fields, atoms = rows.shape
    w = window
    a, b = dft_blocks(w)
    prop = propagator(w)
    spec = start_spectrum(w)
    full = lambda shape: pl.BlockSpec(shape, lambda h, l, pos: (0,) * len(shape))
    steps = batch * hops * layers
    flops = steps * 4 * 2 * w * (2 * w) * (2 * w) + batch * hops * 2 * w * atoms * layers * w
    return pl.pallas_call(
        functools.partial(slices_kernel, field_x=float(field_x)),
        out_shape=jax.ShapeDtypeStruct((batch, w, 2 * w), jnp.bfloat16),
        grid_spec=pltpu.PrefetchScalarGridSpec(
            num_scalar_prefetch=1,
            grid=(hops, layers),
            in_specs=[
                pl.BlockSpec((1, fields, atoms), lambda h, l, pos: (h, 0, 0)),
                pl.BlockSpec((1, atoms, fields), lambda h, l, pos: (h, 0, 0)),
                full((2 * w, 2 * w)),
                full((2 * w, 2 * w)),
                full((2, w, w)),
                full((2 * w, w)),
            ],
            out_specs=full((batch, w, 2 * w)),
            scratch_shapes=[
                pltpu.VMEM((batch, w, 2 * w), jnp.bfloat16),
                pltpu.VMEM((batch, w, layers * w), jnp.float32),
            ],
        ),
        compiler_params=pltpu.CompilerParams(
            dimension_semantics=("arbitrary", "arbitrary"),
        ),
        cost_estimate=pl.CostEstimate(
            flops=flops,
            transcendentals=steps * 2 * w * w + batch * hops * 2 * atoms * w,
            bytes_accessed=2 * (2 * w) ** 2 * 2 + 3 * w * w * 4 + batch * w * w * 4,
        ),
    )(probe_pos, rows, cols, jnp.asarray(a), jnp.asarray(b), jnp.asarray(prop), jnp.asarray(spec))


def shards(atom_xy, atom_species, atom_slab, species_amp, species_spread, margin, probe_pos):
    layers = SL_DEV
    window = W
    atoms = atom_xy.shape[-1]
    cap = margin.shape[-1]
    n_lat = lax.axis_size("lat")
    owners = lax.axis_size("slc")
    field_x = n_lat * atoms * (2 * window // cap)
    fields = atom_fields(
        atom_xy[0, 0], atom_species[0, 0], atom_slab[0, 0], species_amp, species_spread, layers
    )
    field_count = fields.shape[0]
    pick_table = margin[0, 0, :, 0]
    picked = jax.vmap(jax.vmap(lambda lst: pick_rows(fields, lst)))(pick_table)
    to_left = lax.ppermute(
        picked[:, 0], "lat", [((i + 1) % n_lat, i) for i in range(n_lat)]
    )
    to_right = lax.ppermute(
        picked[:, 2], "lat", [(i, (i + 1) % n_lat) for i in range(n_lat)]
    )
    local = jnp.stack([to_right, picked[:, 1], to_left], 1)
    gathered = lax.all_gather(local, "slc", axis=0, tiled=False)
    me = lax.axis_index("slc")
    mine = lax.dynamic_index_in_dim(gathered, me, 1, keepdims=False)
    hop_owner = (me + jnp.arange(owners)) % owners
    rows = jnp.take(mine, hop_owner, axis=0)
    rows = jnp.transpose(rows, (0, 2, 1, 3)).reshape(owners, field_count, 3 * cap)
    cols = jnp.transpose(rows, (0, 2, 1))
    batch = probe_pos.shape[0]
    wave = run_slices(probe_pos, rows, cols, window, layers, field_x)
    return wave.reshape(batch, window, 2, window)


def solution(mesh):
    in_specs = (
        P(("groups", "lat"), "slc", None, None),
        P(("groups", "lat"), "slc", None),
        P(("groups", "lat"), "slc", None),
        P(),
        P(),
        P(("groups", "lat"), "slc", None, "rep", None, None),
        P(("groups", "lat", "slc", "rep"), None),
    )
    out_specs = P(("groups", "lat", "slc", "rep"), None, None, None)
    return jax.shard_map(shards, mesh=mesh, in_specs=in_specs, out_specs=out_specs, check_vma=False)
```

```python
import functools
import math

import jax
import numpy as np
import jax.numpy as jnp
from jax import lax
from jax.experimental import pallas as pl
from jax.experimental.pallas import tpu as pltpu
from jax.sharding import PartitionSpec as P

W = 256
SL_DEV = 2


PROPAGATION_COEF = 0.001
DEFOCUS_COEF = 4.19


def centered_frequency(window):
    indices = np.arange(window, dtype=np.int32)
    return np.where(indices < window // 2, indices, indices - window).astype(np.float32)


def squared_radius(window):
    frequency = centered_frequency(window)
    return frequency[:, None] * frequency[:, None] + frequency[None, :] * frequency[None, :]


def dft_blocks(window):
    indices = np.arange(window, dtype=np.int32)
    product = indices[:, None] * indices[None, :] % window
    angle = np.float32(2.0 * math.pi / window) * product.astype(np.float32)
    scale = np.float32(math.sqrt(window))
    re = (np.cos(angle) / scale).astype(jnp.bfloat16)
    im = (np.sin(angle) / scale).astype(jnp.bfloat16)
    a = np.block([[re, -im], [im, re]])
    b = np.block([[re, im], [-im, re]])
    return a, b


def propagator(window):
    radius = squared_radius(window)
    inside = (np.float32(9.0) * radius < window * window).astype(np.float32)
    phase_angle = np.float32(-PROPAGATION_COEF * (65536.0 / (window * window))) * radius
    return np.stack([inside * np.cos(phase_angle), inside * np.sin(phase_angle)], 0)


def start_spectrum(window):
    radius = squared_radius(window)
    inside = (np.float32(16.0) * radius < window * window).astype(np.float32)
    norm_scale = np.float32(window) / np.sqrt(np.sum(inside, dtype=np.float32))
    phase_angle = np.float32(-(DEFOCUS_COEF / window)) * radius
    spectrum = np.concatenate(
        [inside * norm_scale * np.cos(phase_angle), inside * norm_scale * np.sin(phase_angle)], 0
    )
    return spectrum.astype(jnp.bfloat16)


def atom_fields(positions, species, slab, species_amp, species_spread, layers):
    species_match = (
        species[None, :] == jnp.arange(species_amp.shape[0], dtype=jnp.int32)[:, None]
    ).astype(species_amp.dtype)
    amplitude = jnp.sum(species_match * species_amp[:, None], 0)
    spread = jnp.sum(species_match * species_spread[:, None], 0)
    inverse = 0.5 / (spread * spread)
    slab_match = (slab[None, :] == jnp.arange(layers, dtype=jnp.int32)[:, None]).astype(
        amplitude.dtype
    )
    return jnp.concatenate([positions, inverse[None, :], slab_match * amplitude[None, :]], 0)


def pick_rows(fields, pick_list):
    valid_mask = (pick_list >= 0).astype(fields.dtype)
    safe_index = jnp.maximum(pick_list, 0)
    gathered = fields[:, safe_index]
    return jnp.concatenate([gathered[:3], gathered[3:] * valid_mask[None]], 0)


def wrap(value, period):
    return value - period * jnp.floor(value * (1.0 / period))


def sincos(v):
    q = jnp.floor(v * 0.6366197723675814 + 0.5)
    r = v - q * 1.5703125
    r = r - q * 4.837512969970703125e-4
    r = r - q * 7.549789954891882e-8
    z = r * r
    s = r + r * z * (-1.6666654611e-1 + z * (8.3321608736e-3 + z * -1.9515295891e-4))
    c = 1.0 - 0.5 * z + z * z * (4.166664568298827e-2 + z * (-1.388731625493765e-3 + z * 2.443315711809948e-5))
    n = q.astype(jnp.int32)
    swap = (n & 1) == 1
    sin_v = jnp.where(swap, c, s)
    cos_v = jnp.where(swap, s, c)
    sin_v = jnp.where((n & 2) == 2, -sin_v, sin_v)
    cos_v = jnp.where(((n + 1) & 2) == 2, -cos_v, cos_v)
    return sin_v, cos_v


def slices_kernel(*refs, field_x, carried):
    if carried:
        pos_ref, rows_ref, cols_ref, a_ref, b_ref, prop_ref, start_ref, out_ref, wave_ref, pot_ref = refs
    else:
        pos_ref, rows_ref, cols_ref, a_ref, b_ref, prop_ref, spec_ref, out_ref, wave_ref, pot_ref = refs
    batch = wave_ref.shape[0]
    w = prop_ref.shape[-1]
    layers = pot_ref.shape[-1] // w
    hop = pl.program_id(0)
    layer = pl.program_id(1)
    f32, bf16 = jnp.float32, jnp.bfloat16

    def dot(a, b):
        return jnp.dot(a, b, preferred_element_type=f32)

    @pl.when((hop == 0) & (layer == 0))
    def _():
        if carried:
            wave_ref[...] = start_ref[...]
        else:
            rows = dot(a_ref[...], spec_ref[...]).astype(bf16)
            rows = jnp.concatenate([rows[:w], rows[w:]], 1)
            start = dot(rows, b_ref[...]).astype(bf16)
            for p in range(batch):
                wave_ref[p] = start

    @pl.when(layer == 0)
    def _():
        atom_x = rows_ref[0, 0:1, :]
        inverse_row = rows_ref[0, 2:3, :]
        atom_y = cols_ref[0, :, 1:2]
        inverse_col = cols_ref[0, :, 2:3]
        pixel_col = lax.broadcasted_iota(jnp.int32, (w, 1), 0).astype(f32)
        pixel_row = lax.broadcasted_iota(jnp.int32, (1, w), 1).astype(f32)
        for p in range(batch):
            shift_x = pos_ref[p, 0].astype(f32)
            shift_y = pos_ref[p, 1].astype(f32)
            dist_x = wrap(atom_x - shift_x - pixel_col + 0.5 * field_x, field_x) - 0.5 * field_x
            across = jnp.exp(-dist_x * dist_x * inverse_row).astype(bf16)
            dist_y = wrap(atom_y - shift_y - pixel_row + 0.5 * w, w) - 0.5 * w
            along = jnp.exp(-dist_y * dist_y * inverse_col)
            weighted = jnp.concatenate(
                [(cols_ref[0, :, 3 + l : 4 + l] * along).astype(bf16) for l in range(layers)], 1
            )
            pot_ref[p] = dot(across, weighted)

    pr = prop_ref[0]
    pi = prop_ref[1]
    column = pl.ds(pl.multiple_of(layer * w, w), w)
    for p in range(batch):
        psi = wave_ref[p]
        wr = psi[:, :w].astype(f32)
        wi = psi[:, w:].astype(f32)
        v = pot_ref[p, :, column]
        sv, cv = sincos(v)
        tr = (wr * cv - wi * sv).astype(bf16)
        ti = (wr * sv + wi * cv).astype(bf16)
        rw = dot(jnp.concatenate([tr, ti], 1), a_ref[...]).astype(bf16)
        sp = dot(b_ref[...], jnp.concatenate([rw[:, :w], rw[:, w:]], 0))
        sr = sp[:w]
        si = sp[w:]
        spb = jnp.concatenate(
            [(sr * pr - si * pi).astype(bf16), (sr * pi + si * pr).astype(bf16)], 0
        )
        br = dot(a_ref[...], spb).astype(bf16)
        psi = dot(jnp.concatenate([br[:w], br[w:]], 1), b_ref[...]).astype(bf16)
        wave_ref[p] = psi

    @pl.when((hop == pl.num_programs(0) - 1) & (layer == pl.num_programs(1) - 1))
    def _():
        out_ref[...] = wave_ref[...]


def run_slices(probe_pos, rows, window, layers, field_x, wave=None):
    batch = probe_pos.shape[0]
    hops, fields, atoms = rows.shape
    cols = jnp.transpose(rows, (0, 2, 1))
    w = window
    a, b = dft_blocks(w)
    prop = propagator(w)
    full = lambda shape: pl.BlockSpec(shape, lambda h, l, pos: (0,) * len(shape))
    carried = wave is not None
    last = wave if carried else jnp.asarray(start_spectrum(w))
    last_spec = full((batch, w, 2 * w)) if carried else full((2 * w, w))
    steps = batch * hops * layers
    flops = steps * 4 * 2 * w * (2 * w) * (2 * w) + batch * hops * 2 * w * atoms * layers * w
    return pl.pallas_call(
        functools.partial(slices_kernel, field_x=float(field_x), carried=carried),
        out_shape=jax.ShapeDtypeStruct((batch, w, 2 * w), jnp.bfloat16),
        grid_spec=pltpu.PrefetchScalarGridSpec(
            num_scalar_prefetch=1,
            grid=(hops, layers),
            in_specs=[
                pl.BlockSpec((1, fields, atoms), lambda h, l, pos: (h, 0, 0)),
                pl.BlockSpec((1, atoms, fields), lambda h, l, pos: (h, 0, 0)),
                full((2 * w, 2 * w)),
                full((2 * w, 2 * w)),
                full((2, w, w)),
                last_spec,
            ],
            out_specs=full((batch, w, 2 * w)),
            scratch_shapes=[
                pltpu.VMEM((batch, w, 2 * w), jnp.bfloat16),
                pltpu.VMEM((batch, w, layers * w), jnp.float32),
            ],
        ),
        compiler_params=pltpu.CompilerParams(
            dimension_semantics=("arbitrary", "arbitrary"),
        ),
        cost_estimate=pl.CostEstimate(
            flops=flops,
            transcendentals=steps * 2 * w * w + batch * hops * 2 * atoms * w,
            bytes_accessed=2 * (2 * w) ** 2 * 2 + 3 * w * w * 4 + batch * w * w * 4,
        ),
    )(probe_pos, rows, cols, jnp.asarray(a), jnp.asarray(b), jnp.asarray(prop), last)


def shards(atom_xy, atom_species, atom_slab, species_amp, species_spread, margin, probe_pos):
    layers = SL_DEV
    window = W
    atoms = atom_xy.shape[-1]
    cap = margin.shape[-1]
    n_lat = lax.axis_size("lat")
    owners = lax.axis_size("slc")
    field_x = n_lat * atoms * (2 * window // cap)
    f32 = jnp.float32
    raw = jnp.concatenate(
        [atom_xy[0, 0], atom_species[0, 0][None].astype(f32), atom_slab[0, 0][None].astype(f32)], 0
    )
    marg = margin[0, 0, :, 0].astype(f32)
    size = raw.size

    def pack(o):
        return jnp.concatenate([raw.reshape(-1), marg[:, o].reshape(-1)])

    from_left = lax.ppermute(pack(2), "lat", [(i, (i + 1) % n_lat) for i in range(n_lat)])
    from_right = lax.ppermute(pack(0), "lat", [((i + 1) % n_lat, i) for i in range(n_lat)])

    def unpack(packed):
        return packed[:size].reshape(raw.shape), packed[size:].reshape(marg.shape[0], cap)

    left_raw, left_marg = unpack(from_left)
    right_raw, right_marg = unpack(from_right)
    raws = jnp.stack([left_raw, raw, right_raw], 0)
    margs = jnp.stack([left_marg, marg[:, 1], right_marg], 0).astype(jnp.int32)
    fields = jax.vmap(
        lambda r: atom_fields(
            r[:2], r[2].astype(jnp.int32), r[3].astype(jnp.int32), species_amp, species_spread, layers
        )
    )(raws)
    picked = jax.vmap(lambda f, m: jax.vmap(lambda lst: pick_rows(f, lst))(m))(fields, margs)
    field_count = picked.shape[2]
    rows_all = jnp.transpose(picked, (1, 2, 0, 3)).reshape(-1, field_count, 3 * cap)
    me = lax.axis_index("slc")
    first = lax.dynamic_index_in_dim(rows_all, me, 0, keepdims=True)
    later = []
    for hop in range(1, owners):
        outgoing = lax.dynamic_index_in_dim(rows_all, (me - hop) % owners, 0, keepdims=True)
        later.append(
            lax.ppermute(outgoing, "slc", [(i, (i - hop) % owners) for i in range(owners)])
        )
    batch = probe_pos.shape[0]
    wave = run_slices(probe_pos, first, window, layers, field_x)
    if later:
        wave = run_slices(probe_pos, jnp.concatenate(later, 0), window, layers, field_x, wave)
    return wave.reshape(batch, window, 2, window)


def solution(mesh):
    in_specs = (
        P(("groups", "lat"), "slc", None, None),
        P(("groups", "lat"), "slc", None),
        P(("groups", "lat"), "slc", None),
        P(),
        P(),
        P(("groups", "lat"), "slc", None, "rep", None, None),
        P(("groups", "lat", "slc", "rep"), None),
    )
    out_specs = P(("groups", "lat", "slc", "rep"), None, None, None)
    return jax.shard_map(shards, mesh=mesh, in_specs=in_specs, out_specs=out_specs, check_vma=False)
```

```python
import functools
import math

import jax
import numpy as np
import jax.numpy as jnp
from jax import lax
from jax.experimental import pallas as pl
from jax.experimental.pallas import tpu as pltpu
from jax.sharding import PartitionSpec as P

W = 256
SL_DEV = 2


PROPAGATION_COEF = 0.001
DEFOCUS_COEF = 4.19


def centered_frequency(window):
    indices = np.arange(window, dtype=np.int32)
    return np.where(indices < window // 2, indices, indices - window).astype(np.float32)


def squared_radius(window):
    frequency = centered_frequency(window)
    return frequency[:, None] * frequency[:, None] + frequency[None, :] * frequency[None, :]


def dft_blocks(window):
    indices = np.arange(window, dtype=np.int32)
    product = indices[:, None] * indices[None, :] % window
    angle = np.float32(2.0 * math.pi / window) * product.astype(np.float32)
    scale = np.float32(math.sqrt(window))
    re = (np.cos(angle) / scale).astype(jnp.bfloat16)
    im = (np.sin(angle) / scale).astype(jnp.bfloat16)
    a = np.block([[re, -im], [im, re]])
    b = np.block([[re, im], [-im, re]])
    return a, b


def propagator(window):
    radius = squared_radius(window)
    inside = (np.float32(9.0) * radius < window * window).astype(np.float32)
    phase_angle = np.float32(-PROPAGATION_COEF * (65536.0 / (window * window))) * radius
    return np.stack([inside * np.cos(phase_angle), inside * np.sin(phase_angle)], 0)


def start_spectrum(window):
    radius = squared_radius(window)
    inside = (np.float32(16.0) * radius < window * window).astype(np.float32)
    norm_scale = np.float32(window) / np.sqrt(np.sum(inside, dtype=np.float32))
    phase_angle = np.float32(-(DEFOCUS_COEF / window)) * radius
    spectrum = np.concatenate(
        [inside * norm_scale * np.cos(phase_angle), inside * norm_scale * np.sin(phase_angle)], 0
    )
    return spectrum.astype(jnp.bfloat16)


def atom_fields(positions, species, slab, species_amp, species_spread, layers):
    species_match = (
        species[None, :] == jnp.arange(species_amp.shape[0], dtype=jnp.int32)[:, None]
    ).astype(species_amp.dtype)
    amplitude = jnp.sum(species_match * species_amp[:, None], 0)
    spread = jnp.sum(species_match * species_spread[:, None], 0)
    inverse = 0.5 / (spread * spread)
    slab_match = (slab[None, :] == jnp.arange(layers, dtype=jnp.int32)[:, None]).astype(
        amplitude.dtype
    )
    return jnp.concatenate([positions, inverse[None, :], slab_match * amplitude[None, :]], 0)


def pick_rows(fields, pick_list):
    valid_mask = (pick_list >= 0).astype(fields.dtype)
    safe_index = jnp.maximum(pick_list, 0)
    gathered = fields[:, safe_index]
    return jnp.concatenate([gathered[:3], gathered[3:] * valid_mask[None]], 0)


def wrap(value, period):
    return value - period * jnp.floor(value * (1.0 / period))


def sincos(v):
    q = jnp.floor(v * 0.6366197723675814 + 0.5)
    r = v - q * 1.5703125
    r = r - q * 4.837512969970703125e-4
    r = r - q * 7.549789954891882e-8
    z = r * r
    s = r + r * z * (-1.6666654611e-1 + z * (8.3321608736e-3 + z * -1.9515295891e-4))
    c = 1.0 - 0.5 * z + z * z * (4.166664568298827e-2 + z * (-1.388731625493765e-3 + z * 2.443315711809948e-5))
    n = q.astype(jnp.int32)
    swap = (n & 1) == 1
    sin_v = jnp.where(swap, c, s)
    cos_v = jnp.where(swap, s, c)
    sin_v = jnp.where((n & 2) == 2, -sin_v, sin_v)
    cos_v = jnp.where(((n + 1) & 2) == 2, -cos_v, cos_v)
    return sin_v, cos_v


def slices_kernel(*refs, field_x, carried, cap):
    (pos_ref, owner_ref, table_ref, pk_ref, a_ref, b_ref, prop_ref, last_ref,
     out_ref, wave_ref, pot_ref) = refs
    batch = wave_ref.shape[0]
    w = prop_ref.shape[-1]
    layers = pot_ref.shape[-1] // w
    species_count = table_ref.shape[1]
    hop = pl.program_id(0)
    layer = pl.program_id(1)
    f32, bf16 = jnp.float32, jnp.bfloat16

    def dot(a, b):
        return jnp.dot(a, b, preferred_element_type=f32)

    @pl.when((hop == 0) & (layer == 0))
    def _():
        if carried:
            wave_ref[...] = last_ref[...]
        else:
            rows = dot(a_ref[...], last_ref[...]).astype(bf16)
            rows = jnp.concatenate([rows[:w], rows[w:]], 1)
            start = dot(rows, b_ref[...]).astype(bf16)
            for p in range(batch):
                wave_ref[p] = start

    @pl.when(layer == 0)
    def _():
        entry = owner_ref[0]
        blocks = []
        for slot in range(3):
            raw = pk_ref[0, slot, 0:4, :]
            listed = pk_ref[0, slot, pl.ds(4 + entry, 1), :][:, :cap]
            species = raw[2:3]
            slab = raw[3:4]
            amplitude = jnp.zeros_like(species)
            inverse = jnp.zeros_like(species)
            for k in range(species_count):
                match = species == float(k)
                amplitude = jnp.where(match, table_ref[0, k], amplitude)
                inverse = jnp.where(match, table_ref[1, k], inverse)
            zero = jnp.zeros_like(species)
            per_layer = [jnp.where(slab == float(l), amplitude, zero) for l in range(layers)]
            fields = jnp.concatenate(
                [raw[0:2], inverse] + per_layer + [zero] * (8 - 3 - layers), 0
            )
            atoms = fields.shape[1]
            safe = jnp.maximum(listed, 0.0).astype(jnp.int32)
            onehot = (lax.broadcasted_iota(jnp.int32, (atoms, cap), 0) == safe).astype(f32)
            picked = jnp.dot(
                fields, onehot, preferred_element_type=f32, precision=lax.Precision.HIGHEST
            )
            valid = (listed >= 0.0).astype(f32)
            keep = lax.broadcasted_iota(jnp.int32, (8, 1), 0) < 3
            picked = jnp.where(keep, picked, picked * valid)
            blocks.append(picked)
        rows = jnp.concatenate(blocks, 1)
        cols = rows.T
        atom_x = rows[0:1]
        inverse_row = rows[2:3]
        atom_y = cols[:, 1:2]
        inverse_col = cols[:, 2:3]
        pixel_col = lax.broadcasted_iota(jnp.int32, (w, 1), 0).astype(f32)
        pixel_row = lax.broadcasted_iota(jnp.int32, (1, w), 1).astype(f32)
        for p in range(batch):
            shift_x = pos_ref[p, 0].astype(f32)
            shift_y = pos_ref[p, 1].astype(f32)
            dist_x = wrap(atom_x - shift_x - pixel_col + 0.5 * field_x, field_x) - 0.5 * field_x
            across = jnp.exp(-dist_x * dist_x * inverse_row).astype(bf16)
            dist_y = wrap(atom_y - shift_y - pixel_row + 0.5 * w, w) - 0.5 * w
            along = jnp.exp(-dist_y * dist_y * inverse_col)
            weighted = jnp.concatenate(
                [(cols[:, 3 + l : 4 + l] * along).astype(bf16) for l in range(layers)], 1
            )
            pot_ref[p] = dot(across, weighted)

    pr = prop_ref[0]
    pi = prop_ref[1]
    column = pl.ds(pl.multiple_of(layer * w, w), w)
    for p in range(batch):
        psi = wave_ref[p]
        wr = psi[:, :w].astype(f32)
        wi = psi[:, w:].astype(f32)
        v = pot_ref[p, :, column]
        sv, cv = sincos(v)
        tr = (wr * cv - wi * sv).astype(bf16)
        ti = (wr * sv + wi * cv).astype(bf16)
        rw = dot(jnp.concatenate([tr, ti], 1), a_ref[...]).astype(bf16)
        sp = dot(b_ref[...], jnp.concatenate([rw[:, :w], rw[:, w:]], 0))
        sr = sp[:w]
        si = sp[w:]
        spb = jnp.concatenate(
            [(sr * pr - si * pi).astype(bf16), (sr * pi + si * pr).astype(bf16)], 0
        )
        br = dot(a_ref[...], spb).astype(bf16)
        psi = dot(jnp.concatenate([br[:w], br[w:]], 1), b_ref[...]).astype(bf16)
        wave_ref[p] = psi

    @pl.when((hop == pl.num_programs(0) - 1) & (layer == pl.num_programs(1) - 1))
    def _():
        out_ref[...] = wave_ref[...]


def run_slices(probe_pos, entry, table, packs, window, layers, field_x, cap, wave=None):
    batch = probe_pos.shape[0]
    hops = packs.shape[0]
    w = window
    a, b = dft_blocks(w)
    prop = propagator(w)
    full = lambda shape: pl.BlockSpec(shape, lambda h, l, *_: (0,) * len(shape))
    carried = wave is not None
    last = wave if carried else jnp.asarray(start_spectrum(w))
    atoms = 3 * cap
    steps = batch * hops * layers
    flops = steps * 4 * 2 * w * (2 * w) * (2 * w) + batch * hops * 2 * w * atoms * layers * w
    return pl.pallas_call(
        functools.partial(slices_kernel, field_x=float(field_x), carried=carried, cap=cap),
        out_shape=jax.ShapeDtypeStruct((batch, w, 2 * w), jnp.bfloat16),
        grid_spec=pltpu.PrefetchScalarGridSpec(
            num_scalar_prefetch=2,
            grid=(hops, layers),
            in_specs=[
                pl.BlockSpec(memory_space=pltpu.SMEM),
                pl.BlockSpec((1,) + packs.shape[1:], lambda h, l, *_: (h, 0, 0, 0)),
                full((2 * w, 2 * w)),
                full((2 * w, 2 * w)),
                full((2, w, w)),
                full(last.shape),
            ],
            out_specs=full((batch, w, 2 * w)),
            scratch_shapes=[
                pltpu.VMEM((batch, w, 2 * w), jnp.bfloat16),
                pltpu.VMEM((batch, w, layers * w), jnp.float32),
            ],
        ),
        compiler_params=pltpu.CompilerParams(
            dimension_semantics=("arbitrary", "arbitrary"),
        ),
        cost_estimate=pl.CostEstimate(
            flops=flops,
            transcendentals=steps * 2 * w * w + batch * hops * 2 * atoms * w,
            bytes_accessed=2 * (2 * w) ** 2 * 2 + 3 * w * w * 4 + batch * w * w * 4,
        ),
    )(probe_pos, entry, table, packs, jnp.asarray(a), jnp.asarray(b), jnp.asarray(prop), last)


def shards(atom_xy, atom_species, atom_slab, species_amp, species_spread, margin, probe_pos):
    layers = SL_DEV
    window = W
    atoms = atom_xy.shape[-1]
    cap = margin.shape[-1]
    n_lat = lax.axis_size("lat")
    owners = lax.axis_size("slc")
    field_x = n_lat * atoms * (2 * window // cap)
    f32 = jnp.float32
    raw = jnp.concatenate(
        [atom_xy[0, 0], atom_species[0, 0][None].astype(f32), atom_slab[0, 0][None].astype(f32)], 0
    )
    marg = jnp.transpose(margin[0, 0, :, 0], (1, 0, 2)).astype(f32)
    marg = jnp.pad(marg, ((0, 0), (0, 0), (0, atoms - cap)), constant_values=-1.0)
    packs = jnp.concatenate([jnp.broadcast_to(raw[None], (3,) + raw.shape), marg], 1)
    from_left = lax.ppermute(packs[2], "lat", [(i, (i + 1) % n_lat) for i in range(n_lat)])
    from_right = lax.ppermute(packs[0], "lat", [((i + 1) % n_lat, i) for i in range(n_lat)])
    local = jnp.stack([from_left, packs[1], from_right], 0)[None]
    me = lax.axis_index("slc")
    entry = jnp.reshape(me, (1,)).astype(jnp.int32)
    later = [
        lax.ppermute(local, "slc", [(i, (i - hop) % owners) for i in range(owners)])
        for hop in range(1, owners)
    ]
    table = jnp.stack([species_amp, 0.5 / (species_spread * species_spread)], 0)
    batch = probe_pos.shape[0]
    wave = run_slices(probe_pos, entry, table, local, window, layers, field_x, cap)
    if later:
        wave = run_slices(
            probe_pos, entry, table, jnp.concatenate(later, 0), window, layers, field_x, cap, wave
        )
    return wave.reshape(batch, window, 2, window)


def solution(mesh):
    in_specs = (
        P(("groups", "lat"), "slc", None, None),
        P(("groups", "lat"), "slc", None),
        P(("groups", "lat"), "slc", None),
        P(),
        P(),
        P(("groups", "lat"), "slc", None, "rep", None, None),
        P(("groups", "lat", "slc", "rep"), None),
    )
    out_specs = P(("groups", "lat", "slc", "rep"), None, None, None)
    return jax.shard_map(shards, mesh=mesh, in_specs=in_specs, out_specs=out_specs, check_vma=False)
```

```python
import functools
import math

import jax
import numpy as np
import jax.numpy as jnp
from jax import lax
from jax.experimental import pallas as pl
from jax.experimental.pallas import tpu as pltpu
from jax.sharding import PartitionSpec as P

W = 256
SL_DEV = 2


PROPAGATION_COEF = 0.001
DEFOCUS_COEF = 4.19


def centered_frequency(window):
    indices = np.arange(window, dtype=np.int32)
    return np.where(indices < window // 2, indices, indices - window).astype(np.float32)


def squared_radius(window):
    frequency = centered_frequency(window)
    return frequency[:, None] * frequency[:, None] + frequency[None, :] * frequency[None, :]


def dft_blocks(window):
    indices = np.arange(window, dtype=np.int32)
    product = indices[:, None] * indices[None, :] % window
    angle = np.float32(2.0 * math.pi / window) * product.astype(np.float32)
    scale = np.float32(math.sqrt(window))
    re = (np.cos(angle) / scale).astype(jnp.bfloat16)
    im = (np.sin(angle) / scale).astype(jnp.bfloat16)
    a = np.block([[re, -im], [im, re]])
    b = np.block([[re, im], [-im, re]])
    return a, b


def propagator(window):
    radius = squared_radius(window)
    inside = (np.float32(9.0) * radius < window * window).astype(np.float32)
    phase_angle = np.float32(-PROPAGATION_COEF * (65536.0 / (window * window))) * radius
    return np.stack([inside * np.cos(phase_angle), inside * np.sin(phase_angle)], 0)


def start_spectrum(window):
    radius = squared_radius(window)
    inside = (np.float32(16.0) * radius < window * window).astype(np.float32)
    norm_scale = np.float32(window) / np.sqrt(np.sum(inside, dtype=np.float32))
    phase_angle = np.float32(-(DEFOCUS_COEF / window)) * radius
    spectrum = np.concatenate(
        [inside * norm_scale * np.cos(phase_angle), inside * norm_scale * np.sin(phase_angle)], 0
    )
    return spectrum.astype(jnp.bfloat16)


def atom_fields(positions, species, slab, species_amp, species_spread, layers):
    species_match = (
        species[None, :] == jnp.arange(species_amp.shape[0], dtype=jnp.int32)[:, None]
    ).astype(species_amp.dtype)
    amplitude = jnp.sum(species_match * species_amp[:, None], 0)
    spread = jnp.sum(species_match * species_spread[:, None], 0)
    inverse = 0.5 / (spread * spread)
    slab_match = (slab[None, :] == jnp.arange(layers, dtype=jnp.int32)[:, None]).astype(
        amplitude.dtype
    )
    return jnp.concatenate([positions, inverse[None, :], slab_match * amplitude[None, :]], 0)


def pick_rows(fields, pick_list):
    valid_mask = (pick_list >= 0).astype(fields.dtype)
    safe_index = jnp.maximum(pick_list, 0)
    gathered = fields[:, safe_index]
    return jnp.concatenate([gathered[:3], gathered[3:] * valid_mask[None]], 0)


def wrap(value, period):
    return value - period * jnp.floor(value * (1.0 / period))


def sincos(v):
    q = jnp.floor(v * 0.6366197723675814 + 0.5)
    r = v - q * 1.5703125
    r = r - q * 4.837512969970703125e-4
    r = r - q * 7.549789954891882e-8
    z = r * r
    s = r + r * z * (-1.6666654611e-1 + z * (8.3321608736e-3 + z * -1.9515295891e-4))
    c = 1.0 - 0.5 * z + z * z * (4.166664568298827e-2 + z * (-1.388731625493765e-3 + z * 2.443315711809948e-5))
    n = q.astype(jnp.int32)
    swap = (n & 1) == 1
    sin_v = jnp.where(swap, c, s)
    cos_v = jnp.where(swap, s, c)
    sin_v = jnp.where((n & 2) == 2, -sin_v, sin_v)
    cos_v = jnp.where(((n + 1) & 2) == 2, -cos_v, cos_v)
    return sin_v, cos_v


def slices_kernel(*refs, field_x, carried, cap, final):
    (pos_ref, owner_ref, table_ref, pk_ref, a_ref, b_ref, prop_ref, last_ref,
     out_ref, wave_ref, pot_ref) = refs
    batch = wave_ref.shape[0]
    w = prop_ref.shape[-1]
    layers = pot_ref.shape[-1] // w
    species_count = table_ref.shape[1]
    hop = pl.program_id(0)
    layer = pl.program_id(1)
    f32, bf16 = jnp.float32, jnp.bfloat16

    def dot(a, b):
        return jnp.dot(a, b, preferred_element_type=f32)

    @pl.when((hop == 0) & (layer == 0))
    def _():
        if carried:
            wave_ref[...] = last_ref[...]
        else:
            rows = dot(a_ref[...], last_ref[...]).astype(bf16)
            rows = jnp.concatenate([rows[:w], rows[w:]], 1)
            start = dot(rows, b_ref[...]).astype(bf16)
            for p in range(batch):
                wave_ref[p] = start

    @pl.when(layer == 0)
    def _():
        entry = owner_ref[0]
        blocks = []
        for slot in range(3):
            raw = pk_ref[0, slot, 0:4, :]
            listed = pk_ref[0, slot, pl.ds(4 + entry, 1), :][:, :cap]
            species = raw[2:3]
            slab = raw[3:4]
            amplitude = jnp.zeros_like(species)
            inverse = jnp.zeros_like(species)
            for k in range(species_count):
                match = species == float(k)
                amplitude = jnp.where(match, table_ref[0, k], amplitude)
                inverse = jnp.where(match, table_ref[1, k], inverse)
            zero = jnp.zeros_like(species)
            per_layer = [jnp.where(slab == float(l), amplitude, zero) for l in range(layers)]
            fields = jnp.concatenate(
                [raw[0:2], inverse] + per_layer + [zero] * (8 - 3 - layers), 0
            )
            atoms = fields.shape[1]
            safe = jnp.maximum(listed, 0.0).astype(jnp.int32)
            onehot = (lax.broadcasted_iota(jnp.int32, (atoms, cap), 0) == safe).astype(f32)
            picked = jnp.dot(
                fields, onehot, preferred_element_type=f32, precision=lax.Precision.HIGHEST
            )
            valid = (listed >= 0.0).astype(f32)
            keep = lax.broadcasted_iota(jnp.int32, (8, 1), 0) < 3
            picked = jnp.where(keep, picked, picked * valid)
            blocks.append(picked)
        rows = jnp.concatenate(blocks, 1)
        cols = rows.T
        atom_x = rows[0:1]
        inverse_row = rows[2:3]
        atom_y = cols[:, 1:2]
        inverse_col = cols[:, 2:3]
        pixel_col = lax.broadcasted_iota(jnp.int32, (w, 1), 0).astype(f32)
        pixel_row = lax.broadcasted_iota(jnp.int32, (1, w), 1).astype(f32)
        for p in range(batch):
            shift_x = pos_ref[p, 0].astype(f32)
            shift_y = pos_ref[p, 1].astype(f32)
            dist_x = wrap(atom_x - shift_x - pixel_col + 0.5 * field_x, field_x) - 0.5 * field_x
            across = jnp.exp(-dist_x * dist_x * inverse_row).astype(bf16)
            dist_y = wrap(atom_y - shift_y - pixel_row + 0.5 * w, w) - 0.5 * w
            along = jnp.exp(-dist_y * dist_y * inverse_col)
            weighted = jnp.concatenate(
                [(cols[:, 3 + l : 4 + l] * along).astype(bf16) for l in range(layers)], 1
            )
            pot_ref[p] = dot(across, weighted)

    pr = prop_ref[0]
    pi = prop_ref[1]
    column = pl.ds(pl.multiple_of(layer * w, w), w)
    for p in range(batch):
        psi = wave_ref[p]
        wr = psi[:, :w].astype(f32)
        wi = psi[:, w:].astype(f32)
        v = pot_ref[p, :, column]
        sv, cv = sincos(v)
        tr = (wr * cv - wi * sv).astype(bf16)
        ti = (wr * sv + wi * cv).astype(bf16)
        rw = dot(jnp.concatenate([tr, ti], 1), a_ref[...]).astype(bf16)
        sp = dot(b_ref[...], jnp.concatenate([rw[:, :w], rw[:, w:]], 0))
        sr = sp[:w]
        si = sp[w:]
        spb = jnp.concatenate(
            [(sr * pr - si * pi).astype(bf16), (sr * pi + si * pr).astype(bf16)], 0
        )
        br = dot(a_ref[...], spb).astype(bf16)
        psi = dot(jnp.concatenate([br[:w], br[w:]], 1), b_ref[...]).astype(bf16)
        wave_ref[p] = psi

    @pl.when((hop == pl.num_programs(0) - 1) & (layer == pl.num_programs(1) - 1))
    def _():
        if final:
            for p in range(batch):
                out_ref[p, :, 0, :] = wave_ref[p, :, :w]
                out_ref[p, :, 1, :] = wave_ref[p, :, w:]
        else:
            out_ref[...] = wave_ref[...]


def run_slices(probe_pos, entry, table, packs, window, layers, field_x, cap, wave=None, final=False):
    batch = probe_pos.shape[0]
    hops = packs.shape[0]
    w = window
    a, b = dft_blocks(w)
    prop = propagator(w)
    full = lambda shape: pl.BlockSpec(shape, lambda h, l, *_: (0,) * len(shape))
    carried = wave is not None
    out_shape = (batch, w, 2, w) if final else (batch, w, 2 * w)
    last = wave if carried else jnp.asarray(start_spectrum(w))
    atoms = 3 * cap
    steps = batch * hops * layers
    flops = steps * 4 * 2 * w * (2 * w) * (2 * w) + batch * hops * 2 * w * atoms * layers * w
    return pl.pallas_call(
        functools.partial(slices_kernel, field_x=float(field_x), carried=carried, cap=cap, final=final),
        out_shape=jax.ShapeDtypeStruct(out_shape, jnp.bfloat16),
        grid_spec=pltpu.PrefetchScalarGridSpec(
            num_scalar_prefetch=2,
            grid=(hops, layers),
            in_specs=[
                pl.BlockSpec(memory_space=pltpu.SMEM),
                pl.BlockSpec((1,) + packs.shape[1:], lambda h, l, *_: (h, 0, 0, 0)),
                full((2 * w, 2 * w)),
                full((2 * w, 2 * w)),
                full((2, w, w)),
                full(last.shape),
            ],
            out_specs=full(out_shape),
            scratch_shapes=[
                pltpu.VMEM((batch, w, 2 * w), jnp.bfloat16),
                pltpu.VMEM((batch, w, layers * w), jnp.float32),
            ],
        ),
        compiler_params=pltpu.CompilerParams(
            dimension_semantics=("arbitrary", "arbitrary"),
        ),
        cost_estimate=pl.CostEstimate(
            flops=flops,
            transcendentals=steps * 2 * w * w + batch * hops * 2 * atoms * w,
            bytes_accessed=2 * (2 * w) ** 2 * 2 + 3 * w * w * 4 + batch * w * w * 4,
        ),
    )(probe_pos, entry, table, packs, jnp.asarray(a), jnp.asarray(b), jnp.asarray(prop), last)


def shards(atom_xy, atom_species, atom_slab, species_amp, species_spread, margin, probe_pos):
    layers = SL_DEV
    window = W
    atoms = atom_xy.shape[-1]
    cap = margin.shape[-1]
    n_lat = lax.axis_size("lat")
    owners = lax.axis_size("slc")
    field_x = n_lat * atoms * (2 * window // cap)
    f32 = jnp.float32
    raw = jnp.concatenate(
        [atom_xy[0, 0], atom_species[0, 0][None].astype(f32), atom_slab[0, 0][None].astype(f32)], 0
    )
    marg = jnp.transpose(margin[0, 0, :, 0], (1, 0, 2)).astype(f32)
    marg = jnp.pad(marg, ((0, 0), (0, 0), (0, atoms - cap)), constant_values=-1.0)
    packs = jnp.concatenate([jnp.broadcast_to(raw[None], (3,) + raw.shape), marg], 1)
    from_left = lax.ppermute(packs[2], "lat", [(i, (i + 1) % n_lat) for i in range(n_lat)])
    from_right = lax.ppermute(packs[0], "lat", [((i + 1) % n_lat, i) for i in range(n_lat)])
    local = jnp.stack([from_left, packs[1], from_right], 0)[None]
    me = lax.axis_index("slc")
    entry = jnp.reshape(me, (1,)).astype(jnp.int32)
    later = [
        lax.ppermute(local, "slc", [(i, (i - hop) % owners) for i in range(owners)])
        for hop in range(1, owners)
    ]
    table = jnp.stack([species_amp, 0.5 / (species_spread * species_spread)], 0)
    batch = probe_pos.shape[0]
    wave = run_slices(probe_pos, entry, table, local, window, layers, field_x, cap, final=not later)
    if later:
        wave = run_slices(
            probe_pos, entry, table, jnp.concatenate(later, 0), window, layers, field_x, cap, wave,
            final=True,
        )
    return wave


def solution(mesh):
    in_specs = (
        P(("groups", "lat"), "slc", None, None),
        P(("groups", "lat"), "slc", None),
        P(("groups", "lat"), "slc", None),
        P(),
        P(),
        P(("groups", "lat"), "slc", None, "rep", None, None),
        P(("groups", "lat", "slc", "rep"), None),
    )
    out_specs = P(("groups", "lat", "slc", "rep"), None, None, None)
    return jax.shard_map(shards, mesh=mesh, in_specs=in_specs, out_specs=out_specs, check_vma=False)
```

```python
import functools
import math

import jax
import numpy as np
import jax.numpy as jnp
from jax import lax
from jax.experimental import pallas as pl
from jax.experimental.pallas import tpu as pltpu
from jax.sharding import PartitionSpec as P

W = 256
SL_DEV = 2


PROPAGATION_COEF = 0.001
DEFOCUS_COEF = 4.19


def centered_frequency(window):
    indices = np.arange(window, dtype=np.int32)
    return np.where(indices < window // 2, indices, indices - window).astype(np.float32)


def squared_radius(window):
    frequency = centered_frequency(window)
    return frequency[:, None] * frequency[:, None] + frequency[None, :] * frequency[None, :]


def dft_blocks(window):
    indices = np.arange(window, dtype=np.int32)
    product = indices[:, None] * indices[None, :] % window
    angle = np.float32(2.0 * math.pi / window) * product.astype(np.float32)
    scale = np.float32(math.sqrt(window))
    re = (np.cos(angle) / scale).astype(jnp.bfloat16)
    im = (np.sin(angle) / scale).astype(jnp.bfloat16)
    a = np.block([[re, -im], [im, re]])
    b = np.block([[re, im], [-im, re]])
    return a, b


def propagator(window):
    radius = squared_radius(window)
    inside = (np.float32(9.0) * radius < window * window).astype(np.float32)
    phase_angle = np.float32(-PROPAGATION_COEF * (65536.0 / (window * window))) * radius
    return np.stack([inside * np.cos(phase_angle), inside * np.sin(phase_angle)], 0)


def start_spectrum(window):
    radius = squared_radius(window)
    inside = (np.float32(16.0) * radius < window * window).astype(np.float32)
    norm_scale = np.float32(window) / np.sqrt(np.sum(inside, dtype=np.float32))
    phase_angle = np.float32(-(DEFOCUS_COEF / window)) * radius
    spectrum = np.concatenate(
        [inside * norm_scale * np.cos(phase_angle), inside * norm_scale * np.sin(phase_angle)], 0
    )
    return spectrum.astype(jnp.bfloat16)


def atom_fields(positions, species, slab, species_amp, species_spread, layers):
    species_match = (
        species[None, :] == jnp.arange(species_amp.shape[0], dtype=jnp.int32)[:, None]
    ).astype(species_amp.dtype)
    amplitude = jnp.sum(species_match * species_amp[:, None], 0)
    spread = jnp.sum(species_match * species_spread[:, None], 0)
    inverse = 0.5 / (spread * spread)
    slab_match = (slab[None, :] == jnp.arange(layers, dtype=jnp.int32)[:, None]).astype(
        amplitude.dtype
    )
    return jnp.concatenate([positions, inverse[None, :], slab_match * amplitude[None, :]], 0)


def pick_rows(fields, pick_list):
    valid_mask = (pick_list >= 0).astype(fields.dtype)
    safe_index = jnp.maximum(pick_list, 0)
    gathered = fields[:, safe_index]
    return jnp.concatenate([gathered[:3], gathered[3:] * valid_mask[None]], 0)


def wrap(value, period):
    return value - period * jnp.floor(value * (1.0 / period))


def sincos(v):
    q = jnp.floor(v * 0.6366197723675814 + 0.5)
    r = v - q * 1.5703125
    r = r - q * 4.837512969970703125e-4
    r = r - q * 7.549789954891882e-8
    z = r * r
    s = r + r * z * (-1.6666654611e-1 + z * (8.3321608736e-3 + z * -1.9515295891e-4))
    c = 1.0 - 0.5 * z + z * z * (4.166664568298827e-2 + z * (-1.388731625493765e-3 + z * 2.443315711809948e-5))
    n = q.astype(jnp.int32)
    swap = (n & 1) == 1
    sin_v = jnp.where(swap, c, s)
    cos_v = jnp.where(swap, s, c)
    sin_v = jnp.where((n & 2) == 2, -sin_v, sin_v)
    cos_v = jnp.where(((n + 1) & 2) == 2, -cos_v, cos_v)
    return sin_v, cos_v


def slices_kernel(*refs, field_x, carried, cap, final):
    (pos_ref, owner_ref, table_ref, pk_ref, a_hbm, b_hbm, prop_hbm, last_hbm,
     out_ref, wave_ref, pot_ref, a_ref, b_ref, prop_ref, last_ref, sems) = refs
    batch = wave_ref.shape[0]
    w = prop_ref.shape[-1]
    layers = pot_ref.shape[-1] // w
    species_count = table_ref.shape[1]
    hop = pl.program_id(0)
    layer = pl.program_id(1)
    f32, bf16 = jnp.float32, jnp.bfloat16

    def dot(a, b):
        return jnp.dot(a, b, preferred_element_type=f32)

    first = (hop == 0) & (layer == 0)
    copies = [
        pltpu.make_async_copy(src, dst, sems.at[k])
        for k, (src, dst) in enumerate(
            [(a_hbm, a_ref), (b_hbm, b_ref), (prop_hbm, prop_ref), (last_hbm, last_ref)]
        )
    ]

    @pl.when(first)
    def _():
        for copy in copies:
            copy.start()

    @pl.when(layer == 0)
    def _():
        entry = owner_ref[0]
        blocks = []
        for slot in range(3):
            raw = pk_ref[0, slot, 0:4, :]
            listed = pk_ref[0, slot, pl.ds(4 + entry, 1), :][:, :cap]
            species = raw[2:3]
            slab = raw[3:4]
            amplitude = jnp.zeros_like(species)
            inverse = jnp.zeros_like(species)
            for k in range(species_count):
                match = species == float(k)
                amplitude = jnp.where(match, table_ref[0, k], amplitude)
                inverse = jnp.where(match, table_ref[1, k], inverse)
            zero = jnp.zeros_like(species)
            per_layer = [jnp.where(slab == float(l), amplitude, zero) for l in range(layers)]
            fields = jnp.concatenate(
                [raw[0:2], inverse] + per_layer + [zero] * (8 - 3 - layers), 0
            )
            atoms = fields.shape[1]
            safe = jnp.maximum(listed, 0.0).astype(jnp.int32)
            onehot = (lax.broadcasted_iota(jnp.int32, (atoms, cap), 0) == safe).astype(f32)
            picked = jnp.dot(
                fields, onehot, preferred_element_type=f32, precision=lax.Precision.HIGHEST
            )
            valid = (listed >= 0.0).astype(f32)
            keep = lax.broadcasted_iota(jnp.int32, (8, 1), 0) < 3
            picked = jnp.where(keep, picked, picked * valid)
            blocks.append(picked)
        rows = jnp.concatenate(blocks, 1)
        cols = rows.T
        atom_x = rows[0:1]
        inverse_row = rows[2:3]
        atom_y = cols[:, 1:2]
        inverse_col = cols[:, 2:3]
        pixel_col = lax.broadcasted_iota(jnp.int32, (w, 1), 0).astype(f32)
        pixel_row = lax.broadcasted_iota(jnp.int32, (1, w), 1).astype(f32)
        for p in range(batch):
            shift_x = pos_ref[p, 0].astype(f32)
            shift_y = pos_ref[p, 1].astype(f32)
            dist_x = wrap(atom_x - shift_x - pixel_col + 0.5 * field_x, field_x) - 0.5 * field_x
            across = jnp.exp(-dist_x * dist_x * inverse_row).astype(bf16)
            dist_y = wrap(atom_y - shift_y - pixel_row + 0.5 * w, w) - 0.5 * w
            along = jnp.exp(-dist_y * dist_y * inverse_col)
            weighted = jnp.concatenate(
                [(cols[:, 3 + l : 4 + l] * along).astype(bf16) for l in range(layers)], 1
            )
            pot_ref[p] = dot(across, weighted)

    @pl.when(first)
    def _():
        for copy in copies:
            copy.wait()
        if carried:
            wave_ref[...] = last_ref[...]
        else:
            rows = dot(a_ref[...], last_ref[...]).astype(bf16)
            rows = jnp.concatenate([rows[:w], rows[w:]], 1)
            start = dot(rows, b_ref[...]).astype(bf16)
            for p in range(batch):
                wave_ref[p] = start

    pr = prop_ref[0]
    pi = prop_ref[1]
    column = pl.ds(pl.multiple_of(layer * w, w), w)
    for p in range(batch):
        psi = wave_ref[p]
        wr = psi[:, :w].astype(f32)
        wi = psi[:, w:].astype(f32)
        v = pot_ref[p, :, column]
        sv, cv = sincos(v)
        tr = (wr * cv - wi * sv).astype(bf16)
        ti = (wr * sv + wi * cv).astype(bf16)
        rw = dot(jnp.concatenate([tr, ti], 1), a_ref[...]).astype(bf16)
        sp = dot(b_ref[...], jnp.concatenate([rw[:, :w], rw[:, w:]], 0))
        sr = sp[:w]
        si = sp[w:]
        spb = jnp.concatenate(
            [(sr * pr - si * pi).astype(bf16), (sr * pi + si * pr).astype(bf16)], 0
        )
        br = dot(a_ref[...], spb).astype(bf16)
        psi = dot(jnp.concatenate([br[:w], br[w:]], 1), b_ref[...]).astype(bf16)
        wave_ref[p] = psi

    @pl.when((hop == pl.num_programs(0) - 1) & (layer == pl.num_programs(1) - 1))
    def _():
        if final:
            for p in range(batch):
                out_ref[p, :, 0, :] = wave_ref[p, :, :w]
                out_ref[p, :, 1, :] = wave_ref[p, :, w:]
        else:
            out_ref[...] = wave_ref[...]


def run_slices(probe_pos, entry, table, packs, window, layers, field_x, cap, wave=None, final=False):
    batch = probe_pos.shape[0]
    hops = packs.shape[0]
    w = window
    a, b = dft_blocks(w)
    prop = propagator(w)
    full = lambda shape: pl.BlockSpec(shape, lambda h, l, *_: (0,) * len(shape))
    carried = wave is not None
    out_shape = (batch, w, 2, w) if final else (batch, w, 2 * w)
    last = wave if carried else jnp.asarray(start_spectrum(w))
    atoms = 3 * cap
    steps = batch * hops * layers
    flops = steps * 4 * 2 * w * (2 * w) * (2 * w) + batch * hops * 2 * w * atoms * layers * w
    return pl.pallas_call(
        functools.partial(slices_kernel, field_x=float(field_x), carried=carried, cap=cap, final=final),
        out_shape=jax.ShapeDtypeStruct(out_shape, jnp.bfloat16),
        grid_spec=pltpu.PrefetchScalarGridSpec(
            num_scalar_prefetch=2,
            grid=(hops, layers),
            in_specs=[
                pl.BlockSpec(memory_space=pltpu.SMEM),
                pl.BlockSpec((1,) + packs.shape[1:], lambda h, l, *_: (h, 0, 0, 0)),
                pl.BlockSpec(memory_space=pl.ANY),
                pl.BlockSpec(memory_space=pl.ANY),
                pl.BlockSpec(memory_space=pl.ANY),
                pl.BlockSpec(memory_space=pl.ANY),
            ],
            out_specs=full(out_shape),
            scratch_shapes=[
                pltpu.VMEM((batch, w, 2 * w), jnp.bfloat16),
                pltpu.VMEM((batch, w, layers * w), jnp.float32),
                pltpu.VMEM(a.shape, jnp.bfloat16),
                pltpu.VMEM(b.shape, jnp.bfloat16),
                pltpu.VMEM(prop.shape, jnp.float32),
                pltpu.VMEM(last.shape, jnp.bfloat16),
                pltpu.SemaphoreType.DMA((4,)),
            ],
        ),
        compiler_params=pltpu.CompilerParams(
            dimension_semantics=("arbitrary", "arbitrary"),
        ),
        cost_estimate=pl.CostEstimate(
            flops=flops,
            transcendentals=steps * 2 * w * w + batch * hops * 2 * atoms * w,
            bytes_accessed=2 * (2 * w) ** 2 * 2 + 3 * w * w * 4 + batch * w * w * 4,
        ),
    )(probe_pos, entry, table, packs, jnp.asarray(a), jnp.asarray(b), jnp.asarray(prop), last)


def shards(atom_xy, atom_species, atom_slab, species_amp, species_spread, margin, probe_pos):
    layers = SL_DEV
    window = W
    atoms = atom_xy.shape[-1]
    cap = margin.shape[-1]
    n_lat = lax.axis_size("lat")
    owners = lax.axis_size("slc")
    field_x = n_lat * atoms * (2 * window // cap)
    f32 = jnp.float32
    raw = jnp.concatenate(
        [atom_xy[0, 0], atom_species[0, 0][None].astype(f32), atom_slab[0, 0][None].astype(f32)], 0
    )
    marg = jnp.transpose(margin[0, 0, :, 0], (1, 0, 2)).astype(f32)
    marg = jnp.pad(marg, ((0, 0), (0, 0), (0, atoms - cap)), constant_values=-1.0)
    packs = jnp.concatenate([jnp.broadcast_to(raw[None], (3,) + raw.shape), marg], 1)
    from_left = lax.ppermute(packs[2], "lat", [(i, (i + 1) % n_lat) for i in range(n_lat)])
    from_right = lax.ppermute(packs[0], "lat", [((i + 1) % n_lat, i) for i in range(n_lat)])
    local = jnp.stack([from_left, packs[1], from_right], 0)[None]
    me = lax.axis_index("slc")
    entry = jnp.reshape(me, (1,)).astype(jnp.int32)
    later = [
        lax.ppermute(local, "slc", [(i, (i - hop) % owners) for i in range(owners)])
        for hop in range(1, owners)
    ]
    table = jnp.stack([species_amp, 0.5 / (species_spread * species_spread)], 0)
    batch = probe_pos.shape[0]
    wave = run_slices(probe_pos, entry, table, local, window, layers, field_x, cap, final=not later)
    if later:
        wave = run_slices(
            probe_pos, entry, table, jnp.concatenate(later, 0), window, layers, field_x, cap, wave,
            final=True,
        )
    return wave


def solution(mesh):
    in_specs = (
        P(("groups", "lat"), "slc", None, None),
        P(("groups", "lat"), "slc", None),
        P(("groups", "lat"), "slc", None),
        P(),
        P(),
        P(("groups", "lat"), "slc", None, "rep", None, None),
        P(("groups", "lat", "slc", "rep"), None),
    )
    out_specs = P(("groups", "lat", "slc", "rep"), None, None, None)
    return jax.shard_map(shards, mesh=mesh, in_specs=in_specs, out_specs=out_specs, check_vma=False)
```

```python
import functools
import math

import jax
import numpy as np
import jax.numpy as jnp
from jax import lax
from jax.experimental import pallas as pl
from jax.experimental.pallas import tpu as pltpu
from jax.sharding import PartitionSpec as P

W = 256
SL_DEV = 2


PROPAGATION_COEF = 0.001
DEFOCUS_COEF = 4.19


def centered_frequency(window):
    indices = np.arange(window, dtype=np.int32)
    return np.where(indices < window // 2, indices, indices - window).astype(np.float32)


def squared_radius(window):
    frequency = centered_frequency(window)
    return frequency[:, None] * frequency[:, None] + frequency[None, :] * frequency[None, :]


def dft_blocks(window):
    indices = np.arange(window, dtype=np.int32)
    product = indices[:, None] * indices[None, :] % window
    angle = np.float32(2.0 * math.pi / window) * product.astype(np.float32)
    scale = np.float32(math.sqrt(window))
    re = (np.cos(angle) / scale).astype(jnp.bfloat16)
    im = (np.sin(angle) / scale).astype(jnp.bfloat16)
    a = np.block([[re, -im], [im, re]])
    b = np.block([[re, im], [-im, re]])
    return a, b


def propagator(window):
    radius = squared_radius(window)
    inside = (np.float32(9.0) * radius < window * window).astype(np.float32)
    phase_angle = np.float32(-PROPAGATION_COEF * (65536.0 / (window * window))) * radius
    return np.stack([inside * np.cos(phase_angle), inside * np.sin(phase_angle)], 0)


def start_spectrum(window):
    radius = squared_radius(window)
    inside = (np.float32(16.0) * radius < window * window).astype(np.float32)
    norm_scale = np.float32(window) / np.sqrt(np.sum(inside, dtype=np.float32))
    phase_angle = np.float32(-(DEFOCUS_COEF / window)) * radius
    spectrum = np.concatenate(
        [inside * norm_scale * np.cos(phase_angle), inside * norm_scale * np.sin(phase_angle)], 0
    )
    return spectrum.astype(jnp.bfloat16)


def atom_fields(positions, species, slab, species_amp, species_spread, layers):
    species_match = (
        species[None, :] == jnp.arange(species_amp.shape[0], dtype=jnp.int32)[:, None]
    ).astype(species_amp.dtype)
    amplitude = jnp.sum(species_match * species_amp[:, None], 0)
    spread = jnp.sum(species_match * species_spread[:, None], 0)
    inverse = 0.5 / (spread * spread)
    slab_match = (slab[None, :] == jnp.arange(layers, dtype=jnp.int32)[:, None]).astype(
        amplitude.dtype
    )
    return jnp.concatenate([positions, inverse[None, :], slab_match * amplitude[None, :]], 0)


def pick_rows(fields, pick_list):
    valid_mask = (pick_list >= 0).astype(fields.dtype)
    safe_index = jnp.maximum(pick_list, 0)
    gathered = fields[:, safe_index]
    return jnp.concatenate([gathered[:3], gathered[3:] * valid_mask[None]], 0)


def wrap(value, period):
    return value - period * jnp.floor(value * (1.0 / period))


def sincos(v):
    q = jnp.floor(v * 0.6366197723675814 + 0.5)
    r = v - q * 1.5703125
    r = r - q * 4.837512969970703125e-4
    r = r - q * 7.549789954891882e-8
    z = r * r
    s = r + r * z * (-1.6666654611e-1 + z * (8.3321608736e-3 + z * -1.9515295891e-4))
    c = 1.0 - 0.5 * z + z * z * (4.166664568298827e-2 + z * (-1.388731625493765e-3 + z * 2.443315711809948e-5))
    n = q.astype(jnp.int32)
    swap = (n & 1) == 1
    sin_v = jnp.where(swap, c, s)
    cos_v = jnp.where(swap, s, c)
    sin_v = jnp.where((n & 2) == 2, -sin_v, sin_v)
    cos_v = jnp.where(((n + 1) & 2) == 2, -cos_v, cos_v)
    return sin_v, cos_v


def slices_kernel(*refs, field_x, carried, cap, final):
    (pos_ref, owner_ref, table_ref, pk_ref, a_hbm, b_hbm, prop_hbm, last_hbm,
     out_ref, wave_ref, pot_ref, a_ref, b_ref, prop_ref, last_ref, sems) = refs
    batch = wave_ref.shape[0]
    w = prop_ref.shape[-1]
    layers = pot_ref.shape[-1] // w
    species_count = table_ref.shape[1]
    hop = pl.program_id(0)
    layer = pl.program_id(1)
    f32, bf16 = jnp.float32, jnp.bfloat16

    def dot(a, b):
        return jnp.dot(a, b, preferred_element_type=f32)

    first = (hop == 0) & (layer == 0)
    copies = [
        pltpu.make_async_copy(src, dst, sems.at[k])
        for k, (src, dst) in enumerate(
            [(a_hbm, a_ref), (b_hbm, b_ref), (prop_hbm, prop_ref), (last_hbm, last_ref)]
        )
    ]

    @pl.when(first)
    def _():
        for copy in copies:
            copy.start()

    @pl.when(layer == 0)
    def _():
        entry = owner_ref[0]
        blocks = []
        for slot in range(3):
            raw = pk_ref[0, slot, 0:4, :]
            listed = pk_ref[0, slot, pl.ds(4 + entry, 1), :][:, :cap]
            species = raw[2:3]
            slab = raw[3:4]
            amplitude = jnp.zeros_like(species)
            inverse = jnp.zeros_like(species)
            for k in range(species_count):
                match = species == float(k)
                amplitude = jnp.where(match, table_ref[0, k], amplitude)
                inverse = jnp.where(match, table_ref[1, k], inverse)
            zero = jnp.zeros_like(species)
            per_layer = [jnp.where(slab == float(l), amplitude, zero) for l in range(layers)]
            fields = jnp.concatenate(
                [raw[0:2], inverse] + per_layer + [zero] * (8 - 3 - layers), 0
            )
            atoms = fields.shape[1]
            safe = jnp.maximum(listed, 0.0).astype(jnp.int32)
            onehot = (lax.broadcasted_iota(jnp.int32, (atoms, cap), 0) == safe).astype(f32)
            picked = jnp.dot(
                fields, onehot, preferred_element_type=f32, precision=lax.Precision.HIGHEST
            )
            valid = (listed >= 0.0).astype(f32)
            keep = lax.broadcasted_iota(jnp.int32, (8, 1), 0) < 3
            picked = jnp.where(keep, picked, picked * valid)
            blocks.append(picked)
        rows = jnp.concatenate(blocks, 1)
        cols = rows.T
        atom_x = rows[0:1]
        inverse_row = rows[2:3]
        atom_y = cols[:, 1:2]
        inverse_col = cols[:, 2:3]
        pixel_col = lax.broadcasted_iota(jnp.int32, (w, 1), 0).astype(f32)
        pixel_row = lax.broadcasted_iota(jnp.int32, (1, w), 1).astype(f32)
        shift_x = pos_ref[0, 0].astype(f32)
        dist_x = wrap(atom_x - shift_x - pixel_col + 0.5 * field_x, field_x) - 0.5 * field_x
        across = jnp.exp(-dist_x * dist_x * inverse_row).astype(bf16)
        for p in range(batch):
            shift_y = pos_ref[p, 1].astype(f32)
            dist_y = wrap(atom_y - shift_y - pixel_row + 0.5 * w, w) - 0.5 * w
            along = jnp.exp(-dist_y * dist_y * inverse_col)
            weighted = jnp.concatenate(
                [(cols[:, 3 + l : 4 + l] * along).astype(bf16) for l in range(layers)], 1
            )
            pot_ref[p] = dot(across, weighted)

    @pl.when(first)
    def _():
        for copy in copies:
            copy.wait()
        if carried:
            wave_ref[...] = last_ref[...]
        else:
            rows = dot(a_ref[...], last_ref[...]).astype(bf16)
            rows = jnp.concatenate([rows[:w], rows[w:]], 1)
            start = dot(rows, b_ref[...]).astype(bf16)
            for p in range(batch):
                wave_ref[p] = start

    pr = prop_ref[0]
    pi = prop_ref[1]
    column = pl.ds(pl.multiple_of(layer * w, w), w)
    transmitted = []
    for p in range(batch):
        psi = wave_ref[p]
        wr = psi[:, :w].astype(f32)
        wi = psi[:, w:].astype(f32)
        v = pot_ref[p, :, column]
        sv, cv = sincos(v)
        tr = (wr * cv - wi * sv).astype(bf16)
        ti = (wr * sv + wi * cv).astype(bf16)
        transmitted.append(jnp.concatenate([tr, ti], 1))
    rowwise = [dot(t, a_ref[...]).astype(bf16) for t in transmitted]
    spectra = [dot(b_ref[...], jnp.concatenate([rw[:, :w], rw[:, w:]], 0)) for rw in rowwise]
    propagated = []
    for sp in spectra:
        sr = sp[:w]
        si = sp[w:]
        propagated.append(
            jnp.concatenate([(sr * pr - si * pi).astype(bf16), (sr * pi + si * pr).astype(bf16)], 0)
        )
    back = [dot(a_ref[...], spb).astype(bf16) for spb in propagated]
    for p, br in enumerate(back):
        wave_ref[p] = dot(jnp.concatenate([br[:w], br[w:]], 1), b_ref[...]).astype(bf16)

    @pl.when((hop == pl.num_programs(0) - 1) & (layer == pl.num_programs(1) - 1))
    def _():
        if final:
            for p in range(batch):
                out_ref[p, :, 0, :] = wave_ref[p, :, :w]
                out_ref[p, :, 1, :] = wave_ref[p, :, w:]
        else:
            out_ref[...] = wave_ref[...]


def run_slices(probe_pos, entry, table, packs, window, layers, field_x, cap, wave=None, final=False):
    batch = probe_pos.shape[0]
    hops = packs.shape[0]
    w = window
    a, b = dft_blocks(w)
    prop = propagator(w)
    full = lambda shape: pl.BlockSpec(shape, lambda h, l, *_: (0,) * len(shape))
    carried = wave is not None
    out_shape = (batch, w, 2, w) if final else (batch, w, 2 * w)
    last = wave if carried else jnp.asarray(start_spectrum(w))
    atoms = 3 * cap
    steps = batch * hops * layers
    flops = steps * 4 * 2 * w * (2 * w) * (2 * w) + batch * hops * 2 * w * atoms * layers * w
    return pl.pallas_call(
        functools.partial(slices_kernel, field_x=float(field_x), carried=carried, cap=cap, final=final),
        out_shape=jax.ShapeDtypeStruct(out_shape, jnp.bfloat16),
        grid_spec=pltpu.PrefetchScalarGridSpec(
            num_scalar_prefetch=2,
            grid=(hops, layers),
            in_specs=[
                pl.BlockSpec(memory_space=pltpu.SMEM),
                pl.BlockSpec((1,) + packs.shape[1:], lambda h, l, *_: (h, 0, 0, 0)),
                pl.BlockSpec(memory_space=pl.ANY),
                pl.BlockSpec(memory_space=pl.ANY),
                pl.BlockSpec(memory_space=pl.ANY),
                pl.BlockSpec(memory_space=pl.ANY),
            ],
            out_specs=full(out_shape),
            scratch_shapes=[
                pltpu.VMEM((batch, w, 2 * w), jnp.bfloat16),
                pltpu.VMEM((batch, w, layers * w), jnp.float32),
                pltpu.VMEM(a.shape, jnp.bfloat16),
                pltpu.VMEM(b.shape, jnp.bfloat16),
                pltpu.VMEM(prop.shape, jnp.float32),
                pltpu.VMEM(last.shape, jnp.bfloat16),
                pltpu.SemaphoreType.DMA((4,)),
            ],
        ),
        compiler_params=pltpu.CompilerParams(
            dimension_semantics=("arbitrary", "arbitrary"),
        ),
        cost_estimate=pl.CostEstimate(
            flops=flops,
            transcendentals=steps * 2 * w * w + batch * hops * 2 * atoms * w,
            bytes_accessed=2 * (2 * w) ** 2 * 2 + 3 * w * w * 4 + batch * w * w * 4,
        ),
    )(probe_pos, entry, table, packs, jnp.asarray(a), jnp.asarray(b), jnp.asarray(prop), last)


def shards(atom_xy, atom_species, atom_slab, species_amp, species_spread, margin, probe_pos):
    layers = SL_DEV
    window = W
    atoms = atom_xy.shape[-1]
    cap = margin.shape[-1]
    n_lat = lax.axis_size("lat")
    owners = lax.axis_size("slc")
    field_x = n_lat * atoms * (2 * window // cap)
    f32 = jnp.float32
    raw = jnp.concatenate(
        [atom_xy[0, 0], atom_species[0, 0][None].astype(f32), atom_slab[0, 0][None].astype(f32)], 0
    )
    marg = jnp.transpose(margin[0, 0, :, 0], (1, 0, 2)).astype(f32)
    marg = jnp.pad(marg, ((0, 0), (0, 0), (0, atoms - cap)), constant_values=-1.0)
    packs = jnp.concatenate([jnp.broadcast_to(raw[None], (3,) + raw.shape), marg], 1)
    from_left = lax.ppermute(packs[2], "lat", [(i, (i + 1) % n_lat) for i in range(n_lat)])
    from_right = lax.ppermute(packs[0], "lat", [((i + 1) % n_lat, i) for i in range(n_lat)])
    local = jnp.stack([from_left, packs[1], from_right], 0)[None]
    me = lax.axis_index("slc")
    entry = jnp.reshape(me, (1,)).astype(jnp.int32)
    later = [
        lax.ppermute(local, "slc", [(i, (i - hop) % owners) for i in range(owners)])
        for hop in range(1, owners)
    ]
    table = jnp.stack([species_amp, 0.5 / (species_spread * species_spread)], 0)
    batch = probe_pos.shape[0]
    wave = run_slices(probe_pos, entry, table, local, window, layers, field_x, cap, final=not later)
    if later:
        wave = run_slices(
            probe_pos, entry, table, jnp.concatenate(later, 0), window, layers, field_x, cap, wave,
            final=True,
        )
    return wave


def solution(mesh):
    in_specs = (
        P(("groups", "lat"), "slc", None, None),
        P(("groups", "lat"), "slc", None),
        P(("groups", "lat"), "slc", None),
        P(),
        P(),
        P(("groups", "lat"), "slc", None, "rep", None, None),
        P(("groups", "lat", "slc", "rep"), None),
    )
    out_specs = P(("groups", "lat", "slc", "rep"), None, None, None)
    return jax.shard_map(shards, mesh=mesh, in_specs=in_specs, out_specs=out_specs, check_vma=False)
```

```python
import functools
import math

import jax
import numpy as np
import jax.numpy as jnp
from jax import lax
from jax.experimental import pallas as pl
from jax.experimental.pallas import tpu as pltpu
from jax.sharding import PartitionSpec as P

W = 256
SL_DEV = 2


PROPAGATION_COEF = 0.001
DEFOCUS_COEF = 4.19


def centered_frequency(window):
    indices = np.arange(window, dtype=np.int32)
    return np.where(indices < window // 2, indices, indices - window).astype(np.float32)


def squared_radius(window):
    frequency = centered_frequency(window)
    return frequency[:, None] * frequency[:, None] + frequency[None, :] * frequency[None, :]


def dft_blocks(window):
    indices = np.arange(window, dtype=np.int32)
    product = indices[:, None] * indices[None, :] % window
    angle = np.float32(2.0 * math.pi / window) * product.astype(np.float32)
    scale = np.float32(math.sqrt(window))
    re = (np.cos(angle) / scale).astype(jnp.bfloat16)
    im = (np.sin(angle) / scale).astype(jnp.bfloat16)
    a = np.block([[re, -im], [im, re]])
    b = np.block([[re, im], [-im, re]])
    return a, b


def propagator(window):
    radius = squared_radius(window)
    inside = (np.float32(9.0) * radius < window * window).astype(np.float32)
    phase_angle = np.float32(-PROPAGATION_COEF * (65536.0 / (window * window))) * radius
    return np.stack([inside * np.cos(phase_angle), inside * np.sin(phase_angle)], 0)


def start_spectrum(window):
    radius = squared_radius(window)
    inside = (np.float32(16.0) * radius < window * window).astype(np.float32)
    norm_scale = np.float32(window) / np.sqrt(np.sum(inside, dtype=np.float32))
    phase_angle = np.float32(-(DEFOCUS_COEF / window)) * radius
    spectrum = np.concatenate(
        [inside * norm_scale * np.cos(phase_angle), inside * norm_scale * np.sin(phase_angle)], 0
    )
    return spectrum.astype(jnp.bfloat16)


def atom_fields(positions, species, slab, species_amp, species_spread, layers):
    species_match = (
        species[None, :] == jnp.arange(species_amp.shape[0], dtype=jnp.int32)[:, None]
    ).astype(species_amp.dtype)
    amplitude = jnp.sum(species_match * species_amp[:, None], 0)
    spread = jnp.sum(species_match * species_spread[:, None], 0)
    inverse = 0.5 / (spread * spread)
    slab_match = (slab[None, :] == jnp.arange(layers, dtype=jnp.int32)[:, None]).astype(
        amplitude.dtype
    )
    return jnp.concatenate([positions, inverse[None, :], slab_match * amplitude[None, :]], 0)


def pick_rows(fields, pick_list):
    valid_mask = (pick_list >= 0).astype(fields.dtype)
    safe_index = jnp.maximum(pick_list, 0)
    gathered = fields[:, safe_index]
    return jnp.concatenate([gathered[:3], gathered[3:] * valid_mask[None]], 0)


def wrap(value, period):
    return value - period * jnp.floor(value * (1.0 / period))


def sincos(v):
    q = jnp.floor(v * 0.6366197723675814 + 0.5)
    r = v - q * 1.5703125
    r = r - q * 4.837512969970703125e-4
    r = r - q * 7.549789954891882e-8
    z = r * r
    s = r + r * z * (-1.6666654611e-1 + z * (8.3321608736e-3 + z * -1.9515295891e-4))
    c = 1.0 - 0.5 * z + z * z * (4.166664568298827e-2 + z * (-1.388731625493765e-3 + z * 2.443315711809948e-5))
    n = q.astype(jnp.int32)
    swap = (n & 1) == 1
    sin_v = jnp.where(swap, c, s)
    cos_v = jnp.where(swap, s, c)
    sin_v = jnp.where((n & 2) == 2, -sin_v, sin_v)
    cos_v = jnp.where(((n + 1) & 2) == 2, -cos_v, cos_v)
    return sin_v, cos_v


def slices_kernel(*refs, field_x, carried, cap, final):
    (pos_ref, owner_ref, table_ref, pk_ref, a_hbm, b_hbm, prop_hbm, last_hbm,
     out_ref, wave_ref, pot_ref, a_ref, b_ref, prop_ref, last_ref, sems) = refs
    batch = wave_ref.shape[0]
    w = prop_ref.shape[-1]
    layers = pot_ref.shape[-1] // w
    species_count = table_ref.shape[1]
    hop = pl.program_id(0)
    layer = pl.program_id(1)
    f32, bf16 = jnp.float32, jnp.bfloat16

    def dot(a, b):
        return jnp.dot(a, b, preferred_element_type=f32)

    first = (hop == 0) & (layer == 0)
    copies = [
        pltpu.make_async_copy(src, dst, sems.at[k])
        for k, (src, dst) in enumerate(
            [(a_hbm, a_ref), (b_hbm, b_ref), (prop_hbm, prop_ref), (last_hbm, last_ref)]
        )
    ]

    @pl.when(first)
    def _():
        for copy in copies:
            copy.start()

    @pl.when(layer == 0)
    def _():
        entry = owner_ref[0]
        blocks = []
        for slot in range(3):
            raw = pk_ref[0, slot, 0:4, :]
            listed = pk_ref[0, slot, pl.ds(4 + entry, 1), :][:, :cap]
            species = raw[2:3]
            slab = raw[3:4]
            amplitude = jnp.zeros_like(species)
            inverse = jnp.zeros_like(species)
            for k in range(species_count):
                match = species == float(k)
                amplitude = jnp.where(match, table_ref[0, k], amplitude)
                inverse = jnp.where(match, table_ref[1, k], inverse)
            zero = jnp.zeros_like(species)
            per_layer = [jnp.where(slab == float(l), amplitude, zero) for l in range(layers)]
            fields = jnp.concatenate(
                [raw[0:2], inverse] + per_layer + [zero] * (8 - 3 - layers), 0
            )
            atoms = fields.shape[1]
            safe = jnp.maximum(listed, 0.0).astype(jnp.int32)
            onehot = (lax.broadcasted_iota(jnp.int32, (atoms, cap), 0) == safe).astype(f32)
            picked = jnp.dot(
                fields, onehot, preferred_element_type=f32, precision=lax.Precision.HIGHEST
            )
            valid = (listed >= 0.0).astype(f32)
            keep = lax.broadcasted_iota(jnp.int32, (8, 1), 0) < 3
            picked = jnp.where(keep, picked, picked * valid)
            blocks.append(picked)
        rows = jnp.concatenate(blocks, 1)
        cols = rows.T
        atom_x = rows[0:1]
        inverse_row = rows[2:3]
        atom_y = cols[:, 1:2]
        inverse_col = cols[:, 2:3]
        pixel_col = lax.broadcasted_iota(jnp.int32, (w, 1), 0).astype(f32)
        pixel_row = lax.broadcasted_iota(jnp.int32, (1, w), 1).astype(f32)
        shift_x = pos_ref[0, 0].astype(f32)
        dist_x = wrap(atom_x - shift_x - pixel_col + 0.5 * field_x, field_x) - 0.5 * field_x
        across = jnp.exp(-dist_x * dist_x * inverse_row).astype(bf16)
        for p in range(batch):
            shift_y = pos_ref[p, 1].astype(f32)
            dist_y = wrap(atom_y - shift_y - pixel_row + 0.5 * w, w) - 0.5 * w
            along = jnp.exp(-dist_y * dist_y * inverse_col)
            weighted = jnp.concatenate(
                [(cols[:, 3 + l : 4 + l] * along).astype(bf16) for l in range(layers)], 1
            )
            pot_ref[p] = dot(across, weighted)

    @pl.when(first)
    def _():
        for copy in copies:
            copy.wait()
        if carried:
            wave_ref[...] = last_ref[...]
        else:
            rows = dot(a_ref[...], last_ref[...]).astype(bf16)
            rows = jnp.concatenate([rows[:w], rows[w:]], 1)
            start = dot(rows, b_ref[...]).astype(bf16)
            for p in range(batch):
                wave_ref[p] = start

    pr = prop_ref[0]
    pi = prop_ref[1]
    column = pl.ds(pl.multiple_of(layer * w, w), w)
    transmitted = []
    for p in range(batch):
        psi = wave_ref[p]
        wr = psi[:, :w].astype(f32)
        wi = psi[:, w:].astype(f32)
        v = pot_ref[p, :, column]
        sv, cv = sincos(v)
        tr = (wr * cv - wi * sv).astype(bf16)
        ti = (wr * sv + wi * cv).astype(bf16)
        transmitted.append(jnp.concatenate([tr, ti], 1))
    rowwise = dot(jnp.concatenate(transmitted, 0), a_ref[...]).astype(bf16)
    planar = jnp.concatenate(
        [
            jnp.concatenate([rowwise[p * w:(p + 1) * w, :w], rowwise[p * w:(p + 1) * w, w:]], 0)
            for p in range(batch)
        ],
        1,
    )
    spectra = dot(b_ref[...], planar)
    sr = spectra[:w]
    si = spectra[w:]
    prb = jnp.concatenate([pr] * batch, 1)
    pib = jnp.concatenate([pi] * batch, 1)
    propagated = jnp.concatenate(
        [(sr * prb - si * pib).astype(bf16), (sr * pib + si * prb).astype(bf16)], 0
    )
    back = dot(a_ref[...], propagated).astype(bf16)
    columns = jnp.concatenate(
        [
            jnp.concatenate([back[:w, p * w:(p + 1) * w], back[w:, p * w:(p + 1) * w]], 1)
            for p in range(batch)
        ],
        0,
    )
    waves = dot(columns, b_ref[...]).astype(bf16)
    for p in range(batch):
        wave_ref[p] = waves[p * w:(p + 1) * w]

    @pl.when((hop == pl.num_programs(0) - 1) & (layer == pl.num_programs(1) - 1))
    def _():
        if final:
            for p in range(batch):
                out_ref[p, :, 0, :] = wave_ref[p, :, :w]
                out_ref[p, :, 1, :] = wave_ref[p, :, w:]
        else:
            out_ref[...] = wave_ref[...]


def run_slices(probe_pos, entry, table, packs, window, layers, field_x, cap, wave=None, final=False):
    batch = probe_pos.shape[0]
    hops = packs.shape[0]
    w = window
    a, b = dft_blocks(w)
    prop = propagator(w)
    full = lambda shape: pl.BlockSpec(shape, lambda h, l, *_: (0,) * len(shape))
    carried = wave is not None
    out_shape = (batch, w, 2, w) if final else (batch, w, 2 * w)
    last = wave if carried else jnp.asarray(start_spectrum(w))
    atoms = 3 * cap
    steps = batch * hops * layers
    flops = steps * 4 * 2 * w * (2 * w) * (2 * w) + batch * hops * 2 * w * atoms * layers * w
    return pl.pallas_call(
        functools.partial(slices_kernel, field_x=float(field_x), carried=carried, cap=cap, final=final),
        out_shape=jax.ShapeDtypeStruct(out_shape, jnp.bfloat16),
        grid_spec=pltpu.PrefetchScalarGridSpec(
            num_scalar_prefetch=2,
            grid=(hops, layers),
            in_specs=[
                pl.BlockSpec(memory_space=pltpu.SMEM),
                pl.BlockSpec((1,) + packs.shape[1:], lambda h, l, *_: (h, 0, 0, 0)),
                pl.BlockSpec(memory_space=pl.ANY),
                pl.BlockSpec(memory_space=pl.ANY),
                pl.BlockSpec(memory_space=pl.ANY),
                pl.BlockSpec(memory_space=pl.ANY),
            ],
            out_specs=full(out_shape),
            scratch_shapes=[
                pltpu.VMEM((batch, w, 2 * w), jnp.bfloat16),
                pltpu.VMEM((batch, w, layers * w), jnp.float32),
                pltpu.VMEM(a.shape, jnp.bfloat16),
                pltpu.VMEM(b.shape, jnp.bfloat16),
                pltpu.VMEM(prop.shape, jnp.float32),
                pltpu.VMEM(last.shape, jnp.bfloat16),
                pltpu.SemaphoreType.DMA((4,)),
            ],
        ),
        compiler_params=pltpu.CompilerParams(
            dimension_semantics=("arbitrary", "arbitrary"),
        ),
        cost_estimate=pl.CostEstimate(
            flops=flops,
            transcendentals=steps * 2 * w * w + batch * hops * 2 * atoms * w,
            bytes_accessed=2 * (2 * w) ** 2 * 2 + 3 * w * w * 4 + batch * w * w * 4,
        ),
    )(probe_pos, entry, table, packs, jnp.asarray(a), jnp.asarray(b), jnp.asarray(prop), last)


def shards(atom_xy, atom_species, atom_slab, species_amp, species_spread, margin, probe_pos):
    layers = SL_DEV
    window = W
    atoms = atom_xy.shape[-1]
    cap = margin.shape[-1]
    n_lat = lax.axis_size("lat")
    owners = lax.axis_size("slc")
    field_x = n_lat * atoms * (2 * window // cap)
    f32 = jnp.float32
    raw = jnp.concatenate(
        [atom_xy[0, 0], atom_species[0, 0][None].astype(f32), atom_slab[0, 0][None].astype(f32)], 0
    )
    marg = jnp.transpose(margin[0, 0, :, 0], (1, 0, 2)).astype(f32)
    marg = jnp.pad(marg, ((0, 0), (0, 0), (0, atoms - cap)), constant_values=-1.0)
    packs = jnp.concatenate([jnp.broadcast_to(raw[None], (3,) + raw.shape), marg], 1)
    from_left = lax.ppermute(packs[2], "lat", [(i, (i + 1) % n_lat) for i in range(n_lat)])
    from_right = lax.ppermute(packs[0], "lat", [((i + 1) % n_lat, i) for i in range(n_lat)])
    local = jnp.stack([from_left, packs[1], from_right], 0)[None]
    me = lax.axis_index("slc")
    entry = jnp.reshape(me, (1,)).astype(jnp.int32)
    later = [
        lax.ppermute(local, "slc", [(i, (i - hop) % owners) for i in range(owners)])
        for hop in range(1, owners)
    ]
    table = jnp.stack([species_amp, 0.5 / (species_spread * species_spread)], 0)
    batch = probe_pos.shape[0]
    wave = run_slices(probe_pos, entry, table, local, window, layers, field_x, cap, final=not later)
    if later:
        wave = run_slices(
            probe_pos, entry, table, jnp.concatenate(later, 0), window, layers, field_x, cap, wave,
            final=True,
        )
    return wave


def solution(mesh):
    in_specs = (
        P(("groups", "lat"), "slc", None, None),
        P(("groups", "lat"), "slc", None),
        P(("groups", "lat"), "slc", None),
        P(),
        P(),
        P(("groups", "lat"), "slc", None, "rep", None, None),
        P(("groups", "lat", "slc", "rep"), None),
    )
    out_specs = P(("groups", "lat", "slc", "rep"), None, None, None)
    return jax.shard_map(shards, mesh=mesh, in_specs=in_specs, out_specs=out_specs, check_vma=False)
```

```python
import functools
import math

import jax
import numpy as np
import jax.numpy as jnp
from jax import lax
from jax.experimental import pallas as pl
from jax.experimental.pallas import tpu as pltpu
from jax.sharding import PartitionSpec as P

W = 256
SL_DEV = 2


PROPAGATION_COEF = 0.001
DEFOCUS_COEF = 4.19


def centered_frequency(window):
    indices = np.arange(window, dtype=np.int32)
    return np.where(indices < window // 2, indices, indices - window).astype(np.float32)


def squared_radius(window):
    frequency = centered_frequency(window)
    return frequency[:, None] * frequency[:, None] + frequency[None, :] * frequency[None, :]


def dft_blocks(window):
    indices = np.arange(window, dtype=np.int32)
    product = indices[:, None] * indices[None, :] % window
    angle = np.float32(2.0 * math.pi / window) * product.astype(np.float32)
    scale = np.float32(math.sqrt(window))
    re = (np.cos(angle) / scale).astype(jnp.bfloat16)
    im = (np.sin(angle) / scale).astype(jnp.bfloat16)
    a = np.block([[re, -im], [im, re]])
    b = np.block([[re, im], [-im, re]])
    return a, b


def propagator(window):
    radius = squared_radius(window)
    inside = (np.float32(9.0) * radius < window * window).astype(np.float32)
    phase_angle = np.float32(-PROPAGATION_COEF * (65536.0 / (window * window))) * radius
    return np.stack([inside * np.cos(phase_angle), inside * np.sin(phase_angle)], 0)


def start_spectrum(window):
    radius = squared_radius(window)
    inside = (np.float32(16.0) * radius < window * window).astype(np.float32)
    norm_scale = np.float32(window) / np.sqrt(np.sum(inside, dtype=np.float32))
    phase_angle = np.float32(-(DEFOCUS_COEF / window)) * radius
    spectrum = np.concatenate(
        [inside * norm_scale * np.cos(phase_angle), inside * norm_scale * np.sin(phase_angle)], 0
    )
    return spectrum.astype(jnp.bfloat16)


def atom_fields(positions, species, slab, species_amp, species_spread, layers):
    species_match = (
        species[None, :] == jnp.arange(species_amp.shape[0], dtype=jnp.int32)[:, None]
    ).astype(species_amp.dtype)
    amplitude = jnp.sum(species_match * species_amp[:, None], 0)
    spread = jnp.sum(species_match * species_spread[:, None], 0)
    inverse = 0.5 / (spread * spread)
    slab_match = (slab[None, :] == jnp.arange(layers, dtype=jnp.int32)[:, None]).astype(
        amplitude.dtype
    )
    return jnp.concatenate([positions, inverse[None, :], slab_match * amplitude[None, :]], 0)


def pick_rows(fields, pick_list):
    valid_mask = (pick_list >= 0).astype(fields.dtype)
    safe_index = jnp.maximum(pick_list, 0)
    gathered = fields[:, safe_index]
    return jnp.concatenate([gathered[:3], gathered[3:] * valid_mask[None]], 0)


def wrap(value, period):
    return value - period * jnp.floor(value * (1.0 / period))


def sincos(v):
    q = jnp.floor(v * 0.6366197723675814 + 0.5)
    r = v - q * 1.5703125
    r = r - q * 4.837512969970703125e-4
    r = r - q * 7.549789954891882e-8
    z = r * r
    s = r + r * z * (-1.6666654611e-1 + z * (8.3321608736e-3 + z * -1.9515295891e-4))
    c = 1.0 - 0.5 * z + z * z * (4.166664568298827e-2 + z * (-1.388731625493765e-3 + z * 2.443315711809948e-5))
    n = q.astype(jnp.int32)
    swap = (n & 1) == 1
    sin_v = jnp.where(swap, c, s)
    cos_v = jnp.where(swap, s, c)
    sin_v = jnp.where((n & 2) == 2, -sin_v, sin_v)
    cos_v = jnp.where(((n + 1) & 2) == 2, -cos_v, cos_v)
    return sin_v, cos_v


def slices_kernel(*refs, field_x, carried, cap, final):
    (pos_ref, owner_ref, table_ref, pk_ref, a_hbm, b_hbm, prop_hbm, last_hbm,
     out_ref, wave_ref, pot_ref, a_ref, b_ref, prop_ref, last_ref, sems) = refs
    batch = wave_ref.shape[0]
    w = prop_ref.shape[-1]
    layers = pot_ref.shape[-1] // w
    species_count = table_ref.shape[1]
    hop = pl.program_id(0)
    f32, bf16 = jnp.float32, jnp.bfloat16

    def dot(a, b):
        return jnp.dot(a, b, preferred_element_type=f32)

    first = hop == 0
    copies = [
        pltpu.make_async_copy(src, dst, sems.at[k])
        for k, (src, dst) in enumerate(
            [(a_hbm, a_ref), (b_hbm, b_ref), (prop_hbm, prop_ref), (last_hbm, last_ref)]
        )
    ]

    @pl.when(first)
    def _():
        for copy in copies:
            copy.start()

    def potentials():
        entry = owner_ref[0]
        blocks = []
        for slot in range(3):
            raw = pk_ref[0, slot, 0:4, :]
            listed = pk_ref[0, slot, pl.ds(4 + entry, 1), :][:, :cap]
            species = raw[2:3]
            slab = raw[3:4]
            amplitude = jnp.zeros_like(species)
            inverse = jnp.zeros_like(species)
            for k in range(species_count):
                match = species == float(k)
                amplitude = jnp.where(match, table_ref[0, k], amplitude)
                inverse = jnp.where(match, table_ref[1, k], inverse)
            zero = jnp.zeros_like(species)
            per_layer = [jnp.where(slab == float(l), amplitude, zero) for l in range(layers)]
            fields = jnp.concatenate(
                [raw[0:2], inverse] + per_layer + [zero] * (8 - 3 - layers), 0
            )
            atoms = fields.shape[1]
            safe = jnp.maximum(listed, 0.0).astype(jnp.int32)
            onehot = (lax.broadcasted_iota(jnp.int32, (atoms, cap), 0) == safe).astype(f32)
            picked = jnp.dot(
                fields, onehot, preferred_element_type=f32, precision=lax.Precision.HIGHEST
            )
            valid = (listed >= 0.0).astype(f32)
            keep = lax.broadcasted_iota(jnp.int32, (8, 1), 0) < 3
            picked = jnp.where(keep, picked, picked * valid)
            blocks.append(picked)
        rows = jnp.concatenate(blocks, 1)
        cols = rows.T
        atom_x = rows[0:1]
        inverse_row = rows[2:3]
        atom_y = cols[:, 1:2]
        inverse_col = cols[:, 2:3]
        pixel_col = lax.broadcasted_iota(jnp.int32, (w, 1), 0).astype(f32)
        pixel_row = lax.broadcasted_iota(jnp.int32, (1, w), 1).astype(f32)
        shift_x = pos_ref[0, 0].astype(f32)
        dist_x = wrap(atom_x - shift_x - pixel_col + 0.5 * field_x, field_x) - 0.5 * field_x
        across = jnp.exp(-dist_x * dist_x * inverse_row).astype(bf16)
        for p in range(batch):
            shift_y = pos_ref[p, 1].astype(f32)
            dist_y = wrap(atom_y - shift_y - pixel_row + 0.5 * w, w) - 0.5 * w
            along = jnp.exp(-dist_y * dist_y * inverse_col)
            weighted = jnp.concatenate(
                [(cols[:, 3 + l : 4 + l] * along).astype(bf16) for l in range(layers)], 1
            )
            pot_ref[p] = dot(across, weighted)

    potentials()

    @pl.when(first)
    def _():
        for copy in copies:
            copy.wait()
        if carried:
            wave_ref[...] = last_ref[...]
        else:
            rows = dot(a_ref[...], last_ref[...]).astype(bf16)
            rows = jnp.concatenate([rows[:w], rows[w:]], 1)
            start = dot(rows, b_ref[...]).astype(bf16)
            for p in range(batch):
                wave_ref[p] = start

    pr = prop_ref[0]
    pi = prop_ref[1]
    for layer in range(layers):
        column = pl.ds(layer * w, w)
        transmitted = []
        for p in range(batch):
            psi = wave_ref[p]
            wr = psi[:, :w].astype(f32)
            wi = psi[:, w:].astype(f32)
            v = pot_ref[p, :, column]
            sv, cv = sincos(v)
            tr = (wr * cv - wi * sv).astype(bf16)
            ti = (wr * sv + wi * cv).astype(bf16)
            transmitted.append(jnp.concatenate([tr, ti], 1))
        rowwise = [dot(t, a_ref[...]).astype(bf16) for t in transmitted]
        spectra = [dot(b_ref[...], jnp.concatenate([rw[:, :w], rw[:, w:]], 0)) for rw in rowwise]
        propagated = []
        for sp in spectra:
            sr = sp[:w]
            si = sp[w:]
            propagated.append(
                jnp.concatenate([(sr * pr - si * pi).astype(bf16), (sr * pi + si * pr).astype(bf16)], 0)
            )
        back = [dot(a_ref[...], spb).astype(bf16) for spb in propagated]
        for p, br in enumerate(back):
            wave_ref[p] = dot(jnp.concatenate([br[:w], br[w:]], 1), b_ref[...]).astype(bf16)

    @pl.when(hop == pl.num_programs(0) - 1)
    def _():
        if final:
            for p in range(batch):
                out_ref[p, :, 0, :] = wave_ref[p, :, :w]
                out_ref[p, :, 1, :] = wave_ref[p, :, w:]
        else:
            out_ref[...] = wave_ref[...]


def run_slices(probe_pos, entry, table, packs, window, layers, field_x, cap, wave=None, final=False):
    batch = probe_pos.shape[0]
    hops = packs.shape[0]
    w = window
    a, b = dft_blocks(w)
    prop = propagator(w)
    full = lambda shape: pl.BlockSpec(shape, lambda h, *_: (0,) * len(shape))
    carried = wave is not None
    out_shape = (batch, w, 2, w) if final else (batch, w, 2 * w)
    last = wave if carried else jnp.asarray(start_spectrum(w))
    atoms = 3 * cap
    steps = batch * hops * layers
    flops = steps * 4 * 2 * w * (2 * w) * (2 * w) + batch * hops * 2 * w * atoms * layers * w
    return pl.pallas_call(
        functools.partial(slices_kernel, field_x=float(field_x), carried=carried, cap=cap, final=final),
        out_shape=jax.ShapeDtypeStruct(out_shape, jnp.bfloat16),
        grid_spec=pltpu.PrefetchScalarGridSpec(
            num_scalar_prefetch=2,
            grid=(hops,),
            in_specs=[
                pl.BlockSpec(memory_space=pltpu.SMEM),
                pl.BlockSpec((1,) + packs.shape[1:], lambda h, *_: (h, 0, 0, 0)),
                pl.BlockSpec(memory_space=pl.ANY),
                pl.BlockSpec(memory_space=pl.ANY),
                pl.BlockSpec(memory_space=pl.ANY),
                pl.BlockSpec(memory_space=pl.ANY),
            ],
            out_specs=full(out_shape),
            scratch_shapes=[
                pltpu.VMEM((batch, w, 2 * w), jnp.bfloat16),
                pltpu.VMEM((batch, w, layers * w), jnp.float32),
                pltpu.VMEM(a.shape, jnp.bfloat16),
                pltpu.VMEM(b.shape, jnp.bfloat16),
                pltpu.VMEM(prop.shape, jnp.float32),
                pltpu.VMEM(last.shape, jnp.bfloat16),
                pltpu.SemaphoreType.DMA((4,)),
            ],
        ),
        compiler_params=pltpu.CompilerParams(
            dimension_semantics=("arbitrary",),
        ),
        cost_estimate=pl.CostEstimate(
            flops=flops,
            transcendentals=steps * 2 * w * w + batch * hops * 2 * atoms * w,
            bytes_accessed=2 * (2 * w) ** 2 * 2 + 3 * w * w * 4 + batch * w * w * 4,
        ),
    )(probe_pos, entry, table, packs, jnp.asarray(a), jnp.asarray(b), jnp.asarray(prop), last)


def shards(atom_xy, atom_species, atom_slab, species_amp, species_spread, margin, probe_pos):
    layers = SL_DEV
    window = W
    atoms = atom_xy.shape[-1]
    cap = margin.shape[-1]
    n_lat = lax.axis_size("lat")
    owners = lax.axis_size("slc")
    field_x = n_lat * atoms * (2 * window // cap)
    f32 = jnp.float32
    raw = jnp.concatenate(
        [atom_xy[0, 0], atom_species[0, 0][None].astype(f32), atom_slab[0, 0][None].astype(f32)], 0
    )
    marg = jnp.transpose(margin[0, 0, :, 0], (1, 0, 2)).astype(f32)
    marg = jnp.pad(marg, ((0, 0), (0, 0), (0, atoms - cap)), constant_values=-1.0)
    packs = jnp.concatenate([jnp.broadcast_to(raw[None], (3,) + raw.shape), marg], 1)
    from_left = lax.ppermute(packs[2], "lat", [(i, (i + 1) % n_lat) for i in range(n_lat)])
    from_right = lax.ppermute(packs[0], "lat", [((i + 1) % n_lat, i) for i in range(n_lat)])
    local = jnp.stack([from_left, packs[1], from_right], 0)[None]
    me = lax.axis_index("slc")
    entry = jnp.reshape(me, (1,)).astype(jnp.int32)
    later = [
        lax.ppermute(local, "slc", [(i, (i - hop) % owners) for i in range(owners)])
        for hop in range(1, owners)
    ]
    table = jnp.stack([species_amp, 0.5 / (species_spread * species_spread)], 0)
    batch = probe_pos.shape[0]
    wave = run_slices(probe_pos, entry, table, local, window, layers, field_x, cap, final=not later)
    if later:
        wave = run_slices(
            probe_pos, entry, table, jnp.concatenate(later, 0), window, layers, field_x, cap, wave,
            final=True,
        )
    return wave


def solution(mesh):
    in_specs = (
        P(("groups", "lat"), "slc", None, None),
        P(("groups", "lat"), "slc", None),
        P(("groups", "lat"), "slc", None),
        P(),
        P(),
        P(("groups", "lat"), "slc", None, "rep", None, None),
        P(("groups", "lat", "slc", "rep"), None),
    )
    out_specs = P(("groups", "lat", "slc", "rep"), None, None, None)
    return jax.shard_map(shards, mesh=mesh, in_specs=in_specs, out_specs=out_specs, check_vma=False)
```

```python
import functools
import math

import jax
import numpy as np
import jax.numpy as jnp
from jax import lax
from jax.experimental import pallas as pl
from jax.experimental.pallas import tpu as pltpu
from jax.sharding import PartitionSpec as P

W = 256
SL_DEV = 2


PROPAGATION_COEF = 0.001
DEFOCUS_COEF = 4.19


def centered_frequency(window):
    indices = np.arange(window, dtype=np.int32)
    return np.where(indices < window // 2, indices, indices - window).astype(np.float32)


def squared_radius(window):
    frequency = centered_frequency(window)
    return frequency[:, None] * frequency[:, None] + frequency[None, :] * frequency[None, :]


def dft_blocks(window):
    indices = np.arange(window, dtype=np.int32)
    product = indices[:, None] * indices[None, :] % window
    angle = np.float32(2.0 * math.pi / window) * product.astype(np.float32)
    scale = np.float32(math.sqrt(window))
    re = (np.cos(angle) / scale).astype(jnp.bfloat16)
    im = (np.sin(angle) / scale).astype(jnp.bfloat16)
    a = np.block([[re, -im], [im, re]])
    b = np.block([[re, im], [-im, re]])
    return a, b


def propagator(window):
    radius = squared_radius(window)
    inside = (np.float32(9.0) * radius < window * window).astype(np.float32)
    phase_angle = np.float32(-PROPAGATION_COEF * (65536.0 / (window * window))) * radius
    return np.stack([inside * np.cos(phase_angle), inside * np.sin(phase_angle)], 0)


def start_spectrum(window):
    radius = squared_radius(window)
    inside = (np.float32(16.0) * radius < window * window).astype(np.float32)
    norm_scale = np.float32(window) / np.sqrt(np.sum(inside, dtype=np.float32))
    phase_angle = np.float32(-(DEFOCUS_COEF / window)) * radius
    spectrum = np.concatenate(
        [inside * norm_scale * np.cos(phase_angle), inside * norm_scale * np.sin(phase_angle)], 0
    )
    return spectrum.astype(jnp.bfloat16)


def atom_fields(positions, species, slab, species_amp, species_spread, layers):
    species_match = (
        species[None, :] == jnp.arange(species_amp.shape[0], dtype=jnp.int32)[:, None]
    ).astype(species_amp.dtype)
    amplitude = jnp.sum(species_match * species_amp[:, None], 0)
    spread = jnp.sum(species_match * species_spread[:, None], 0)
    inverse = 0.5 / (spread * spread)
    slab_match = (slab[None, :] == jnp.arange(layers, dtype=jnp.int32)[:, None]).astype(
        amplitude.dtype
    )
    return jnp.concatenate([positions, inverse[None, :], slab_match * amplitude[None, :]], 0)


def pick_rows(fields, pick_list):
    valid_mask = (pick_list >= 0).astype(fields.dtype)
    safe_index = jnp.maximum(pick_list, 0)
    gathered = fields[:, safe_index]
    return jnp.concatenate([gathered[:3], gathered[3:] * valid_mask[None]], 0)


def wrap(value, period):
    return value - period * jnp.floor(value * (1.0 / period))


def sincos(v):
    q = jnp.floor(v * 0.6366197723675814 + 0.5)
    r = v - q * 1.5703125
    r = r - q * 4.837512969970703125e-4
    r = r - q * 7.549789954891882e-8
    z = r * r
    s = r + r * z * (-1.6666654611e-1 + z * (8.3321608736e-3 + z * -1.9515295891e-4))
    c = 1.0 - 0.5 * z + z * z * (4.166664568298827e-2 + z * (-1.388731625493765e-3 + z * 2.443315711809948e-5))
    n = q.astype(jnp.int32)
    swap = (n & 1) == 1
    sin_v = jnp.where(swap, c, s)
    cos_v = jnp.where(swap, s, c)
    sin_v = jnp.where((n & 2) == 2, -sin_v, sin_v)
    cos_v = jnp.where(((n + 1) & 2) == 2, -cos_v, cos_v)
    return sin_v, cos_v


def slices_kernel(*refs, field_x, carried, cap, final):
    (pos_ref, owner_ref, amp_ref, spread_ref, pk_ref, a_hbm, b_hbm, prop_hbm, last_hbm,
     out_ref, wave_ref, pot_ref, a_ref, b_ref, prop_ref, last_ref, sems) = refs
    batch = wave_ref.shape[0]
    w = prop_ref.shape[-1]
    layers = pot_ref.shape[-1] // w
    species_count = amp_ref.shape[0]
    hop = pl.program_id(0)
    f32, bf16 = jnp.float32, jnp.bfloat16

    def dot(a, b):
        return jnp.dot(a, b, preferred_element_type=f32)

    first = hop == 0
    copies = [
        pltpu.make_async_copy(src, dst, sems.at[k])
        for k, (src, dst) in enumerate(
            [(a_hbm, a_ref), (b_hbm, b_ref), (prop_hbm, prop_ref), (last_hbm, last_ref)]
        )
    ]

    @pl.when(first)
    def _():
        for copy in copies:
            copy.start()

    def potentials():
        entry = owner_ref[0]
        blocks = []
        for slot in range(3):
            raw = pk_ref[hop, slot, 0:4, :]
            listed = pk_ref[hop, slot, pl.ds(4 + entry, 1), :][:, :cap]
            species = raw[2:3]
            slab = raw[3:4]
            amplitude = jnp.zeros_like(species)
            spread = jnp.zeros_like(species)
            for k in range(species_count):
                match = species == float(k)
                amplitude = jnp.where(match, amp_ref[k], amplitude)
                spread = jnp.where(match, spread_ref[k], spread)
            inverse = 0.5 / (spread * spread)
            zero = jnp.zeros_like(species)
            per_layer = [jnp.where(slab == float(l), amplitude, zero) for l in range(layers)]
            fields = jnp.concatenate(
                [raw[0:2], inverse] + per_layer + [zero] * (8 - 3 - layers), 0
            )
            atoms = fields.shape[1]
            safe = jnp.maximum(listed, 0.0).astype(jnp.int32)
            onehot = (lax.broadcasted_iota(jnp.int32, (atoms, cap), 0) == safe).astype(f32)
            picked = jnp.dot(
                fields, onehot, preferred_element_type=f32, precision=lax.Precision.HIGHEST
            )
            valid = (listed >= 0.0).astype(f32)
            keep = lax.broadcasted_iota(jnp.int32, (8, 1), 0) < 3
            picked = jnp.where(keep, picked, picked * valid)
            blocks.append(picked)
        rows = jnp.concatenate(blocks, 1)
        cols = rows.T
        atom_x = rows[0:1]
        inverse_row = rows[2:3]
        atom_y = cols[:, 1:2]
        inverse_col = cols[:, 2:3]
        pixel_col = lax.broadcasted_iota(jnp.int32, (w, 1), 0).astype(f32)
        pixel_row = lax.broadcasted_iota(jnp.int32, (1, w), 1).astype(f32)
        shift_x = pos_ref[0, 0].astype(f32)
        dist_x = wrap(atom_x - shift_x - pixel_col + 0.5 * field_x, field_x) - 0.5 * field_x
        across = jnp.exp(-dist_x * dist_x * inverse_row).astype(bf16)
        for p in range(batch):
            shift_y = pos_ref[p, 1].astype(f32)
            dist_y = wrap(atom_y - shift_y - pixel_row + 0.5 * w, w) - 0.5 * w
            along = jnp.exp(-dist_y * dist_y * inverse_col)
            weighted = jnp.concatenate(
                [(cols[:, 3 + l : 4 + l] * along).astype(bf16) for l in range(layers)], 1
            )
            pot_ref[p] = dot(across, weighted)

    potentials()

    @pl.when(first)
    def _():
        for copy in copies:
            copy.wait()
        if carried:
            wave_ref[...] = last_ref[...]
        else:
            rows = dot(a_ref[...], last_ref[...]).astype(bf16)
            rows = jnp.concatenate([rows[:w], rows[w:]], 1)
            start = dot(rows, b_ref[...]).astype(bf16)
            for p in range(batch):
                wave_ref[p] = start

    pr = prop_ref[0]
    pi = prop_ref[1]
    for layer in range(layers):
        column = pl.ds(layer * w, w)
        transmitted = []
        for p in range(batch):
            psi = wave_ref[p]
            wr = psi[:, :w].astype(f32)
            wi = psi[:, w:].astype(f32)
            v = pot_ref[p, :, column]
            sv, cv = sincos(v)
            tr = (wr * cv - wi * sv).astype(bf16)
            ti = (wr * sv + wi * cv).astype(bf16)
            transmitted.append(jnp.concatenate([tr, ti], 1))
        rowwise = [dot(t, a_ref[...]).astype(bf16) for t in transmitted]
        spectra = [dot(b_ref[...], jnp.concatenate([rw[:, :w], rw[:, w:]], 0)) for rw in rowwise]
        propagated = []
        for sp in spectra:
            sr = sp[:w]
            si = sp[w:]
            propagated.append(
                jnp.concatenate([(sr * pr - si * pi).astype(bf16), (sr * pi + si * pr).astype(bf16)], 0)
            )
        back = [dot(a_ref[...], spb).astype(bf16) for spb in propagated]
        for p, br in enumerate(back):
            wave_ref[p] = dot(jnp.concatenate([br[:w], br[w:]], 1), b_ref[...]).astype(bf16)

    @pl.when(hop == pl.num_programs(0) - 1)
    def _():
        if final:
            for p in range(batch):
                out_ref[p, :, 0, :] = wave_ref[p, :, :w]
                out_ref[p, :, 1, :] = wave_ref[p, :, w:]
        else:
            out_ref[...] = wave_ref[...]


def run_slices(probe_pos, entry, amp, spread, packs, window, layers, field_x, cap, wave=None, final=False):
    batch = probe_pos.shape[0]
    hops = packs.shape[0]
    w = window
    a, b = dft_blocks(w)
    prop = propagator(w)
    full = lambda shape: pl.BlockSpec(shape, lambda h, *_: (0,) * len(shape))
    carried = wave is not None
    out_shape = (batch, w, 2, w) if final else (batch, w, 2 * w)
    last = wave if carried else jnp.asarray(start_spectrum(w))
    atoms = 3 * cap
    steps = batch * hops * layers
    flops = steps * 4 * 2 * w * (2 * w) * (2 * w) + batch * hops * 2 * w * atoms * layers * w
    return pl.pallas_call(
        functools.partial(slices_kernel, field_x=float(field_x), carried=carried, cap=cap, final=final),
        out_shape=jax.ShapeDtypeStruct(out_shape, jnp.bfloat16),
        grid_spec=pltpu.PrefetchScalarGridSpec(
            num_scalar_prefetch=2,
            grid=(hops,),
            in_specs=[
                pl.BlockSpec(memory_space=pltpu.SMEM),
                pl.BlockSpec(memory_space=pltpu.SMEM),
                pl.BlockSpec(memory_space=pltpu.VMEM),
                pl.BlockSpec(memory_space=pl.ANY),
                pl.BlockSpec(memory_space=pl.ANY),
                pl.BlockSpec(memory_space=pl.ANY),
                pl.BlockSpec(memory_space=pl.ANY),
            ],
            out_specs=full(out_shape),
            scratch_shapes=[
                pltpu.VMEM((batch, w, 2 * w), jnp.bfloat16),
                pltpu.VMEM((batch, w, layers * w), jnp.float32),
                pltpu.VMEM(a.shape, jnp.bfloat16),
                pltpu.VMEM(b.shape, jnp.bfloat16),
                pltpu.VMEM(prop.shape, jnp.float32),
                pltpu.VMEM(last.shape, jnp.bfloat16),
                pltpu.SemaphoreType.DMA((4,)),
            ],
        ),
        compiler_params=pltpu.CompilerParams(
            dimension_semantics=("arbitrary",),
        ),
        cost_estimate=pl.CostEstimate(
            flops=flops,
            transcendentals=steps * 2 * w * w + batch * hops * 2 * atoms * w,
            bytes_accessed=2 * (2 * w) ** 2 * 2 + 3 * w * w * 4 + batch * w * w * 4,
        ),
    )(probe_pos, entry, amp, spread, packs, jnp.asarray(a), jnp.asarray(b), jnp.asarray(prop), last)


def shards(atom_xy, atom_species, atom_slab, species_amp, species_spread, margin, probe_pos):
    layers = SL_DEV
    window = W
    atoms = atom_xy.shape[-1]
    cap = margin.shape[-1]
    n_lat = lax.axis_size("lat")
    owners = lax.axis_size("slc")
    field_x = n_lat * atoms * (2 * window // cap)
    f32 = jnp.float32
    raw = jnp.concatenate(
        [atom_xy[0, 0], atom_species[0, 0][None].astype(f32), atom_slab[0, 0][None].astype(f32)], 0
    )
    marg = jnp.transpose(margin[0, 0, :, 0], (1, 0, 2)).astype(f32)
    marg = jnp.pad(marg, ((0, 0), (0, 0), (0, atoms - cap)), constant_values=-1.0)
    packs = jnp.concatenate([jnp.broadcast_to(raw[None], (3,) + raw.shape), marg], 1)
    from_left = lax.ppermute(packs[2], "lat", [(i, (i + 1) % n_lat) for i in range(n_lat)])
    from_right = lax.ppermute(packs[0], "lat", [((i + 1) % n_lat, i) for i in range(n_lat)])
    local = jnp.stack([from_left, packs[1], from_right], 0)[None]
    me = lax.axis_index("slc")
    entry = jnp.reshape(me, (1,)).astype(jnp.int32)
    later = [
        lax.ppermute(local, "slc", [(i, (i - hop) % owners) for i in range(owners)])
        for hop in range(1, owners)
    ]
    batch = probe_pos.shape[0]
    wave = run_slices(probe_pos, entry, species_amp, species_spread, local, window, layers, field_x, cap, final=not later)
    if later:
        wave = run_slices(
            probe_pos, entry, species_amp, species_spread, jnp.concatenate(later, 0), window, layers, field_x, cap, wave,
            final=True,
        )
    return wave


def solution(mesh):
    in_specs = (
        P(("groups", "lat"), "slc", None, None),
        P(("groups", "lat"), "slc", None),
        P(("groups", "lat"), "slc", None),
        P(),
        P(),
        P(("groups", "lat"), "slc", None, "rep", None, None),
        P(("groups", "lat", "slc", "rep"), None),
    )
    out_specs = P(("groups", "lat", "slc", "rep"), None, None, None)
    return jax.shard_map(shards, mesh=mesh, in_specs=in_specs, out_specs=out_specs, check_vma=False)
```

```python
import functools
import math

import jax
import numpy as np
import jax.numpy as jnp
from jax import lax
from jax.experimental import pallas as pl
from jax.experimental.pallas import tpu as pltpu
from jax.sharding import PartitionSpec as P

W = 256
SL_DEV = 2


PROPAGATION_COEF = 0.001
DEFOCUS_COEF = 4.19


def centered_frequency(window):
    indices = np.arange(window, dtype=np.int32)
    return np.where(indices < window // 2, indices, indices - window).astype(np.float32)


def squared_radius(window):
    frequency = centered_frequency(window)
    return frequency[:, None] * frequency[:, None] + frequency[None, :] * frequency[None, :]


def dft_blocks(window):
    indices = np.arange(window, dtype=np.int32)
    product = indices[:, None] * indices[None, :] % window
    angle = np.float32(2.0 * math.pi / window) * product.astype(np.float32)
    scale = np.float32(math.sqrt(window))
    re = (np.cos(angle) / scale).astype(jnp.bfloat16)
    im = (np.sin(angle) / scale).astype(jnp.bfloat16)
    a = np.block([[re, -im], [im, re]])
    b = np.block([[re, im], [-im, re]])
    return a, b


def propagator(window):
    radius = squared_radius(window)
    inside = (np.float32(9.0) * radius < window * window).astype(np.float32)
    phase_angle = np.float32(-PROPAGATION_COEF * (65536.0 / (window * window))) * radius
    return np.stack([inside * np.cos(phase_angle), inside * np.sin(phase_angle)], 0)


def start_spectrum(window):
    radius = squared_radius(window)
    inside = (np.float32(16.0) * radius < window * window).astype(np.float32)
    norm_scale = np.float32(window) / np.sqrt(np.sum(inside, dtype=np.float32))
    phase_angle = np.float32(-(DEFOCUS_COEF / window)) * radius
    spectrum = np.concatenate(
        [inside * norm_scale * np.cos(phase_angle), inside * norm_scale * np.sin(phase_angle)], 0
    )
    return spectrum.astype(jnp.bfloat16)


def atom_fields(positions, species, slab, species_amp, species_spread, layers):
    species_match = (
        species[None, :] == jnp.arange(species_amp.shape[0], dtype=jnp.int32)[:, None]
    ).astype(species_amp.dtype)
    amplitude = jnp.sum(species_match * species_amp[:, None], 0)
    spread = jnp.sum(species_match * species_spread[:, None], 0)
    inverse = 0.5 / (spread * spread)
    slab_match = (slab[None, :] == jnp.arange(layers, dtype=jnp.int32)[:, None]).astype(
        amplitude.dtype
    )
    return jnp.concatenate([positions, inverse[None, :], slab_match * amplitude[None, :]], 0)


def pick_rows(fields, pick_list):
    valid_mask = (pick_list >= 0).astype(fields.dtype)
    safe_index = jnp.maximum(pick_list, 0)
    gathered = fields[:, safe_index]
    return jnp.concatenate([gathered[:3], gathered[3:] * valid_mask[None]], 0)


def wrap(value, period):
    return value - period * jnp.floor(value * (1.0 / period))


def sincos(v):
    q = jnp.floor(v * 0.6366197723675814 + 0.5)
    r = v - q * 1.5703125
    r = r - q * 4.837512969970703125e-4
    r = r - q * 7.549789954891882e-8
    z = r * r
    s = r + r * z * (-1.6666654611e-1 + z * (8.3321608736e-3 + z * -1.9515295891e-4))
    c = 1.0 - 0.5 * z + z * z * (4.166664568298827e-2 + z * (-1.388731625493765e-3 + z * 2.443315711809948e-5))
    n = q.astype(jnp.int32)
    swap = (n & 1) == 1
    sin_v = jnp.where(swap, c, s)
    cos_v = jnp.where(swap, s, c)
    sin_v = jnp.where((n & 2) == 2, -sin_v, sin_v)
    cos_v = jnp.where(((n + 1) & 2) == 2, -cos_v, cos_v)
    return sin_v, cos_v


def slices_kernel(*refs, field_x, carried, cap, final):
    (pos_ref, owner_ref, amp_ref, spread_ref, pk_ref, a_hbm, b_hbm, prop_hbm, last_hbm,
     out_ref, wave_ref, pot_ref, a_ref, b_ref, prop_ref, last_ref, sems) = refs
    batch = wave_ref.shape[0]
    w = prop_ref.shape[-1]
    layers = pot_ref.shape[-1] // w
    species_count = amp_ref.shape[0]
    hop = pl.program_id(0)
    f32, bf16 = jnp.float32, jnp.bfloat16

    def dot(a, b):
        return jnp.dot(a, b, preferred_element_type=f32)

    first = hop == 0
    copies = [
        pltpu.make_async_copy(src, dst, sems.at[k])
        for k, (src, dst) in enumerate(
            [(a_hbm, a_ref), (b_hbm, b_ref), (prop_hbm, prop_ref), (last_hbm, last_ref)]
        )
    ]

    @pl.when(first)
    def _():
        for copy in copies:
            copy.start()

    def potentials():
        entry = owner_ref[0]
        blocks = []
        for slot in range(3):
            raw = pk_ref[hop, slot, 0:4, :]
            listed = pk_ref[hop, slot, pl.ds(4 + entry, 1), :][:, :cap]
            species = raw[2:3]
            slab = raw[3:4]
            amplitude = jnp.zeros_like(species)
            spread = jnp.zeros_like(species)
            for k in range(species_count):
                match = species == float(k)
                amplitude = jnp.where(match, amp_ref[k], amplitude)
                spread = jnp.where(match, spread_ref[k], spread)
            inverse = 0.5 / (spread * spread)
            zero = jnp.zeros_like(species)
            per_layer = [jnp.where(slab == float(l), amplitude, zero) for l in range(layers)]
            fields = jnp.concatenate(
                [raw[0:2], inverse] + per_layer + [zero] * (8 - 3 - layers), 0
            )
            atoms = fields.shape[1]
            safe = jnp.maximum(listed, 0.0).astype(jnp.int32)
            onehot = (lax.broadcasted_iota(jnp.int32, (atoms, cap), 0) == safe).astype(f32)
            picked = jnp.dot(
                fields, onehot, preferred_element_type=f32, precision=lax.Precision.HIGHEST
            )
            valid = (listed >= 0.0).astype(f32)
            keep = lax.broadcasted_iota(jnp.int32, (8, 1), 0) < 3
            picked = jnp.where(keep, picked, picked * valid)
            blocks.append(picked)
        rows = jnp.concatenate(blocks, 1)
        cols = rows.T
        atom_x = rows[0:1]
        inverse_row = rows[2:3]
        atom_y = cols[:, 1:2]
        inverse_col = cols[:, 2:3]
        pixel_col = lax.broadcasted_iota(jnp.int32, (w, 1), 0).astype(f32)
        pixel_row = lax.broadcasted_iota(jnp.int32, (1, w), 1).astype(f32)
        shift_x = pos_ref[0, 0].astype(f32)
        dist_x = wrap(atom_x - shift_x - pixel_col + 0.5 * field_x, field_x) - 0.5 * field_x
        across = jnp.exp(-dist_x * dist_x * inverse_row).astype(bf16)
        for p in range(batch):
            shift_y = pos_ref[p, 1].astype(f32)
            dist_y = wrap(atom_y - shift_y - pixel_row + 0.5 * w, w) - 0.5 * w
            along = jnp.exp(-dist_y * dist_y * inverse_col)
            weighted = jnp.concatenate(
                [(cols[:, 3 + l : 4 + l] * along).astype(bf16) for l in range(layers)], 1
            )
            pot_ref[p] = dot(across, weighted)

    potentials()

    @pl.when(first)
    def _():
        for copy in copies:
            copy.wait()
        if carried:
            wave_ref[...] = last_ref[...]
        else:
            rows = dot(a_ref[...], last_ref[...]).astype(bf16)
            rows = jnp.concatenate([rows[:w], rows[w:]], 1)
            start = dot(rows, b_ref[...]).astype(bf16)
            for p in range(batch):
                wave_ref[p] = start

    pr = prop_ref[0]
    pi = prop_ref[1]
    def transmit(p, layer):
        def stage(_):
            psi = wave_ref[p]
            wr = psi[:, :w].astype(f32)
            wi = psi[:, w:].astype(f32)
            sv, cv = sincos(pot_ref[p, :, pl.ds(layer * w, w)])
            tr = (wr * cv - wi * sv).astype(bf16)
            ti = (wr * sv + wi * cv).astype(bf16)
            return jnp.concatenate([tr, ti], 1)
        return stage

    def rowwise(t):
        return dot(t, a_ref[...]).astype(bf16)

    def spectrum(rw):
        return dot(b_ref[...], jnp.concatenate([rw[:, :w], rw[:, w:]], 0))

    def propagate(sp):
        sr = sp[:w]
        si = sp[w:]
        return jnp.concatenate(
            [(sr * pr - si * pi).astype(bf16), (sr * pi + si * pr).astype(bf16)], 0
        )

    def back_rows(spb):
        return dot(a_ref[...], spb).astype(bf16)

    def store(p):
        def stage(br):
            wave_ref[p] = dot(jnp.concatenate([br[:w], br[w:]], 1), b_ref[...]).astype(bf16)
            return None
        return stage

    chains = [
        [
            stage
            for layer in range(layers)
            for stage in (transmit(p, layer), rowwise, spectrum, propagate, back_rows, store(p))
        ]
        for p in range(batch)
    ]
    values = [None] * batch
    length = len(chains[0])
    for t in range(length + batch - 1):
        for p in range(batch):
            k = t - p
            if 0 <= k < length:
                values[p] = chains[p][k](values[p])

    @pl.when(hop == pl.num_programs(0) - 1)
    def _():
        if final:
            for p in range(batch):
                out_ref[p, :, 0, :] = wave_ref[p, :, :w]
                out_ref[p, :, 1, :] = wave_ref[p, :, w:]
        else:
            out_ref[...] = wave_ref[...]


def run_slices(probe_pos, entry, amp, spread, packs, window, layers, field_x, cap, wave=None, final=False):
    batch = probe_pos.shape[0]
    hops = packs.shape[0]
    w = window
    a, b = dft_blocks(w)
    prop = propagator(w)
    full = lambda shape: pl.BlockSpec(shape, lambda h, *_: (0,) * len(shape))
    carried = wave is not None
    out_shape = (batch, w, 2, w) if final else (batch, w, 2 * w)
    last = wave if carried else jnp.asarray(start_spectrum(w))
    atoms = 3 * cap
    steps = batch * hops * layers
    flops = steps * 4 * 2 * w * (2 * w) * (2 * w) + batch * hops * 2 * w * atoms * layers * w
    return pl.pallas_call(
        functools.partial(slices_kernel, field_x=float(field_x), carried=carried, cap=cap, final=final),
        out_shape=jax.ShapeDtypeStruct(out_shape, jnp.bfloat16),
        grid_spec=pltpu.PrefetchScalarGridSpec(
            num_scalar_prefetch=2,
            grid=(hops,),
            in_specs=[
                pl.BlockSpec(memory_space=pltpu.SMEM),
                pl.BlockSpec(memory_space=pltpu.SMEM),
                pl.BlockSpec(memory_space=pltpu.VMEM),
                pl.BlockSpec(memory_space=pl.ANY),
                pl.BlockSpec(memory_space=pl.ANY),
                pl.BlockSpec(memory_space=pl.ANY),
                pl.BlockSpec(memory_space=pl.ANY),
            ],
            out_specs=full(out_shape),
            scratch_shapes=[
                pltpu.VMEM((batch, w, 2 * w), jnp.bfloat16),
                pltpu.VMEM((batch, w, layers * w), jnp.float32),
                pltpu.VMEM(a.shape, jnp.bfloat16),
                pltpu.VMEM(b.shape, jnp.bfloat16),
                pltpu.VMEM(prop.shape, jnp.float32),
                pltpu.VMEM(last.shape, jnp.bfloat16),
                pltpu.SemaphoreType.DMA((4,)),
            ],
        ),
        compiler_params=pltpu.CompilerParams(
            dimension_semantics=("arbitrary",),
        ),
        cost_estimate=pl.CostEstimate(
            flops=flops,
            transcendentals=steps * 2 * w * w + batch * hops * 2 * atoms * w,
            bytes_accessed=2 * (2 * w) ** 2 * 2 + 3 * w * w * 4 + batch * w * w * 4,
        ),
    )(probe_pos, entry, amp, spread, packs, jnp.asarray(a), jnp.asarray(b), jnp.asarray(prop), last)


def shards(atom_xy, atom_species, atom_slab, species_amp, species_spread, margin, probe_pos):
    layers = SL_DEV
    window = W
    atoms = atom_xy.shape[-1]
    cap = margin.shape[-1]
    n_lat = lax.axis_size("lat")
    owners = lax.axis_size("slc")
    field_x = n_lat * atoms * (2 * window // cap)
    f32 = jnp.float32
    raw = jnp.concatenate(
        [atom_xy[0, 0], atom_species[0, 0][None].astype(f32), atom_slab[0, 0][None].astype(f32)], 0
    )
    marg = jnp.transpose(margin[0, 0, :, 0], (1, 0, 2)).astype(f32)
    marg = jnp.pad(marg, ((0, 0), (0, 0), (0, atoms - cap)), constant_values=-1.0)
    packs = jnp.concatenate([jnp.broadcast_to(raw[None], (3,) + raw.shape), marg], 1)
    from_left = lax.ppermute(packs[2], "lat", [(i, (i + 1) % n_lat) for i in range(n_lat)])
    from_right = lax.ppermute(packs[0], "lat", [((i + 1) % n_lat, i) for i in range(n_lat)])
    local = jnp.stack([from_left, packs[1], from_right], 0)[None]
    me = lax.axis_index("slc")
    entry = jnp.reshape(me, (1,)).astype(jnp.int32)
    later = [
        lax.ppermute(local, "slc", [(i, (i - hop) % owners) for i in range(owners)])
        for hop in range(1, owners)
    ]
    batch = probe_pos.shape[0]
    wave = run_slices(probe_pos, entry, species_amp, species_spread, local, window, layers, field_x, cap, final=not later)
    if later:
        wave = run_slices(
            probe_pos, entry, species_amp, species_spread, jnp.concatenate(later, 0), window, layers, field_x, cap, wave,
            final=True,
        )
    return wave


def solution(mesh):
    in_specs = (
        P(("groups", "lat"), "slc", None, None),
        P(("groups", "lat"), "slc", None),
        P(("groups", "lat"), "slc", None),
        P(),
        P(),
        P(("groups", "lat"), "slc", None, "rep", None, None),
        P(("groups", "lat", "slc", "rep"), None),
    )
    out_specs = P(("groups", "lat", "slc", "rep"), None, None, None)
    return jax.shard_map(shards, mesh=mesh, in_specs=in_specs, out_specs=out_specs, check_vma=False)
```

```python
import functools
import math

import jax
import numpy as np
import jax.numpy as jnp
from jax import lax
from jax.experimental import pallas as pl
from jax.experimental.pallas import tpu as pltpu
from jax.sharding import PartitionSpec as P

W = 256
SL_DEV = 2


PROPAGATION_COEF = 0.001
DEFOCUS_COEF = 4.19


def centered_frequency(window):
    indices = np.arange(window, dtype=np.int32)
    return np.where(indices < window // 2, indices, indices - window).astype(np.float32)


def squared_radius(window):
    frequency = centered_frequency(window)
    return frequency[:, None] * frequency[:, None] + frequency[None, :] * frequency[None, :]


def dft_blocks(window):
    indices = np.arange(window, dtype=np.int32)
    product = indices[:, None] * indices[None, :] % window
    angle = np.float32(2.0 * math.pi / window) * product.astype(np.float32)
    scale = np.float32(math.sqrt(window))
    re = (np.cos(angle) / scale).astype(jnp.bfloat16)
    im = (np.sin(angle) / scale).astype(jnp.bfloat16)
    a = np.block([[re, -im], [im, re]])
    b = np.block([[re, im], [-im, re]])
    return a, b


def propagator(window):
    radius = squared_radius(window)
    inside = (np.float32(9.0) * radius < window * window).astype(np.float32)
    phase_angle = np.float32(-PROPAGATION_COEF * (65536.0 / (window * window))) * radius
    return np.stack([inside * np.cos(phase_angle), inside * np.sin(phase_angle)], 0)


def start_spectrum(window):
    radius = squared_radius(window)
    inside = (np.float32(16.0) * radius < window * window).astype(np.float32)
    norm_scale = np.float32(window) / np.sqrt(np.sum(inside, dtype=np.float32))
    phase_angle = np.float32(-(DEFOCUS_COEF / window)) * radius
    spectrum = np.concatenate(
        [inside * norm_scale * np.cos(phase_angle), inside * norm_scale * np.sin(phase_angle)], 0
    )
    return spectrum.astype(jnp.bfloat16)


def atom_fields(positions, species, slab, species_amp, species_spread, layers):
    species_match = (
        species[None, :] == jnp.arange(species_amp.shape[0], dtype=jnp.int32)[:, None]
    ).astype(species_amp.dtype)
    amplitude = jnp.sum(species_match * species_amp[:, None], 0)
    spread = jnp.sum(species_match * species_spread[:, None], 0)
    inverse = 0.5 / (spread * spread)
    slab_match = (slab[None, :] == jnp.arange(layers, dtype=jnp.int32)[:, None]).astype(
        amplitude.dtype
    )
    return jnp.concatenate([positions, inverse[None, :], slab_match * amplitude[None, :]], 0)


def pick_rows(fields, pick_list):
    valid_mask = (pick_list >= 0).astype(fields.dtype)
    safe_index = jnp.maximum(pick_list, 0)
    gathered = fields[:, safe_index]
    return jnp.concatenate([gathered[:3], gathered[3:] * valid_mask[None]], 0)


def wrap(value, period):
    return value - period * jnp.floor(value * (1.0 / period))


def sincos(v):
    q = jnp.floor(v * 0.6366197723675814 + 0.5)
    r = v - q * 1.5703125
    r = r - q * 4.837512969970703125e-4
    r = r - q * 7.549789954891882e-8
    z = r * r
    s = r + r * z * (-1.6666654611e-1 + z * (8.3321608736e-3 + z * -1.9515295891e-4))
    c = 1.0 - 0.5 * z + z * z * (4.166664568298827e-2 + z * (-1.388731625493765e-3 + z * 2.443315711809948e-5))
    n = q.astype(jnp.int32)
    swap = (n & 1) == 1
    sin_v = jnp.where(swap, c, s)
    cos_v = jnp.where(swap, s, c)
    sin_v = jnp.where((n & 2) == 2, -sin_v, sin_v)
    cos_v = jnp.where(((n + 1) & 2) == 2, -cos_v, cos_v)
    return sin_v, cos_v


def slices_kernel(*refs, field_x, carried, cap, final):
    (pos_ref, owner_ref, amp_ref, spread_ref, pk_ref, a_hbm, b_hbm, prop_hbm, last_hbm,
     out_ref, wave_ref, pot_ref, a_ref, b_ref, prop_ref, last_ref, sems) = refs
    batch = wave_ref.shape[0]
    w = prop_ref.shape[-1]
    layers = pot_ref.shape[-1] // w
    species_count = amp_ref.shape[0]
    hop = pl.program_id(0)
    f32, bf16 = jnp.float32, jnp.bfloat16

    def dot(a, b):
        return jnp.dot(a, b, preferred_element_type=f32)

    first = hop == 0
    copies = [
        pltpu.make_async_copy(src, dst, sems.at[k])
        for k, (src, dst) in enumerate(
            [(a_hbm, a_ref), (b_hbm, b_ref), (prop_hbm, prop_ref), (last_hbm, last_ref)]
        )
    ]

    @pl.when(first)
    def _():
        for copy in copies:
            copy.start()

    def potentials():
        entry = owner_ref[0]
        blocks = []
        for slot in range(3):
            raw = pk_ref[hop, slot, 0:4, :]
            listed = pk_ref[hop, slot, pl.ds(4 + entry, 1), :][:, :cap]
            species = raw[2:3]
            slab = raw[3:4]
            amplitude = jnp.zeros_like(species)
            spread = jnp.zeros_like(species)
            for k in range(species_count):
                match = species == float(k)
                amplitude = jnp.where(match, amp_ref[k], amplitude)
                spread = jnp.where(match, spread_ref[k], spread)
            inverse = 0.5 / (spread * spread)
            zero = jnp.zeros_like(species)
            per_layer = [jnp.where(slab == float(l), amplitude, zero) for l in range(layers)]
            fields = jnp.concatenate(
                [raw[0:2], inverse] + per_layer + [zero] * (8 - 3 - layers), 0
            )
            atoms = fields.shape[1]
            safe = jnp.maximum(listed, 0.0).astype(jnp.int32)
            onehot = (lax.broadcasted_iota(jnp.int32, (atoms, cap), 0) == safe).astype(f32)
            picked = jnp.dot(
                fields, onehot, preferred_element_type=f32, precision=lax.Precision.HIGHEST
            )
            valid = (listed >= 0.0).astype(f32)
            keep = lax.broadcasted_iota(jnp.int32, (8, 1), 0) < 3
            picked = jnp.where(keep, picked, picked * valid)
            blocks.append(picked)
        rows = jnp.concatenate(blocks, 1)
        cols = rows.T
        atom_x = rows[0:1]
        inverse_row = rows[2:3]
        atom_y = cols[:, 1:2]
        inverse_col = cols[:, 2:3]
        pixel_col = lax.broadcasted_iota(jnp.int32, (w, 1), 0).astype(f32)
        pixel_row = lax.broadcasted_iota(jnp.int32, (1, w), 1).astype(f32)
        shift_x = pos_ref[0, 0].astype(f32)
        dist_x = wrap(atom_x - shift_x - pixel_col + 0.5 * field_x, field_x) - 0.5 * field_x
        across = jnp.exp(-dist_x * dist_x * inverse_row).astype(bf16)
        shift_y = pos_ref[0, 1].astype(f32)
        dist_y = wrap(atom_y - shift_y - pixel_row + 0.5 * w, w) - 0.5 * w
        base = jnp.exp(-dist_y * dist_y * inverse_col)
        for p in range(batch):
            if p == 0:
                along = base
            else:
                turn = lax.rem(lax.rem(pos_ref[0, 1] - pos_ref[p, 1], w) + w, w)
                along = pltpu.roll(base, turn, 1)
            weighted = jnp.concatenate(
                [(cols[:, 3 + l : 4 + l] * along).astype(bf16) for l in range(layers)], 1
            )
            pot_ref[p] = dot(across, weighted)

    potentials()

    @pl.when(first)
    def _():
        for copy in copies:
            copy.wait()
        if carried:
            wave_ref[...] = last_ref[...]
        else:
            rows = dot(a_ref[...], last_ref[...]).astype(bf16)
            rows = jnp.concatenate([rows[:w], rows[w:]], 1)
            start = dot(rows, b_ref[...]).astype(bf16)
            for p in range(batch):
                wave_ref[p] = start

    pr = prop_ref[0]
    pi = prop_ref[1]
    for layer in range(layers):
        column = pl.ds(layer * w, w)
        transmitted = []
        for p in range(batch):
            psi = wave_ref[p]
            wr = psi[:, :w].astype(f32)
            wi = psi[:, w:].astype(f32)
            v = pot_ref[p, :, column]
            sv, cv = sincos(v)
            tr = (wr * cv - wi * sv).astype(bf16)
            ti = (wr * sv + wi * cv).astype(bf16)
            transmitted.append(jnp.concatenate([tr, ti], 1))
        rowwise = [dot(t, a_ref[...]).astype(bf16) for t in transmitted]
        spectra = [dot(b_ref[...], jnp.concatenate([rw[:, :w], rw[:, w:]], 0)) for rw in rowwise]
        propagated = []
        for sp in spectra:
            sr = sp[:w]
            si = sp[w:]
            propagated.append(
                jnp.concatenate([(sr * pr - si * pi).astype(bf16), (sr * pi + si * pr).astype(bf16)], 0)
            )
        back = [dot(a_ref[...], spb).astype(bf16) for spb in propagated]
        for p, br in enumerate(back):
            wave_ref[p] = dot(jnp.concatenate([br[:w], br[w:]], 1), b_ref[...]).astype(bf16)

    @pl.when(hop == pl.num_programs(0) - 1)
    def _():
        if final:
            for p in range(batch):
                out_ref[p, :, 0, :] = wave_ref[p, :, :w]
                out_ref[p, :, 1, :] = wave_ref[p, :, w:]
        else:
            out_ref[...] = wave_ref[...]


def run_slices(probe_pos, entry, amp, spread, packs, window, layers, field_x, cap, wave=None, final=False):
    batch = probe_pos.shape[0]
    hops = packs.shape[0]
    w = window
    a, b = dft_blocks(w)
    prop = propagator(w)
    full = lambda shape: pl.BlockSpec(shape, lambda h, *_: (0,) * len(shape))
    carried = wave is not None
    out_shape = (batch, w, 2, w) if final else (batch, w, 2 * w)
    last = wave if carried else jnp.asarray(start_spectrum(w))
    atoms = 3 * cap
    steps = batch * hops * layers
    flops = steps * 4 * 2 * w * (2 * w) * (2 * w) + batch * hops * 2 * w * atoms * layers * w
    return pl.pallas_call(
        functools.partial(slices_kernel, field_x=float(field_x), carried=carried, cap=cap, final=final),
        out_shape=jax.ShapeDtypeStruct(out_shape, jnp.bfloat16),
        grid_spec=pltpu.PrefetchScalarGridSpec(
            num_scalar_prefetch=2,
            grid=(hops,),
            in_specs=[
                pl.BlockSpec(memory_space=pltpu.SMEM),
                pl.BlockSpec(memory_space=pltpu.SMEM),
                pl.BlockSpec(memory_space=pltpu.VMEM),
                pl.BlockSpec(memory_space=pl.ANY),
                pl.BlockSpec(memory_space=pl.ANY),
                pl.BlockSpec(memory_space=pl.ANY),
                pl.BlockSpec(memory_space=pl.ANY),
            ],
            out_specs=full(out_shape),
            scratch_shapes=[
                pltpu.VMEM((batch, w, 2 * w), jnp.bfloat16),
                pltpu.VMEM((batch, w, layers * w), jnp.float32),
                pltpu.VMEM(a.shape, jnp.bfloat16),
                pltpu.VMEM(b.shape, jnp.bfloat16),
                pltpu.VMEM(prop.shape, jnp.float32),
                pltpu.VMEM(last.shape, jnp.bfloat16),
                pltpu.SemaphoreType.DMA((4,)),
            ],
        ),
        compiler_params=pltpu.CompilerParams(
            dimension_semantics=("arbitrary",),
        ),
        cost_estimate=pl.CostEstimate(
            flops=flops,
            transcendentals=steps * 2 * w * w + batch * hops * 2 * atoms * w,
            bytes_accessed=2 * (2 * w) ** 2 * 2 + 3 * w * w * 4 + batch * w * w * 4,
        ),
    )(probe_pos, entry, amp, spread, packs, jnp.asarray(a), jnp.asarray(b), jnp.asarray(prop), last)


def shards(atom_xy, atom_species, atom_slab, species_amp, species_spread, margin, probe_pos):
    layers = SL_DEV
    window = W
    atoms = atom_xy.shape[-1]
    cap = margin.shape[-1]
    n_lat = lax.axis_size("lat")
    owners = lax.axis_size("slc")
    field_x = n_lat * atoms * (2 * window // cap)
    f32 = jnp.float32
    raw = jnp.concatenate(
        [atom_xy[0, 0], atom_species[0, 0][None].astype(f32), atom_slab[0, 0][None].astype(f32)], 0
    )
    marg = jnp.transpose(margin[0, 0, :, 0], (1, 0, 2)).astype(f32)
    marg = jnp.pad(marg, ((0, 0), (0, 0), (0, atoms - cap)), constant_values=-1.0)
    packs = jnp.concatenate([jnp.broadcast_to(raw[None], (3,) + raw.shape), marg], 1)
    from_left = lax.ppermute(packs[2], "lat", [(i, (i + 1) % n_lat) for i in range(n_lat)])
    from_right = lax.ppermute(packs[0], "lat", [((i + 1) % n_lat, i) for i in range(n_lat)])
    local = jnp.stack([from_left, packs[1], from_right], 0)[None]
    me = lax.axis_index("slc")
    entry = jnp.reshape(me, (1,)).astype(jnp.int32)
    later = [
        lax.ppermute(local, "slc", [(i, (i - hop) % owners) for i in range(owners)])
        for hop in range(1, owners)
    ]
    batch = probe_pos.shape[0]
    wave = run_slices(probe_pos, entry, species_amp, species_spread, local, window, layers, field_x, cap, final=not later)
    if later:
        wave = run_slices(
            probe_pos, entry, species_amp, species_spread, jnp.concatenate(later, 0), window, layers, field_x, cap, wave,
            final=True,
        )
    return wave


def solution(mesh):
    in_specs = (
        P(("groups", "lat"), "slc", None, None),
        P(("groups", "lat"), "slc", None),
        P(("groups", "lat"), "slc", None),
        P(),
        P(),
        P(("groups", "lat"), "slc", None, "rep", None, None),
        P(("groups", "lat", "slc", "rep"), None),
    )
    out_specs = P(("groups", "lat", "slc", "rep"), None, None, None)
    return jax.shard_map(shards, mesh=mesh, in_specs=in_specs, out_specs=out_specs, check_vma=False)
```

```python
import functools
import math

import jax
import numpy as np
import jax.numpy as jnp
from jax import lax
from jax.experimental import pallas as pl
from jax.experimental.pallas import tpu as pltpu
from jax.sharding import PartitionSpec as P

W = 256
SL_DEV = 2


PROPAGATION_COEF = 0.001
DEFOCUS_COEF = 4.19


def centered_frequency(window):
    indices = np.arange(window, dtype=np.int32)
    return np.where(indices < window // 2, indices, indices - window).astype(np.float32)


def squared_radius(window):
    frequency = centered_frequency(window)
    return frequency[:, None] * frequency[:, None] + frequency[None, :] * frequency[None, :]


def dft_blocks(window):
    indices = np.arange(window, dtype=np.int32)
    product = indices[:, None] * indices[None, :] % window
    angle = np.float32(2.0 * math.pi / window) * product.astype(np.float32)
    scale = np.float32(math.sqrt(window))
    re = (np.cos(angle) / scale).astype(jnp.bfloat16)
    im = (np.sin(angle) / scale).astype(jnp.bfloat16)
    a = np.block([[re, -im], [im, re]])
    b = np.block([[re, im], [-im, re]])
    return a, b


def propagator(window):
    radius = squared_radius(window)
    inside = (np.float32(9.0) * radius < window * window).astype(np.float32)
    phase_angle = np.float32(-PROPAGATION_COEF * (65536.0 / (window * window))) * radius
    return np.stack([inside * np.cos(phase_angle), inside * np.sin(phase_angle)], 0)


def start_spectrum(window):
    radius = squared_radius(window)
    inside = (np.float32(16.0) * radius < window * window).astype(np.float32)
    norm_scale = np.float32(window) / np.sqrt(np.sum(inside, dtype=np.float32))
    phase_angle = np.float32(-(DEFOCUS_COEF / window)) * radius
    spectrum = np.concatenate(
        [inside * norm_scale * np.cos(phase_angle), inside * norm_scale * np.sin(phase_angle)], 0
    )
    return spectrum.astype(jnp.bfloat16)


def atom_fields(positions, species, slab, species_amp, species_spread, layers):
    species_match = (
        species[None, :] == jnp.arange(species_amp.shape[0], dtype=jnp.int32)[:, None]
    ).astype(species_amp.dtype)
    amplitude = jnp.sum(species_match * species_amp[:, None], 0)
    spread = jnp.sum(species_match * species_spread[:, None], 0)
    inverse = 0.5 / (spread * spread)
    slab_match = (slab[None, :] == jnp.arange(layers, dtype=jnp.int32)[:, None]).astype(
        amplitude.dtype
    )
    return jnp.concatenate([positions, inverse[None, :], slab_match * amplitude[None, :]], 0)


def pick_rows(fields, pick_list):
    valid_mask = (pick_list >= 0).astype(fields.dtype)
    safe_index = jnp.maximum(pick_list, 0)
    gathered = fields[:, safe_index]
    return jnp.concatenate([gathered[:3], gathered[3:] * valid_mask[None]], 0)


def wrap(value, period):
    return value - period * jnp.floor(value * (1.0 / period))


def sincos(v):
    q = jnp.floor(v * 0.6366197723675814 + 0.5)
    r = v - q * 1.5703125
    r = r - q * 4.837512969970703125e-4
    r = r - q * 7.549789954891882e-8
    z = r * r
    s = r + r * z * (-1.6666654611e-1 + z * (8.3321608736e-3 + z * -1.9515295891e-4))
    c = 1.0 - 0.5 * z + z * z * (4.166664568298827e-2 + z * (-1.388731625493765e-3 + z * 2.443315711809948e-5))
    n = q.astype(jnp.int32)
    swap = (n & 1) == 1
    sin_v = jnp.where(swap, c, s)
    cos_v = jnp.where(swap, s, c)
    sin_v = jnp.where((n & 2) == 2, -sin_v, sin_v)
    cos_v = jnp.where(((n + 1) & 2) == 2, -cos_v, cos_v)
    return sin_v, cos_v


def slices_kernel(*refs, field_x, carried, cap, final):
    (pos_ref, owner_ref, amp_ref, spread_ref, pk_ref, a_hbm, b_hbm, prop_hbm, last_hbm,
     out_ref, wave_ref, pot_ref, a_ref, b_ref, prop_ref, last_ref, sems) = refs
    batch = wave_ref.shape[0]
    w = prop_ref.shape[-1]
    layers = pot_ref.shape[-1] // w
    species_count = amp_ref.shape[0]
    hop = pl.program_id(0)
    f32, bf16 = jnp.float32, jnp.bfloat16

    def dot(a, b):
        return jnp.dot(a, b, preferred_element_type=f32)

    first = hop == 0
    copies = [
        pltpu.make_async_copy(src, dst, sems.at[k])
        for k, (src, dst) in enumerate(
            [(a_hbm, a_ref), (b_hbm, b_ref), (prop_hbm, prop_ref), (last_hbm, last_ref)]
        )
    ]

    @pl.when(first)
    def _():
        for copy in copies:
            copy.start()

    def potentials():
        entry = owner_ref[0]
        blocks = []
        for slot in range(3):
            raw = pk_ref[hop, slot, 0:4, :]
            listed = pk_ref[hop, slot, pl.ds(4 + entry, 1), :][:, :cap]
            species = raw[2:3]
            slab = raw[3:4]
            amplitude = jnp.zeros_like(species)
            spread = jnp.zeros_like(species)
            for k in range(species_count):
                match = species == float(k)
                amplitude = jnp.where(match, amp_ref[k], amplitude)
                spread = jnp.where(match, spread_ref[k], spread)
            inverse = 0.5 / (spread * spread)
            zero = jnp.zeros_like(species)
            per_layer = [jnp.where(slab == float(l), amplitude, zero) for l in range(layers)]
            fields = jnp.concatenate(
                [raw[0:2], inverse] + per_layer + [zero] * (8 - 3 - layers), 0
            )
            atoms = fields.shape[1]
            safe = jnp.maximum(listed, 0.0).astype(jnp.int32)
            onehot = (lax.broadcasted_iota(jnp.int32, (atoms, cap), 0) == safe).astype(f32)
            picked = jnp.dot(
                fields, onehot, preferred_element_type=f32, precision=lax.Precision.HIGHEST
            )
            valid = (listed >= 0.0).astype(f32)
            keep = lax.broadcasted_iota(jnp.int32, (8, 1), 0) < 3
            picked = jnp.where(keep, picked, picked * valid)
            blocks.append(picked)
        rows = jnp.concatenate(blocks, 1)
        cols = rows.T
        atom_x = rows[0:1]
        inverse_row = rows[2:3]
        atom_y = cols[:, 1:2]
        inverse_col = cols[:, 2:3]
        pixel_col = lax.broadcasted_iota(jnp.int32, (w, 1), 0).astype(f32)
        pixel_row = lax.broadcasted_iota(jnp.int32, (1, w), 1).astype(f32)
        shift_x = pos_ref[0, 0].astype(f32)
        dist_x = wrap(atom_x - shift_x - pixel_col + 0.5 * field_x, field_x) - 0.5 * field_x
        across = jnp.exp(dist_x * dist_x * -inverse_row).astype(bf16)
        for p in range(batch):
            shift_y = pos_ref[p, 1].astype(f32)
            dist_y = wrap(atom_y - shift_y - pixel_row + 0.5 * w, w) - 0.5 * w
            along = jnp.exp(dist_y * dist_y * -inverse_col)
            weighted = jnp.concatenate(
                [(cols[:, 3 + l : 4 + l] * along).astype(bf16) for l in range(layers)], 1
            )
            pot_ref[p] = dot(across, weighted)

    potentials()

    @pl.when(first)
    def _():
        for copy in copies:
            copy.wait()
        if carried:
            wave_ref[...] = last_ref[...]
        else:
            rows = dot(a_ref[...], last_ref[...]).astype(bf16)
            rows = jnp.concatenate([rows[:w], rows[w:]], 1)
            start = dot(rows, b_ref[...]).astype(bf16)
            for p in range(batch):
                wave_ref[p] = start

    pr = prop_ref[0]
    pi = prop_ref[1]
    for layer in range(layers):
        column = pl.ds(layer * w, w)
        transmitted = []
        for p in range(batch):
            psi = wave_ref[p]
            wr = psi[:, :w].astype(f32)
            wi = psi[:, w:].astype(f32)
            v = pot_ref[p, :, column]
            sv, cv = sincos(v)
            tr = (wr * cv - wi * sv).astype(bf16)
            ti = (wr * sv + wi * cv).astype(bf16)
            transmitted.append(jnp.concatenate([tr, ti], 1))
        rowwise = [dot(t, a_ref[...]).astype(bf16) for t in transmitted]
        spectra = [dot(b_ref[...], jnp.concatenate([rw[:, :w], rw[:, w:]], 0)) for rw in rowwise]
        propagated = []
        for sp in spectra:
            sr = sp[:w]
            si = sp[w:]
            propagated.append(
                jnp.concatenate([(sr * pr - si * pi).astype(bf16), (sr * pi + si * pr).astype(bf16)], 0)
            )
        back = [dot(a_ref[...], spb).astype(bf16) for spb in propagated]
        for p, br in enumerate(back):
            wave_ref[p] = dot(jnp.concatenate([br[:w], br[w:]], 1), b_ref[...]).astype(bf16)

    @pl.when(hop == pl.num_programs(0) - 1)
    def _():
        if final:
            for p in range(batch):
                out_ref[p, :, 0, :] = wave_ref[p, :, :w]
                out_ref[p, :, 1, :] = wave_ref[p, :, w:]
        else:
            out_ref[...] = wave_ref[...]


def run_slices(probe_pos, entry, amp, spread, packs, window, layers, field_x, cap, wave=None, final=False):
    batch = probe_pos.shape[0]
    hops = packs.shape[0]
    w = window
    a, b = dft_blocks(w)
    prop = propagator(w)
    full = lambda shape: pl.BlockSpec(shape, lambda h, *_: (0,) * len(shape))
    carried = wave is not None
    out_shape = (batch, w, 2, w) if final else (batch, w, 2 * w)
    last = wave if carried else jnp.asarray(start_spectrum(w))
    atoms = 3 * cap
    steps = batch * hops * layers
    flops = steps * 4 * 2 * w * (2 * w) * (2 * w) + batch * hops * 2 * w * atoms * layers * w
    return pl.pallas_call(
        functools.partial(slices_kernel, field_x=float(field_x), carried=carried, cap=cap, final=final),
        out_shape=jax.ShapeDtypeStruct(out_shape, jnp.bfloat16),
        grid_spec=pltpu.PrefetchScalarGridSpec(
            num_scalar_prefetch=2,
            grid=(hops,),
            in_specs=[
                pl.BlockSpec(memory_space=pltpu.SMEM),
                pl.BlockSpec(memory_space=pltpu.SMEM),
                pl.BlockSpec(memory_space=pltpu.VMEM),
                pl.BlockSpec(memory_space=pl.ANY),
                pl.BlockSpec(memory_space=pl.ANY),
                pl.BlockSpec(memory_space=pl.ANY),
                pl.BlockSpec(memory_space=pl.ANY),
            ],
            out_specs=full(out_shape),
            scratch_shapes=[
                pltpu.VMEM((batch, w, 2 * w), jnp.bfloat16),
                pltpu.VMEM((batch, w, layers * w), jnp.float32),
                pltpu.VMEM(a.shape, jnp.bfloat16),
                pltpu.VMEM(b.shape, jnp.bfloat16),
                pltpu.VMEM(prop.shape, jnp.float32),
                pltpu.VMEM(last.shape, jnp.bfloat16),
                pltpu.SemaphoreType.DMA((4,)),
            ],
        ),
        compiler_params=pltpu.CompilerParams(
            dimension_semantics=("arbitrary",),
        ),
        cost_estimate=pl.CostEstimate(
            flops=flops,
            transcendentals=steps * 2 * w * w + batch * hops * 2 * atoms * w,
            bytes_accessed=2 * (2 * w) ** 2 * 2 + 3 * w * w * 4 + batch * w * w * 4,
        ),
    )(probe_pos, entry, amp, spread, packs, jnp.asarray(a), jnp.asarray(b), jnp.asarray(prop), last)


def shards(atom_xy, atom_species, atom_slab, species_amp, species_spread, margin, probe_pos):
    layers = SL_DEV
    window = W
    atoms = atom_xy.shape[-1]
    cap = margin.shape[-1]
    n_lat = lax.axis_size("lat")
    owners = lax.axis_size("slc")
    field_x = n_lat * atoms * (2 * window // cap)
    f32 = jnp.float32
    raw = jnp.concatenate(
        [atom_xy[0, 0], atom_species[0, 0][None].astype(f32), atom_slab[0, 0][None].astype(f32)], 0
    )
    marg = jnp.transpose(margin[0, 0, :, 0], (1, 0, 2)).astype(f32)
    marg = jnp.pad(marg, ((0, 0), (0, 0), (0, atoms - cap)), constant_values=-1.0)
    packs = jnp.concatenate([jnp.broadcast_to(raw[None], (3,) + raw.shape), marg], 1)
    from_left = lax.ppermute(packs[2], "lat", [(i, (i + 1) % n_lat) for i in range(n_lat)])
    from_right = lax.ppermute(packs[0], "lat", [((i + 1) % n_lat, i) for i in range(n_lat)])
    local = jnp.stack([from_left, packs[1], from_right], 0)[None]
    me = lax.axis_index("slc")
    entry = jnp.reshape(me, (1,)).astype(jnp.int32)
    later = [
        lax.ppermute(local, "slc", [(i, (i - hop) % owners) for i in range(owners)])
        for hop in range(1, owners)
    ]
    batch = probe_pos.shape[0]
    wave = run_slices(probe_pos, entry, species_amp, species_spread, local, window, layers, field_x, cap, final=not later)
    if later:
        wave = run_slices(
            probe_pos, entry, species_amp, species_spread, jnp.concatenate(later, 0), window, layers, field_x, cap, wave,
            final=True,
        )
    return wave


def solution(mesh):
    in_specs = (
        P(("groups", "lat"), "slc", None, None),
        P(("groups", "lat"), "slc", None),
        P(("groups", "lat"), "slc", None),
        P(),
        P(),
        P(("groups", "lat"), "slc", None, "rep", None, None),
        P(("groups", "lat", "slc", "rep"), None),
    )
    out_specs = P(("groups", "lat", "slc", "rep"), None, None, None)
    return jax.shard_map(shards, mesh=mesh, in_specs=in_specs, out_specs=out_specs, check_vma=False)
```

```python
import functools
import math

import jax
import numpy as np
import jax.numpy as jnp
from jax import lax
from jax.experimental import pallas as pl
from jax.experimental.pallas import tpu as pltpu
from jax.sharding import PartitionSpec as P

W = 256
SL_DEV = 2


PROPAGATION_COEF = 0.001
DEFOCUS_COEF = 4.19


def centered_frequency(window):
    indices = np.arange(window, dtype=np.int32)
    return np.where(indices < window // 2, indices, indices - window).astype(np.float32)


def squared_radius(window):
    frequency = centered_frequency(window)
    return frequency[:, None] * frequency[:, None] + frequency[None, :] * frequency[None, :]


def dft_blocks(window):
    indices = np.arange(window, dtype=np.int32)
    product = indices[:, None] * indices[None, :] % window
    angle = np.float32(2.0 * math.pi / window) * product.astype(np.float32)
    scale = np.float32(math.sqrt(window))
    re = (np.cos(angle) / scale).astype(jnp.bfloat16)
    im = (np.sin(angle) / scale).astype(jnp.bfloat16)
    a = np.block([[re, -im], [im, re]])
    b = np.block([[re, im], [-im, re]])
    return a, b


def propagator(window):
    radius = squared_radius(window)
    inside = (np.float32(9.0) * radius < window * window).astype(np.float32)
    phase_angle = np.float32(-PROPAGATION_COEF * (65536.0 / (window * window))) * radius
    return np.stack([inside * np.cos(phase_angle), inside * np.sin(phase_angle)], 0)


def start_spectrum(window):
    radius = squared_radius(window)
    inside = (np.float32(16.0) * radius < window * window).astype(np.float32)
    norm_scale = np.float32(window) / np.sqrt(np.sum(inside, dtype=np.float32))
    phase_angle = np.float32(-(DEFOCUS_COEF / window)) * radius
    spectrum = np.concatenate(
        [inside * norm_scale * np.cos(phase_angle), inside * norm_scale * np.sin(phase_angle)], 0
    )
    return spectrum.astype(jnp.bfloat16)


def atom_fields(positions, species, slab, species_amp, species_spread, layers):
    species_match = (
        species[None, :] == jnp.arange(species_amp.shape[0], dtype=jnp.int32)[:, None]
    ).astype(species_amp.dtype)
    amplitude = jnp.sum(species_match * species_amp[:, None], 0)
    spread = jnp.sum(species_match * species_spread[:, None], 0)
    inverse = 0.5 / (spread * spread)
    slab_match = (slab[None, :] == jnp.arange(layers, dtype=jnp.int32)[:, None]).astype(
        amplitude.dtype
    )
    return jnp.concatenate([positions, inverse[None, :], slab_match * amplitude[None, :]], 0)


def pick_rows(fields, pick_list):
    valid_mask = (pick_list >= 0).astype(fields.dtype)
    safe_index = jnp.maximum(pick_list, 0)
    gathered = fields[:, safe_index]
    return jnp.concatenate([gathered[:3], gathered[3:] * valid_mask[None]], 0)


def centered(value, period):
    return value - period * jnp.floor((value + 0.5 * period) * (1.0 / period))


def sincos(v):
    q = jnp.floor(v * 0.6366197723675814 + 0.5)
    r = v - q * 1.5703125
    r = r - q * 4.837512969970703125e-4
    r = r - q * 7.549789954891882e-8
    z = r * r
    s = r + r * z * (-1.6666654611e-1 + z * (8.3321608736e-3 + z * -1.9515295891e-4))
    c = 1.0 - 0.5 * z + z * z * (4.166664568298827e-2 + z * (-1.388731625493765e-3 + z * 2.443315711809948e-5))
    n = q.astype(jnp.int32)
    swap = (n & 1) == 1
    sin_v = jnp.where(swap, c, s)
    cos_v = jnp.where(swap, s, c)
    sin_v = jnp.where((n & 2) == 2, -sin_v, sin_v)
    cos_v = jnp.where(((n + 1) & 2) == 2, -cos_v, cos_v)
    return sin_v, cos_v


def slices_kernel(*refs, field_x, carried, cap, final):
    (pos_ref, owner_ref, amp_ref, spread_ref, pk_ref, a_hbm, b_hbm, prop_hbm, last_hbm,
     out_ref, wave_ref, pot_ref, a_ref, b_ref, prop_ref, last_ref, sems) = refs
    batch = wave_ref.shape[0]
    w = prop_ref.shape[-1]
    layers = pot_ref.shape[-1] // w
    species_count = amp_ref.shape[0]
    hop = pl.program_id(0)
    f32, bf16 = jnp.float32, jnp.bfloat16

    def dot(a, b):
        return jnp.dot(a, b, preferred_element_type=f32)

    first = hop == 0
    copies = [
        pltpu.make_async_copy(src, dst, sems.at[k])
        for k, (src, dst) in enumerate(
            [(a_hbm, a_ref), (b_hbm, b_ref), (prop_hbm, prop_ref), (last_hbm, last_ref)]
        )
    ]

    @pl.when(first)
    def _():
        for copy in copies:
            copy.start()

    def potentials():
        entry = owner_ref[0]
        blocks = []
        for slot in range(3):
            raw = pk_ref[hop, slot, 0:4, :]
            listed = pk_ref[hop, slot, pl.ds(4 + entry, 1), :][:, :cap]
            species = raw[2:3]
            slab = raw[3:4]
            amplitude = jnp.zeros_like(species)
            spread = jnp.zeros_like(species)
            for k in range(species_count):
                match = species == float(k)
                amplitude = jnp.where(match, amp_ref[k], amplitude)
                spread = jnp.where(match, spread_ref[k], spread)
            inverse = 0.5 / (spread * spread)
            zero = jnp.zeros_like(species)
            per_layer = [jnp.where(slab == float(l), amplitude, zero) for l in range(layers)]
            fields = jnp.concatenate(
                [raw[0:2], inverse] + per_layer + [zero] * (8 - 3 - layers), 0
            )
            atoms = fields.shape[1]
            safe = jnp.maximum(listed, 0.0).astype(jnp.int32)
            onehot = (lax.broadcasted_iota(jnp.int32, (atoms, cap), 0) == safe).astype(f32)
            picked = jnp.dot(
                fields, onehot, preferred_element_type=f32, precision=lax.Precision.HIGHEST
            )
            valid = (listed >= 0.0).astype(f32)
            keep = lax.broadcasted_iota(jnp.int32, (8, 1), 0) < 3
            picked = jnp.where(keep, picked, picked * valid)
            blocks.append(picked)
        rows = jnp.concatenate(blocks, 1)
        cols = rows.T
        atom_x = rows[0:1]
        inverse_row = rows[2:3]
        atom_y = cols[:, 1:2]
        inverse_col = cols[:, 2:3]
        pixel_col = lax.broadcasted_iota(jnp.int32, (w, 1), 0).astype(f32)
        pixel_row = lax.broadcasted_iota(jnp.int32, (1, w), 1).astype(f32)
        shift_x = pos_ref[0, 0].astype(f32)
        dist_x = centered(atom_x - shift_x - pixel_col, field_x)
        across = jnp.exp(dist_x * dist_x * -inverse_row).astype(bf16)
        for p in range(batch):
            shift_y = pos_ref[p, 1].astype(f32)
            dist_y = centered(atom_y - shift_y - pixel_row, w)
            along = jnp.exp(dist_y * dist_y * -inverse_col)
            weighted = jnp.concatenate(
                [(cols[:, 3 + l : 4 + l] * along).astype(bf16) for l in range(layers)], 1
            )
            pot_ref[p] = dot(across, weighted)

    potentials()

    @pl.when(first)
    def _():
        for copy in copies:
            copy.wait()
        if carried:
            wave_ref[...] = last_ref[...]
        else:
            rows = dot(a_ref[...], last_ref[...]).astype(bf16)
            rows = jnp.concatenate([rows[:w], rows[w:]], 1)
            start = dot(rows, b_ref[...]).astype(bf16)
            for p in range(batch):
                wave_ref[p] = start

    pr = prop_ref[0]
    pi = prop_ref[1]
    for layer in range(layers):
        column = pl.ds(layer * w, w)
        transmitted = []
        for p in range(batch):
            psi = wave_ref[p]
            wr = psi[:, :w].astype(f32)
            wi = psi[:, w:].astype(f32)
            v = pot_ref[p, :, column]
            sv, cv = sincos(v)
            tr = (wr * cv - wi * sv).astype(bf16)
            ti = (wr * sv + wi * cv).astype(bf16)
            transmitted.append(jnp.concatenate([tr, ti], 1))
        rowwise = [dot(t, a_ref[...]).astype(bf16) for t in transmitted]
        spectra = [dot(b_ref[...], jnp.concatenate([rw[:, :w], rw[:, w:]], 0)) for rw in rowwise]
        propagated = []
        for sp in spectra:
            sr = sp[:w]
            si = sp[w:]
            propagated.append(
                jnp.concatenate([(sr * pr - si * pi).astype(bf16), (sr * pi + si * pr).astype(bf16)], 0)
            )
        back = [dot(a_ref[...], spb).astype(bf16) for spb in propagated]
        for p, br in enumerate(back):
            wave_ref[p] = dot(jnp.concatenate([br[:w], br[w:]], 1), b_ref[...]).astype(bf16)

    @pl.when(hop == pl.num_programs(0) - 1)
    def _():
        if final:
            for p in range(batch):
                out_ref[p, :, 0, :] = wave_ref[p, :, :w]
                out_ref[p, :, 1, :] = wave_ref[p, :, w:]
        else:
            out_ref[...] = wave_ref[...]


def run_slices(probe_pos, entry, amp, spread, packs, window, layers, field_x, cap, wave=None, final=False):
    batch = probe_pos.shape[0]
    hops = packs.shape[0]
    w = window
    a, b = dft_blocks(w)
    prop = propagator(w)
    full = lambda shape: pl.BlockSpec(shape, lambda h, *_: (0,) * len(shape))
    carried = wave is not None
    out_shape = (batch, w, 2, w) if final else (batch, w, 2 * w)
    last = wave if carried else jnp.asarray(start_spectrum(w))
    atoms = 3 * cap
    steps = batch * hops * layers
    flops = steps * 4 * 2 * w * (2 * w) * (2 * w) + batch * hops * 2 * w * atoms * layers * w
    return pl.pallas_call(
        functools.partial(slices_kernel, field_x=float(field_x), carried=carried, cap=cap, final=final),
        out_shape=jax.ShapeDtypeStruct(out_shape, jnp.bfloat16),
        grid_spec=pltpu.PrefetchScalarGridSpec(
            num_scalar_prefetch=2,
            grid=(hops,),
            in_specs=[
                pl.BlockSpec(memory_space=pltpu.SMEM),
                pl.BlockSpec(memory_space=pltpu.SMEM),
                pl.BlockSpec(memory_space=pltpu.VMEM),
                pl.BlockSpec(memory_space=pl.ANY),
                pl.BlockSpec(memory_space=pl.ANY),
                pl.BlockSpec(memory_space=pl.ANY),
                pl.BlockSpec(memory_space=pl.ANY),
            ],
            out_specs=full(out_shape),
            scratch_shapes=[
                pltpu.VMEM((batch, w, 2 * w), jnp.bfloat16),
                pltpu.VMEM((batch, w, layers * w), jnp.float32),
                pltpu.VMEM(a.shape, jnp.bfloat16),
                pltpu.VMEM(b.shape, jnp.bfloat16),
                pltpu.VMEM(prop.shape, jnp.float32),
                pltpu.VMEM(last.shape, jnp.bfloat16),
                pltpu.SemaphoreType.DMA((4,)),
            ],
        ),
        compiler_params=pltpu.CompilerParams(
            dimension_semantics=("arbitrary",),
        ),
        cost_estimate=pl.CostEstimate(
            flops=flops,
            transcendentals=steps * 2 * w * w + batch * hops * 2 * atoms * w,
            bytes_accessed=2 * (2 * w) ** 2 * 2 + 3 * w * w * 4 + batch * w * w * 4,
        ),
    )(probe_pos, entry, amp, spread, packs, jnp.asarray(a), jnp.asarray(b), jnp.asarray(prop), last)


def shards(atom_xy, atom_species, atom_slab, species_amp, species_spread, margin, probe_pos):
    layers = SL_DEV
    window = W
    atoms = atom_xy.shape[-1]
    cap = margin.shape[-1]
    n_lat = lax.axis_size("lat")
    owners = lax.axis_size("slc")
    field_x = n_lat * atoms * (2 * window // cap)
    f32 = jnp.float32
    raw = jnp.concatenate(
        [atom_xy[0, 0], atom_species[0, 0][None].astype(f32), atom_slab[0, 0][None].astype(f32)], 0
    )
    marg = jnp.transpose(margin[0, 0, :, 0], (1, 0, 2)).astype(f32)
    marg = jnp.pad(marg, ((0, 0), (0, 0), (0, atoms - cap)), constant_values=-1.0)
    packs = jnp.concatenate([jnp.broadcast_to(raw[None], (3,) + raw.shape), marg], 1)
    from_left = lax.ppermute(packs[2], "lat", [(i, (i + 1) % n_lat) for i in range(n_lat)])
    from_right = lax.ppermute(packs[0], "lat", [((i + 1) % n_lat, i) for i in range(n_lat)])
    local = jnp.stack([from_left, packs[1], from_right], 0)[None]
    me = lax.axis_index("slc")
    entry = jnp.reshape(me, (1,)).astype(jnp.int32)
    later = [
        lax.ppermute(local, "slc", [(i, (i - hop) % owners) for i in range(owners)])
        for hop in range(1, owners)
    ]
    batch = probe_pos.shape[0]
    wave = run_slices(probe_pos, entry, species_amp, species_spread, local, window, layers, field_x, cap, final=not later)
    if later:
        wave = run_slices(
            probe_pos, entry, species_amp, species_spread, jnp.concatenate(later, 0), window, layers, field_x, cap, wave,
            final=True,
        )
    return wave


def solution(mesh):
    in_specs = (
        P(("groups", "lat"), "slc", None, None),
        P(("groups", "lat"), "slc", None),
        P(("groups", "lat"), "slc", None),
        P(),
        P(),
        P(("groups", "lat"), "slc", None, "rep", None, None),
        P(("groups", "lat", "slc", "rep"), None),
    )
    out_specs = P(("groups", "lat", "slc", "rep"), None, None, None)
    return jax.shard_map(shards, mesh=mesh, in_specs=in_specs, out_specs=out_specs, check_vma=False)
```

```python
import functools
import math

import jax
import numpy as np
import jax.numpy as jnp
from jax import lax
from jax.experimental import pallas as pl
from jax.experimental.pallas import tpu as pltpu
from jax.sharding import PartitionSpec as P

W = 256
SL_DEV = 2


PROPAGATION_COEF = 0.001
DEFOCUS_COEF = 4.19


def centered_frequency(window):
    indices = np.arange(window, dtype=np.int32)
    return np.where(indices < window // 2, indices, indices - window).astype(np.float32)


def squared_radius(window):
    frequency = centered_frequency(window)
    return frequency[:, None] * frequency[:, None] + frequency[None, :] * frequency[None, :]


def dft_blocks(window):
    indices = np.arange(window, dtype=np.int32)
    product = indices[:, None] * indices[None, :] % window
    angle = np.float32(2.0 * math.pi / window) * product.astype(np.float32)
    scale = np.float32(math.sqrt(window))
    re = (np.cos(angle) / scale).astype(jnp.bfloat16)
    im = (np.sin(angle) / scale).astype(jnp.bfloat16)
    a = np.block([[re, -im], [im, re]])
    b = np.block([[re, im], [-im, re]])
    return a, b


def propagator(window):
    radius = squared_radius(window)
    inside = (np.float32(9.0) * radius < window * window).astype(np.float32)
    phase_angle = np.float32(-PROPAGATION_COEF * (65536.0 / (window * window))) * radius
    return np.stack([inside * np.cos(phase_angle), inside * np.sin(phase_angle)], 0)


def start_spectrum(window):
    radius = squared_radius(window)
    inside = (np.float32(16.0) * radius < window * window).astype(np.float32)
    norm_scale = np.float32(window) / np.sqrt(np.sum(inside, dtype=np.float32))
    phase_angle = np.float32(-(DEFOCUS_COEF / window)) * radius
    spectrum = np.concatenate(
        [inside * norm_scale * np.cos(phase_angle), inside * norm_scale * np.sin(phase_angle)], 0
    )
    return spectrum.astype(jnp.bfloat16)


def atom_fields(positions, species, slab, species_amp, species_spread, layers):
    species_match = (
        species[None, :] == jnp.arange(species_amp.shape[0], dtype=jnp.int32)[:, None]
    ).astype(species_amp.dtype)
    amplitude = jnp.sum(species_match * species_amp[:, None], 0)
    spread = jnp.sum(species_match * species_spread[:, None], 0)
    inverse = 0.5 / (spread * spread)
    slab_match = (slab[None, :] == jnp.arange(layers, dtype=jnp.int32)[:, None]).astype(
        amplitude.dtype
    )
    return jnp.concatenate([positions, inverse[None, :], slab_match * amplitude[None, :]], 0)


def pick_rows(fields, pick_list):
    valid_mask = (pick_list >= 0).astype(fields.dtype)
    safe_index = jnp.maximum(pick_list, 0)
    gathered = fields[:, safe_index]
    return jnp.concatenate([gathered[:3], gathered[3:] * valid_mask[None]], 0)


def wrap(value, period):
    return value - period * jnp.floor(value * (1.0 / period))


def sincos(v):
    q = jnp.floor(v * 0.6366197723675814 + 0.5)
    r = v - q * 1.5703125
    r = r - q * 4.837512969970703125e-4
    r = r - q * 7.549789954891882e-8
    z = r * r
    s = r + r * z * (-1.6666654611e-1 + z * (8.3321608736e-3 + z * -1.9515295891e-4))
    c = 1.0 - 0.5 * z + z * z * (4.166664568298827e-2 + z * (-1.388731625493765e-3 + z * 2.443315711809948e-5))
    n = q.astype(jnp.int32)
    swap = (n & 1) == 1
    sin_v = jnp.where(swap, c, s)
    cos_v = jnp.where(swap, s, c)
    sin_v = jnp.where((n & 2) == 2, -sin_v, sin_v)
    cos_v = jnp.where(((n + 1) & 2) == 2, -cos_v, cos_v)
    return sin_v, cos_v


def slices_kernel(*refs, field_x, carried, cap, final):
    (pos_ref, owner_ref, amp_ref, spread_ref, pk_ref, a_hbm, b_hbm, prop_hbm, last_hbm,
     out_ref, wave_ref, pot_ref, a_ref, b_ref, prop_ref, last_ref, sems) = refs
    batch = wave_ref.shape[0]
    w = prop_ref.shape[-1]
    layers = pot_ref.shape[-1] // w
    species_count = amp_ref.shape[0]
    hop = pl.program_id(0)
    f32, bf16 = jnp.float32, jnp.bfloat16

    def dot(a, b):
        return jnp.dot(a, b, preferred_element_type=f32)

    first = hop == 0
    copies = [
        pltpu.make_async_copy(src, dst, sems.at[k])
        for k, (src, dst) in enumerate(
            [(a_hbm, a_ref), (b_hbm, b_ref), (prop_hbm, prop_ref), (last_hbm, last_ref)]
        )
    ]

    @pl.when(first)
    def _():
        for copy in copies:
            copy.start()

    def potentials():
        entry = owner_ref[0]
        blocks = []
        for slot in range(3):
            raw = pk_ref[hop, slot, 0:4, :]
            listed = pk_ref[hop, slot, pl.ds(4 + entry, 1), :][:, :cap]
            species = raw[2:3]
            slab = raw[3:4]
            amplitude = jnp.zeros_like(species)
            spread = jnp.zeros_like(species)
            for k in range(species_count):
                match = species == float(k)
                amplitude = jnp.where(match, amp_ref[k], amplitude)
                spread = jnp.where(match, spread_ref[k], spread)
            inverse = 0.5 / (spread * spread)
            zero = jnp.zeros_like(species)
            per_layer = [jnp.where(slab == float(l), amplitude, zero) for l in range(layers)]
            fields = jnp.concatenate(
                [raw[0:2], inverse] + per_layer + [zero] * (8 - 3 - layers), 0
            )
            atoms = fields.shape[1]
            safe = jnp.maximum(listed, 0.0).astype(jnp.int32)
            onehot = (lax.broadcasted_iota(jnp.int32, (atoms, cap), 0) == safe).astype(bf16)
            high = fields.astype(bf16)
            rest = fields - high.astype(f32)
            mid = rest.astype(bf16)
            low = (rest - mid.astype(f32)).astype(bf16)
            picked = (dot(high, onehot) + dot(mid, onehot)) + dot(low, onehot)
            valid = (listed >= 0.0).astype(f32)
            keep = lax.broadcasted_iota(jnp.int32, (8, 1), 0) < 3
            picked = jnp.where(keep, picked, picked * valid)
            blocks.append(picked)
        rows = jnp.concatenate(blocks, 1)
        cols = rows.T
        atom_x = rows[0:1]
        inverse_row = rows[2:3]
        atom_y = cols[:, 1:2]
        inverse_col = cols[:, 2:3]
        pixel_col = lax.broadcasted_iota(jnp.int32, (w, 1), 0).astype(f32)
        pixel_row = lax.broadcasted_iota(jnp.int32, (1, w), 1).astype(f32)
        shift_x = pos_ref[0, 0].astype(f32)
        dist_x = wrap(atom_x - shift_x - pixel_col + 0.5 * field_x, field_x) - 0.5 * field_x
        across = jnp.exp(dist_x * dist_x * -inverse_row).astype(bf16)
        for p in range(batch):
            shift_y = pos_ref[p, 1].astype(f32)
            dist_y = wrap(atom_y - shift_y - pixel_row + 0.5 * w, w) - 0.5 * w
            along = jnp.exp(dist_y * dist_y * -inverse_col)
            weighted = jnp.concatenate(
                [(cols[:, 3 + l : 4 + l] * along).astype(bf16) for l in range(layers)], 1
            )
            pot_ref[p] = dot(across, weighted)

    potentials()

    @pl.when(first)
    def _():
        for copy in copies:
            copy.wait()
        if carried:
            wave_ref[...] = last_ref[...]
        else:
            rows = dot(a_ref[...], last_ref[...]).astype(bf16)
            rows = jnp.concatenate([rows[:w], rows[w:]], 1)
            start = dot(rows, b_ref[...]).astype(bf16)
            for p in range(batch):
                wave_ref[p] = start

    pr = prop_ref[0]
    pi = prop_ref[1]
    for layer in range(layers):
        column = pl.ds(layer * w, w)
        transmitted = []
        for p in range(batch):
            psi = wave_ref[p]
            wr = psi[:, :w].astype(f32)
            wi = psi[:, w:].astype(f32)
            v = pot_ref[p, :, column]
            sv, cv = sincos(v)
            tr = (wr * cv - wi * sv).astype(bf16)
            ti = (wr * sv + wi * cv).astype(bf16)
            transmitted.append(jnp.concatenate([tr, ti], 1))
        rowwise = [dot(t, a_ref[...]).astype(bf16) for t in transmitted]
        spectra = [dot(b_ref[...], jnp.concatenate([rw[:, :w], rw[:, w:]], 0)) for rw in rowwise]
        propagated = []
        for sp in spectra:
            sr = sp[:w]
            si = sp[w:]
            propagated.append(
                jnp.concatenate([(sr * pr - si * pi).astype(bf16), (sr * pi + si * pr).astype(bf16)], 0)
            )
        back = [dot(a_ref[...], spb).astype(bf16) for spb in propagated]
        for p, br in enumerate(back):
            wave_ref[p] = dot(jnp.concatenate([br[:w], br[w:]], 1), b_ref[...]).astype(bf16)

    @pl.when(hop == pl.num_programs(0) - 1)
    def _():
        if final:
            for p in range(batch):
                out_ref[p, :, 0, :] = wave_ref[p, :, :w]
                out_ref[p, :, 1, :] = wave_ref[p, :, w:]
        else:
            out_ref[...] = wave_ref[...]


def run_slices(probe_pos, entry, amp, spread, packs, window, layers, field_x, cap, wave=None, final=False):
    batch = probe_pos.shape[0]
    hops = packs.shape[0]
    w = window
    a, b = dft_blocks(w)
    prop = propagator(w)
    full = lambda shape: pl.BlockSpec(shape, lambda h, *_: (0,) * len(shape))
    carried = wave is not None
    out_shape = (batch, w, 2, w) if final else (batch, w, 2 * w)
    last = wave if carried else jnp.asarray(start_spectrum(w))
    atoms = 3 * cap
    steps = batch * hops * layers
    flops = steps * 4 * 2 * w * (2 * w) * (2 * w) + batch * hops * 2 * w * atoms * layers * w
    return pl.pallas_call(
        functools.partial(slices_kernel, field_x=float(field_x), carried=carried, cap=cap, final=final),
        out_shape=jax.ShapeDtypeStruct(out_shape, jnp.bfloat16),
        grid_spec=pltpu.PrefetchScalarGridSpec(
            num_scalar_prefetch=2,
            grid=(hops,),
            in_specs=[
                pl.BlockSpec(memory_space=pltpu.SMEM),
                pl.BlockSpec(memory_space=pltpu.SMEM),
                pl.BlockSpec(memory_space=pltpu.VMEM),
                pl.BlockSpec(memory_space=pl.ANY),
                pl.BlockSpec(memory_space=pl.ANY),
                pl.BlockSpec(memory_space=pl.ANY),
                pl.BlockSpec(memory_space=pl.ANY),
            ],
            out_specs=full(out_shape),
            scratch_shapes=[
                pltpu.VMEM((batch, w, 2 * w), jnp.bfloat16),
                pltpu.VMEM((batch, w, layers * w), jnp.float32),
                pltpu.VMEM(a.shape, jnp.bfloat16),
                pltpu.VMEM(b.shape, jnp.bfloat16),
                pltpu.VMEM(prop.shape, jnp.float32),
                pltpu.VMEM(last.shape, jnp.bfloat16),
                pltpu.SemaphoreType.DMA((4,)),
            ],
        ),
        compiler_params=pltpu.CompilerParams(
            dimension_semantics=("arbitrary",),
        ),
        cost_estimate=pl.CostEstimate(
            flops=flops,
            transcendentals=steps * 2 * w * w + batch * hops * 2 * atoms * w,
            bytes_accessed=2 * (2 * w) ** 2 * 2 + 3 * w * w * 4 + batch * w * w * 4,
        ),
    )(probe_pos, entry, amp, spread, packs, jnp.asarray(a), jnp.asarray(b), jnp.asarray(prop), last)


def shards(atom_xy, atom_species, atom_slab, species_amp, species_spread, margin, probe_pos):
    layers = SL_DEV
    window = W
    atoms = atom_xy.shape[-1]
    cap = margin.shape[-1]
    n_lat = lax.axis_size("lat")
    owners = lax.axis_size("slc")
    field_x = n_lat * atoms * (2 * window // cap)
    f32 = jnp.float32
    raw = jnp.concatenate(
        [atom_xy[0, 0], atom_species[0, 0][None].astype(f32), atom_slab[0, 0][None].astype(f32)], 0
    )
    marg = jnp.transpose(margin[0, 0, :, 0], (1, 0, 2)).astype(f32)
    marg = jnp.pad(marg, ((0, 0), (0, 0), (0, atoms - cap)), constant_values=-1.0)
    packs = jnp.concatenate([jnp.broadcast_to(raw[None], (3,) + raw.shape), marg], 1)
    from_left = lax.ppermute(packs[2], "lat", [(i, (i + 1) % n_lat) for i in range(n_lat)])
    from_right = lax.ppermute(packs[0], "lat", [((i + 1) % n_lat, i) for i in range(n_lat)])
    local = jnp.stack([from_left, packs[1], from_right], 0)[None]
    me = lax.axis_index("slc")
    entry = jnp.reshape(me, (1,)).astype(jnp.int32)
    later = [
        lax.ppermute(local, "slc", [(i, (i - hop) % owners) for i in range(owners)])
        for hop in range(1, owners)
    ]
    batch = probe_pos.shape[0]
    wave = run_slices(probe_pos, entry, species_amp, species_spread, local, window, layers, field_x, cap, final=not later)
    if later:
        wave = run_slices(
            probe_pos, entry, species_amp, species_spread, jnp.concatenate(later, 0), window, layers, field_x, cap, wave,
            final=True,
        )
    return wave


def solution(mesh):
    in_specs = (
        P(("groups", "lat"), "slc", None, None),
        P(("groups", "lat"), "slc", None),
        P(("groups", "lat"), "slc", None),
        P(),
        P(),
        P(("groups", "lat"), "slc", None, "rep", None, None),
        P(("groups", "lat", "slc", "rep"), None),
    )
    out_specs = P(("groups", "lat", "slc", "rep"), None, None, None)
    return jax.shard_map(shards, mesh=mesh, in_specs=in_specs, out_specs=out_specs, check_vma=False)
```

```python
import functools
import math

import jax
import numpy as np
import jax.numpy as jnp
from jax import lax
from jax.experimental import pallas as pl
from jax.experimental.pallas import tpu as pltpu
from jax.sharding import PartitionSpec as P

W = 256
SL_DEV = 2


PROPAGATION_COEF = 0.001
DEFOCUS_COEF = 4.19


def centered_frequency(window):
    indices = np.arange(window, dtype=np.int32)
    return np.where(indices < window // 2, indices, indices - window).astype(np.float32)


def squared_radius(window):
    frequency = centered_frequency(window)
    return frequency[:, None] * frequency[:, None] + frequency[None, :] * frequency[None, :]


def dft_blocks(window):
    indices = np.arange(window, dtype=np.int32)
    product = indices[:, None] * indices[None, :] % window
    angle = np.float32(2.0 * math.pi / window) * product.astype(np.float32)
    scale = np.float32(math.sqrt(window))
    re = (np.cos(angle) / scale).astype(jnp.bfloat16)
    im = (np.sin(angle) / scale).astype(jnp.bfloat16)
    a = np.block([[re, -im], [im, re]])
    b = np.block([[re, im], [-im, re]])
    return a, b


def propagator(window):
    radius = squared_radius(window)
    inside = (np.float32(9.0) * radius < window * window).astype(np.float32)
    phase_angle = np.float32(-PROPAGATION_COEF * (65536.0 / (window * window))) * radius
    return np.stack([inside * np.cos(phase_angle), inside * np.sin(phase_angle)], 0)


def start_spectrum(window):
    radius = squared_radius(window)
    inside = (np.float32(16.0) * radius < window * window).astype(np.float32)
    norm_scale = np.float32(window) / np.sqrt(np.sum(inside, dtype=np.float32))
    phase_angle = np.float32(-(DEFOCUS_COEF / window)) * radius
    spectrum = np.concatenate(
        [inside * norm_scale * np.cos(phase_angle), inside * norm_scale * np.sin(phase_angle)], 0
    )
    return spectrum.astype(jnp.bfloat16)


def atom_fields(positions, species, slab, species_amp, species_spread, layers):
    species_match = (
        species[None, :] == jnp.arange(species_amp.shape[0], dtype=jnp.int32)[:, None]
    ).astype(species_amp.dtype)
    amplitude = jnp.sum(species_match * species_amp[:, None], 0)
    spread = jnp.sum(species_match * species_spread[:, None], 0)
    inverse = 0.5 / (spread * spread)
    slab_match = (slab[None, :] == jnp.arange(layers, dtype=jnp.int32)[:, None]).astype(
        amplitude.dtype
    )
    return jnp.concatenate([positions, inverse[None, :], slab_match * amplitude[None, :]], 0)


def pick_rows(fields, pick_list):
    valid_mask = (pick_list >= 0).astype(fields.dtype)
    safe_index = jnp.maximum(pick_list, 0)
    gathered = fields[:, safe_index]
    return jnp.concatenate([gathered[:3], gathered[3:] * valid_mask[None]], 0)


def centered(value, period):
    return value - period * jnp.floor((value + 0.5 * period) * (1.0 / period))


def sincos(v):
    q = jnp.floor(v * 0.6366197723675814 + 0.5)
    r = v - q * 1.5703125
    r = r - q * 4.837512969970703125e-4
    r = r - q * 7.549789954891882e-8
    z = r * r
    s = r + r * z * (-1.6666654611e-1 + z * (8.3321608736e-3 + z * -1.9515295891e-4))
    c = 1.0 - 0.5 * z + z * z * (4.166664568298827e-2 + z * (-1.388731625493765e-3 + z * 2.443315711809948e-5))
    n = q.astype(jnp.int32)
    swap = (n & 1) == 1
    sin_v = jnp.where(swap, c, s)
    cos_v = jnp.where(swap, s, c)
    sin_v = jnp.where((n & 2) == 2, -sin_v, sin_v)
    cos_v = jnp.where(((n + 1) & 2) == 2, -cos_v, cos_v)
    return sin_v, cos_v


def slices_kernel(*refs, field_x, carried, cap, final):
    (pos_ref, owner_ref, amp_ref, spread_ref, pk_ref, a_hbm, b_hbm, prop_hbm, last_hbm,
     out_ref, wave_ref, pot_ref, a_ref, b_ref, prop_ref, last_ref, sems) = refs
    batch = wave_ref.shape[0]
    w = prop_ref.shape[-1]
    layers = pot_ref.shape[-1] // w
    species_count = amp_ref.shape[0]
    hop = pl.program_id(0)
    f32, bf16 = jnp.float32, jnp.bfloat16

    def dot(a, b):
        return jnp.dot(a, b, preferred_element_type=f32)

    first = hop == 0
    copies = [
        pltpu.make_async_copy(src, dst, sems.at[k])
        for k, (src, dst) in enumerate(
            [(a_hbm, a_ref), (b_hbm, b_ref), (prop_hbm, prop_ref), (last_hbm, last_ref)]
        )
    ]

    @pl.when(first)
    def _():
        for copy in copies:
            copy.start()

    def potentials():
        entry = owner_ref[0]
        blocks = []
        for slot in range(3):
            raw = pk_ref[hop, slot, 0:4, :]
            listed = pk_ref[hop, slot, pl.ds(4 + entry, 1), :][:, :cap]
            species = raw[2:3]
            slab = raw[3:4]
            amplitude = jnp.zeros_like(species)
            spread = jnp.zeros_like(species)
            for k in range(species_count):
                match = species == float(k)
                amplitude = jnp.where(match, amp_ref[k], amplitude)
                spread = jnp.where(match, spread_ref[k], spread)
            inverse = 0.5 / (spread * spread)
            zero = jnp.zeros_like(species)
            per_layer = [jnp.where(slab == float(l), amplitude, zero) for l in range(layers)]
            fields = jnp.concatenate(
                [raw[0:2], inverse] + per_layer + [zero] * (8 - 3 - layers), 0
            )
            atoms = fields.shape[1]
            safe = jnp.maximum(listed, 0.0).astype(jnp.int32)
            onehot = (lax.broadcasted_iota(jnp.int32, (atoms, cap), 0) == safe).astype(bf16)
            high = fields.astype(bf16)
            rest = fields - high.astype(f32)
            mid = rest.astype(bf16)
            low = (rest - mid.astype(f32)).astype(bf16)
            picked = (dot(high, onehot) + dot(mid, onehot)) + dot(low, onehot)
            valid = (listed >= 0.0).astype(f32)
            keep = lax.broadcasted_iota(jnp.int32, (8, 1), 0) < 3
            picked = jnp.where(keep, picked, picked * valid)
            blocks.append(picked)
        rows = jnp.concatenate(blocks, 1)
        cols = rows.T
        atom_x = rows[0:1]
        inverse_row = rows[2:3]
        atom_y = cols[:, 1:2]
        inverse_col = cols[:, 2:3]
        pixel_col = lax.broadcasted_iota(jnp.int32, (w, 1), 0).astype(f32)
        pixel_row = lax.broadcasted_iota(jnp.int32, (1, w), 1).astype(f32)
        shift_x = pos_ref[0, 0].astype(f32)
        dist_x = centered(atom_x - shift_x - pixel_col, field_x)
        across = jnp.exp(dist_x * dist_x * -inverse_row).astype(bf16)
        for p in range(batch):
            shift_y = pos_ref[p, 1].astype(f32)
            dist_y = centered(atom_y - shift_y - pixel_row, w)
            along = jnp.exp(dist_y * dist_y * -inverse_col)
            weighted = jnp.concatenate(
                [(cols[:, 3 + l : 4 + l] * along).astype(bf16) for l in range(layers)], 1
            )
            pot_ref[p] = dot(across, weighted)

    potentials()

    @pl.when(first)
    def _():
        for copy in copies:
            copy.wait()
        if carried:
            wave_ref[...] = last_ref[...]
        else:
            rows = dot(a_ref[...], last_ref[...]).astype(bf16)
            rows = jnp.concatenate([rows[:w], rows[w:]], 1)
            start = dot(rows, b_ref[...]).astype(bf16)
            for p in range(batch):
                wave_ref[p] = start

    pr = prop_ref[0]
    pi = prop_ref[1]
    for layer in range(layers):
        column = pl.ds(layer * w, w)
        transmitted = []
        for p in range(batch):
            psi = wave_ref[p]
            wr = psi[:, :w].astype(f32)
            wi = psi[:, w:].astype(f32)
            v = pot_ref[p, :, column]
            sv, cv = sincos(v)
            tr = (wr * cv - wi * sv).astype(bf16)
            ti = (wr * sv + wi * cv).astype(bf16)
            transmitted.append(jnp.concatenate([tr, ti], 1))
        rowwise = [dot(t, a_ref[...]).astype(bf16) for t in transmitted]
        spectra = [dot(b_ref[...], jnp.concatenate([rw[:, :w], rw[:, w:]], 0)) for rw in rowwise]
        propagated = []
        for sp in spectra:
            sr = sp[:w]
            si = sp[w:]
            propagated.append(
                jnp.concatenate([(sr * pr - si * pi).astype(bf16), (sr * pi + si * pr).astype(bf16)], 0)
            )
        back = [dot(a_ref[...], spb).astype(bf16) for spb in propagated]
        for p, br in enumerate(back):
            wave_ref[p] = dot(jnp.concatenate([br[:w], br[w:]], 1), b_ref[...]).astype(bf16)

    @pl.when(hop == pl.num_programs(0) - 1)
    def _():
        if final:
            for p in range(batch):
                out_ref[p, :, 0, :] = wave_ref[p, :, :w]
                out_ref[p, :, 1, :] = wave_ref[p, :, w:]
        else:
            out_ref[...] = wave_ref[...]


def run_slices(probe_pos, entry, amp, spread, packs, window, layers, field_x, cap, wave=None, final=False):
    batch = probe_pos.shape[0]
    hops = packs.shape[0]
    w = window
    a, b = dft_blocks(w)
    prop = propagator(w)
    full = lambda shape: pl.BlockSpec(shape, lambda h, *_: (0,) * len(shape))
    carried = wave is not None
    out_shape = (batch, w, 2, w) if final else (batch, w, 2 * w)
    last = wave if carried else jnp.asarray(start_spectrum(w))
    atoms = 3 * cap
    steps = batch * hops * layers
    flops = steps * 4 * 2 * w * (2 * w) * (2 * w) + batch * hops * 2 * w * atoms * layers * w
    return pl.pallas_call(
        functools.partial(slices_kernel, field_x=float(field_x), carried=carried, cap=cap, final=final),
        out_shape=jax.ShapeDtypeStruct(out_shape, jnp.bfloat16),
        grid_spec=pltpu.PrefetchScalarGridSpec(
            num_scalar_prefetch=2,
            grid=(hops,),
            in_specs=[
                pl.BlockSpec(memory_space=pltpu.SMEM),
                pl.BlockSpec(memory_space=pltpu.SMEM),
                pl.BlockSpec(memory_space=pltpu.VMEM),
                pl.BlockSpec(memory_space=pl.ANY),
                pl.BlockSpec(memory_space=pl.ANY),
                pl.BlockSpec(memory_space=pl.ANY),
                pl.BlockSpec(memory_space=pl.ANY),
            ],
            out_specs=full(out_shape),
            scratch_shapes=[
                pltpu.VMEM((batch, w, 2 * w), jnp.bfloat16),
                pltpu.VMEM((batch, w, layers * w), jnp.float32),
                pltpu.VMEM(a.shape, jnp.bfloat16),
                pltpu.VMEM(b.shape, jnp.bfloat16),
                pltpu.VMEM(prop.shape, jnp.float32),
                pltpu.VMEM(last.shape, jnp.bfloat16),
                pltpu.SemaphoreType.DMA((4,)),
            ],
        ),
        compiler_params=pltpu.CompilerParams(
            dimension_semantics=("arbitrary",),
        ),
        cost_estimate=pl.CostEstimate(
            flops=flops,
            transcendentals=steps * 2 * w * w + batch * hops * 2 * atoms * w,
            bytes_accessed=2 * (2 * w) ** 2 * 2 + 3 * w * w * 4 + batch * w * w * 4,
        ),
    )(probe_pos, entry, amp, spread, packs, jnp.asarray(a), jnp.asarray(b), jnp.asarray(prop), last)


def shards(atom_xy, atom_species, atom_slab, species_amp, species_spread, margin, probe_pos):
    layers = SL_DEV
    window = W
    atoms = atom_xy.shape[-1]
    cap = margin.shape[-1]
    n_lat = lax.axis_size("lat")
    owners = lax.axis_size("slc")
    field_x = n_lat * atoms * (2 * window // cap)
    f32 = jnp.float32
    raw = jnp.concatenate(
        [atom_xy[0, 0], atom_species[0, 0][None].astype(f32), atom_slab[0, 0][None].astype(f32)], 0
    )
    marg = jnp.transpose(margin[0, 0, :, 0], (1, 0, 2)).astype(f32)
    marg = jnp.pad(marg, ((0, 0), (0, 0), (0, atoms - cap)), constant_values=-1.0)
    packs = jnp.concatenate([jnp.broadcast_to(raw[None], (3,) + raw.shape), marg], 1)
    from_left = lax.ppermute(packs[2], "lat", [(i, (i + 1) % n_lat) for i in range(n_lat)])
    from_right = lax.ppermute(packs[0], "lat", [((i + 1) % n_lat, i) for i in range(n_lat)])
    local = jnp.stack([from_left, packs[1], from_right], 0)[None]
    me = lax.axis_index("slc")
    entry = jnp.reshape(me, (1,)).astype(jnp.int32)
    later = [
        lax.ppermute(local, "slc", [(i, (i - hop) % owners) for i in range(owners)])
        for hop in range(1, owners)
    ]
    batch = probe_pos.shape[0]
    wave = run_slices(probe_pos, entry, species_amp, species_spread, local, window, layers, field_x, cap, final=not later)
    if later:
        wave = run_slices(
            probe_pos, entry, species_amp, species_spread, jnp.concatenate(later, 0), window, layers, field_x, cap, wave,
            final=True,
        )
    return wave


def solution(mesh):
    in_specs = (
        P(("groups", "lat"), "slc", None, None),
        P(("groups", "lat"), "slc", None),
        P(("groups", "lat"), "slc", None),
        P(),
        P(),
        P(("groups", "lat"), "slc", None, "rep", None, None),
        P(("groups", "lat", "slc", "rep"), None),
    )
    out_specs = P(("groups", "lat", "slc", "rep"), None, None, None)
    return jax.shard_map(shards, mesh=mesh, in_specs=in_specs, out_specs=out_specs, check_vma=False)
```
